32 devices in a mesh: groups: 2 (over x), ctx: 4 (over y, core), head: 4 (over z).
Axes of the slice: x: 2, y: 2, z: 4, core: 2. Of those that a mesh axis runs over, the one named last changes fastest.
Arguments:
- tokens: bfloat16 [8192, 2048], P(('groups', 'ctx')), parts along dimension 0, may hold values from -30 to 30
- norm_one: float32 [2048], replicated, may hold values from 0.1 to 1.9
- w_qkv1: bfloat16 [2048, 3, 2048], P(None, None, 'head'), may hold values from -0.125 to 0.125
- lin_gain: float32 [2048], P('head'), may hold values from 0.1 to 1.9
- w_out1: bfloat16 [2048, 2048], P('head'), may hold values from -0.125 to 0.125
- norm_two: float32 [2048], replicated, may hold values from 0.1 to 1.9
- w_qkv2: bfloat16 [2048, 3, 2048], P(None, None, 'head'), may hold values from -0.125 to 0.125
- q_gain: float32 [128], replicated, may hold values from 0.4 to 2.5
- k_gain: float32 [128], replicated, may hold values from 0.4 to 2.5
- w_out2: bfloat16 [2048, 2048], P('head'), may hold values from -0.125 to 0.125
- neighbours: int32 [16, 8], P('ctx'), may hold values from -1 to 15, as said below
Outputs:
- mixed: bfloat16 [8192, 2048], P(('groups', 'ctx', 'head')), parts along dimension 0
The draws below stay inside these ranges and needn't reach their ends.
There are 2 independent parts, one for each index of `groups`. The reference program is written for one: setup_inputs(seed, part) draws one part's arguments, and reference() takes and returns one part's arrays. A program takes and returns all parts, laid end to end along the dimension named above; an argument that names none is the same for every part. Nothing has to cross between parts.
Inputs may be any that keep to these rules, and one draw needn't show every extreme that they name: `neighbours`: tile (i, j, l) of the 4 x 2 x 2 grid is number (i * 2 + j) * 2 + l, and its tokens are a whole tile of the stream. Entry 0 of row t is t itself; every other entry is -1 or a tile other than t whose grid position differs from t's by at most one in each dimension; the tiles of one row are distinct.
All inputs are finite; a program needn't handle non-finite values.
Results may differ from the reference program's by a relative error of at most 0.013.
Values may be sent and summed in bfloat16 or wider, within the bound.
No kernel may reach another device: no remote copies, remote signals or barrier semaphores. Data moves between devices by JAX's collectives and lax.ppermute only.
A program may use at most 192 MiB of HBM per device.

```python
import math
import jax
import jax.numpy as jnp
import numpy as np
from jax import lax

D = 2048
HEADS = 16
HEAD_DIM = 128
TILE = 256
NB = 8
GY = 2
GZ = 2
INNER = 2048
GX = 4
TILES = 16
TOKENS = 4096
N_HEAD = 4


def draw_tokens(key, part):
    key_base, key_rows, key_cols = jax.random.split(key, 3)
    row_scale = jnp.exp(jax.random.uniform(key_rows, (TOKENS, 1), jnp.float32, math.log(0.3), math.log(3.0)))
    col_scale = jnp.exp(jax.random.uniform(key_cols, (1, D), jnp.float32, math.log(0.5), math.log(2.0)))
    base = jnp.clip(jax.random.normal(key_base, (TOKENS, D), jnp.float32), -5.0, 5.0)
    return (row_scale * col_scale * base).astype(jnp.bfloat16)


def draw_neighbours(key, part):
    offset_table = np.array([[a, b, c] for a in (-1, 0, 1) for b in (-1, 0, 1) for c in (-1, 0, 1) if (a, b, c) != (0, 0, 0)], dtype=np.int32)
    tile_ids = jnp.arange(TILES, dtype=jnp.int32)
    pos_x = tile_ids // (GY * GZ)
    pos_y = tile_ids // GZ % GY
    pos_z = tile_ids % GZ
    ranking = jax.random.randint(key, (TILES, 26), 0, 1 << 20, dtype=jnp.int32) * 32 + jnp.arange(26, dtype=jnp.int32)[None, :]
    _, chosen = lax.top_k(ranking, NB - 1)
    picked = jnp.asarray(offset_table)[chosen]
    next_x = pos_x[:, None] + picked[:, :, 0]
    next_y = pos_y[:, None] + picked[:, :, 1]
    next_z = pos_z[:, None] + picked[:, :, 2]
    inside = (next_x >= 0) & (next_x < GX) & (next_y >= 0) & (next_y < GY) & (next_z >= 0) & (next_z < GZ)
    tile_numbers = jnp.where(inside, (next_x * GY + next_y) * GZ + next_z, -1)
    return jnp.concatenate([tile_ids[:, None], tile_numbers], axis=1).astype(jnp.int32)


def level_of(rng, dims, cuts, smallest, largest):
    def one(position, blocks):
        draws = jax.random.uniform(jax.random.fold_in(jax.random.fold_in(rng, 6), position), (blocks,), jnp.float32, smallest / len(cuts), largest / len(cuts))
        return jnp.repeat(jnp.exp(draws), dims[position] // blocks).reshape((-1,) + (1,) * (len(dims) - position - 1))

    factor_of = one(*cuts[0])
    for cut in cuts[1:]:
        factor_of = factor_of * one(*cut)
    return factor_of


def noise(key, extent, width, reach, cuts=(), kind=jnp.bfloat16):
    result = width * jax.random.normal(key, extent, jnp.float32)
    if cuts:
        result = result * level_of(key, extent, cuts, -0.22, 0.18)
    return jnp.clip(result, -reach, reach).astype(kind)


def setup_inputs(seed: int = 0, part: int = 0) -> dict:
    streams_of = jax.random.split(jax.random.key(seed), 12)
    own_keys = jax.random.split(jax.random.fold_in(streams_of[11], part), 12)
    return {
        "tokens": draw_tokens(jax.random.fold_in(jax.random.fold_in(streams_of[11], part), 71), part),
        "norm_one": jnp.clip(1.0 + 0.18 * jax.random.normal(streams_of[1], (D,), jnp.float32), 0.1, 1.9),
        "w_qkv1": noise(streams_of[2], (D, 3, INNER), D ** -0.5, 0.125, ((2, 4),)),
        "lin_gain": jnp.clip(1.0 + 0.18 * jax.random.normal(streams_of[3], (INNER,), jnp.float32), 0.1, 1.9),
        "w_out1": noise(streams_of[4], (INNER, D), INNER ** -0.5, 0.125, ((0, 4),)),
        "norm_two": jnp.clip(1.0 + 0.18 * jax.random.normal(streams_of[5], (D,), jnp.float32), 0.1, 1.9),
        "w_qkv2": noise(streams_of[6], (D, 3, INNER), D ** -0.5, 0.125, ((2, 4),)),
        "q_gain": jnp.clip(jnp.exp(jax.random.uniform(streams_of[7], (HEAD_DIM,), jnp.float32, math.log(0.4), math.log(2.5))), 0.4, 2.5),
        "k_gain": jnp.clip(jnp.exp(jax.random.uniform(streams_of[8], (HEAD_DIM,), jnp.float32, math.log(0.4), math.log(2.5))), 0.4, 2.5),
        "w_out2": noise(streams_of[9], (INNER, D), INNER ** -0.5, 0.125, ((0, 4),)),
        "neighbours": draw_neighbours(jax.random.fold_in(streams_of[11], 71), part),
    }


def rms_rows(value, gain):
    mean_sq = lax.optimization_barrier(jnp.mean(value * value, axis=-1, keepdims=True))
    return value * lax.rsqrt(mean_sq + 1e-06) * gain

def feature_map(value):
    return jnp.where(value > 0, value + 1.0, jnp.exp(jnp.minimum(value, 0.0)))

def rounded(value):
    return lax.optimization_barrier(value.astype(jnp.bfloat16)).astype(jnp.float32)

def mix_groups(attended, w_out):
    per_group = attended.shape[1] // N_HEAD
    total = jnp.zeros((attended.shape[0], w_out.shape[1]), jnp.float32)
    for group in range(N_HEAD):
        low = group * per_group
        term = jnp.dot(attended[:, low:low + per_group], w_out[low:low + per_group], preferred_element_type=jnp.float32)
        total = total + rounded(term)
    return total

def reference(tokens, norm_one, w_qkv1, lin_gain, w_out1, norm_two, w_qkv2, q_gain, k_gain, w_out2, neighbours):
    highest = lax.Precision.HIGHEST
    inner_width = HEADS * HEAD_DIM
    block_rows = 2 * TILE
    block_count = TOKENS // block_rows
    normed = rms_rows(tokens.astype(jnp.float32), norm_one).astype(jnp.bfloat16)
    projected = jnp.dot(normed, w_qkv1.reshape(D, 3 * inner_width), preferred_element_type=jnp.float32)
    projected = projected.reshape(TOKENS, 3, HEADS, HEAD_DIM)
    query_map = rounded(feature_map(projected[:, 0]))
    key_map = rounded(feature_map(projected[:, 1]))
    value_one = rounded(projected[:, 2])

    def shaped(array):
        return array.reshape(block_count, block_rows, HEADS, HEAD_DIM)
    causal = lax.broadcasted_iota(jnp.int32, (block_rows, block_rows), 0) >= lax.broadcasted_iota(jnp.int32, (block_rows, block_rows), 1)

    def advance(carry_state, inputs):
        q_block, k_block, v_block = inputs
        scores = jnp.einsum('the,she->hts', q_block, k_block, precision=highest)
        scores = jnp.where(causal[None], scores, 0.0)
        output = jnp.einsum('hts,she->the', scores, v_block, precision=highest)
        output = output + jnp.einsum('the,hef->thf', q_block, carry_state, precision=highest)
        carry_state = carry_state + jnp.einsum('the,thf->hef', k_block, v_block, precision=highest)
        return (carry_state, output)
    start_state = jnp.zeros((HEADS, HEAD_DIM, HEAD_DIM), jnp.float32)
    _, combined = lax.scan(advance, start_state, (shaped(query_map), shaped(key_map), shaped(value_one)))
    combined = combined.reshape(TOKENS, HEADS, HEAD_DIM)
    attn_one = rms_rows(combined, lin_gain.reshape(HEADS, HEAD_DIM)).astype(jnp.bfloat16).reshape(TOKENS, inner_width)
    residual = (tokens.astype(jnp.float32) + mix_groups(attn_one, w_out1)).astype(jnp.bfloat16)
    normed_two = rms_rows(residual.astype(jnp.float32), norm_two).astype(jnp.bfloat16)
    projected_two = jnp.dot(normed_two, w_qkv2.reshape(D, 3 * inner_width), preferred_element_type=jnp.float32)
    projected_two = projected_two.reshape(TOKENS, 3, HEADS, HEAD_DIM)
    query_hat = rounded(rms_rows(projected_two[:, 0], q_gain))
    key_hat = rounded(rms_rows(projected_two[:, 1], k_gain))
    value_two = rounded(projected_two[:, 2])
    query_tiles = query_hat.reshape(TILES, TILE, HEADS, HEAD_DIM)
    key_tiles = key_hat.reshape(TILES, TILE, HEADS, HEAD_DIM)
    value_tiles = value_two.reshape(TILES, TILE, HEADS, HEAD_DIM)
    score_scale = 1.0 / math.sqrt(HEAD_DIM)

    def one_tile(inputs):
        query_tile, neighbour_row = inputs
        clamped = jnp.maximum(neighbour_row, 0).astype(jnp.int32)
        key_rows = key_tiles[clamped].reshape(NB * TILE, HEADS, HEAD_DIM)
        value_set = value_tiles[clamped].reshape(NB * TILE, HEADS, HEAD_DIM)
        scores = jnp.einsum('the,she->hts', query_tile, key_rows, precision=highest) * score_scale
        valid_keys = jnp.repeat(neighbour_row >= 0, TILE)
        unnormed = jnp.where(valid_keys[None, None, :], jnp.exp(scores), 0.0)
        weights = rounded(unnormed / lax.optimization_barrier(jnp.sum(unnormed, axis=-1, keepdims=True)))
        return jnp.einsum('hts,she->the', weights, value_set, precision=highest).astype(jnp.bfloat16)
    attn_two = lax.map(one_tile, (query_tiles, neighbours)).reshape(TOKENS, inner_width)
    return (residual.astype(jnp.float32) + mix_groups(attn_two, w_out2)).astype(jnp.bfloat16)
```

```python
import math

import jax
import jax.numpy as jnp
from jax import lax
from jax.sharding import PartitionSpec as P

TILE = 256
GY = 2
GZ = 2


EPS = 1e-06


def with_halo(shard, sides, width):
    for axis, dim in sides:
        size, length = (lax.axis_size(axis), shard.shape[dim])
        up = [(i, (i + 1) % size) for i in range(size - 1)]
        down = [(j, i) for i, j in up]
        last = lax.slice_in_dim(shard, length - width, length, axis=dim)
        first = lax.slice_in_dim(shard, 0, width, axis=dim)
        before = lax.ppermute(last, axis, up)
        after = lax.ppermute(first, axis, down)
        shard = jnp.concatenate([before, shard, after], axis=dim)
    return shard


def rms_rows(value, gain):
    mean_sq = jnp.mean(value * value, axis=-1, keepdims=True)
    return value * lax.rsqrt(mean_sq + EPS) * gain


def feature_map(value):
    return jnp.where(value > 0, value + 1.0, jnp.exp(jnp.minimum(value, 0.0)))


def split_two(value):
    high_part = value.astype(jnp.bfloat16)
    low_part = (value - high_part.astype(jnp.float32)).astype(jnp.bfloat16)
    return (high_part, low_part)


def on_device(
    tokens, norm_one, w_qkv1, lin_gain, w_out1, norm_two, w_qkv2, q_gain, k_gain, w_out2, neighbours
):
    f32, bf16 = jnp.float32, jnp.bfloat16
    tok_rows, feature_width = tokens.shape
    inner_dev = w_qkv1.shape[2]
    head_dim = q_gain.shape[0]
    heads_dev = inner_dev // head_dim
    block_rows = 2 * TILE
    block_count = tok_rows // block_rows
    rows_mine = tok_rows // lax.axis_size("head")
    head_index = lax.axis_index("head")
    ctx_index = lax.axis_index("ctx")
    ctx_size = lax.axis_size("ctx")

    normed = rms_rows(tokens.astype(f32), norm_one).astype(bf16)
    projected = jnp.dot(
        normed, w_qkv1.reshape(feature_width, 3 * inner_dev), preferred_element_type=f32
    )
    projected = projected.reshape(tok_rows, 3, heads_dev, head_dim)
    query_map = feature_map(projected[:, 0]).astype(bf16)
    key_map = feature_map(projected[:, 1]).astype(bf16)
    value_one = projected[:, 2].astype(bf16)
    q_blocks = query_map.reshape(block_count, block_rows, heads_dev, head_dim)
    k_blocks = key_map.reshape(block_count, block_rows, heads_dev, head_dim)
    v_blocks = value_one.reshape(block_count, block_rows, heads_dev, head_dim)
    block_states = jnp.einsum(
        "nthe,nthf->nhef", k_blocks, v_blocks, preferred_element_type=f32
    )
    own_total = jnp.sum(block_states, axis=0)
    all_totals = lax.all_gather(own_total.astype(bf16), "ctx", axis=0).astype(f32)
    earlier_dev = jnp.arange(ctx_size, dtype=jnp.int32) < ctx_index
    carried = jnp.sum(jnp.where(earlier_dev[:, None, None, None], all_totals, 0.0), axis=0)

    causal = lax.broadcasted_iota(jnp.int32, (block_rows, block_rows), 0) >= lax.broadcasted_iota(
        jnp.int32, (block_rows, block_rows), 1
    )
    w_qkv2_flat = w_qkv2.reshape(feature_width, 3 * inner_dev)
    residual_parts = []
    q_parts, k_parts, v_parts = [], [], []
    previous = None
    for n in range(block_count):
        q_n, k_n, v_n = q_blocks[n], k_blocks[n], v_blocks[n]
        scores = jnp.einsum("the,she->hts", q_n, k_n, preferred_element_type=f32)
        scores = jnp.where(causal, scores, 0.0)
        score_high, score_low = split_two(scores)
        within = jnp.einsum("hts,she->the", score_high, v_n, preferred_element_type=f32)
        within = within + jnp.einsum("hts,she->the", score_low, v_n, preferred_element_type=f32)
        state_high, state_low = split_two(carried)
        carried_term = jnp.einsum("the,hef->thf", q_n, state_high, preferred_element_type=f32)
        carried_term = carried_term + jnp.einsum(
            "the,hef->thf", q_n, state_low, preferred_element_type=f32
        )
        carried = carried + block_states[n]
        combined = within + carried_term
        attn_n = (
            rms_rows(combined, lin_gain.reshape(heads_dev, head_dim))
            .astype(bf16)
            .reshape(block_rows, inner_dev)
        )
        partial = jnp.dot(attn_n, w_out1, preferred_element_type=f32).astype(bf16)
        if previous is not None:
            partial, previous = lax.optimization_barrier((partial, previous))
            residual_parts[-1] = previous
        summed = lax.psum(partial, "head").astype(f32)
        tokens_n = tokens[n * block_rows : (n + 1) * block_rows].astype(f32)
        residual_n = (tokens_n + summed).astype(bf16)
        residual_parts.append(residual_n)
        previous = residual_n
        normed_n = rms_rows(residual_n.astype(f32), norm_two).astype(bf16)
        proj_n = jnp.dot(normed_n, w_qkv2_flat, preferred_element_type=f32)
        proj_n = proj_n.reshape(block_rows, 3, heads_dev, head_dim)
        q_parts.append(rms_rows(proj_n[:, 0], q_gain).astype(bf16))
        k_parts.append(rms_rows(proj_n[:, 1], k_gain).astype(bf16))
        v_parts.append(proj_n[:, 2].astype(bf16))
    residual = jnp.concatenate(residual_parts, axis=0)
    query_hat = jnp.concatenate(q_parts, axis=0)
    key_hat = jnp.concatenate(k_parts, axis=0)
    value_two = jnp.concatenate(v_parts, axis=0)

    key_value = jnp.stack([key_hat, value_two], axis=1).reshape(tok_rows, 2 * inner_dev)
    plane_tiles = GY * GZ
    widened = with_halo(key_value, (("ctx", 0),), plane_tiles * TILE)
    buffer_rows = widened.shape[0]
    buffer_tiles = buffer_rows // TILE
    tile_count = tok_rows // TILE
    base_tile = ctx_index * tile_count - plane_tiles
    widened = widened.reshape(buffer_rows, 2, heads_dev, head_dim)
    buffer_ids = base_tile + jnp.arange(buffer_tiles, dtype=jnp.int32)
    valid = jnp.any(
        (neighbours[:, :, None] == buffer_ids[None, None, :]) & (neighbours[:, :, None] >= 0),
        axis=1,
    )
    valid_keys = jnp.repeat(valid, TILE, axis=1)
    query_tiles = query_hat.reshape(tile_count, TILE, heads_dev, head_dim)
    score_scale = 1.0 / math.sqrt(head_dim)
    tile_scores = (
        jnp.einsum(
            "pthe,she->phts", query_tiles, widened[:, 0], preferred_element_type=f32
        )
        * score_scale
    )
    unnormed = jnp.where(valid_keys[:, None, None, :], jnp.exp(tile_scores), 0.0)
    weights = (unnormed / jnp.sum(unnormed, axis=-1, keepdims=True)).astype(bf16)
    attn_two = jnp.einsum("phts,she->pthe", weights, widened[:, 1], preferred_element_type=f32)
    attn_two = attn_two.astype(bf16).reshape(tok_rows, inner_dev)
    summed_two = lax.psum_scatter(
        jnp.dot(attn_two, w_out2, preferred_element_type=f32).astype(bf16),
        "head",
        scatter_dimension=0,
        tiled=True,
    ).astype(f32)
    residual_mine = lax.dynamic_slice_in_dim(residual, head_index * rows_mine, rows_mine, 0)
    return (residual_mine.astype(f32) + summed_two).astype(bf16)


def solution(mesh):
    in_specs = (
        P(("groups", "ctx"), None),
        P(),
        P(None, None, "head"),
        P("head"),
        P("head", None),
        P(),
        P(None, None, "head"),
        P(),
        P(),
        P("head", None),
        P("ctx", None),
    )
    out_specs = P(("groups", "ctx", "head"), None)
    return jax.shard_map(
        on_device, mesh=mesh, in_specs=in_specs, out_specs=out_specs, check_vma=False
    )
```

```python
import math

import jax
import jax.numpy as jnp
import numpy as np
from jax import lax
from jax.sharding import PartitionSpec as P

TILE = 256
GY = 2
GZ = 2


EPS = 1e-06


def with_halo(shard, sides, width):
    for axis, dim in sides:
        size, length = (lax.axis_size(axis), shard.shape[dim])
        up = [(i, (i + 1) % size) for i in range(size - 1)]
        down = [(j, i) for i, j in up]
        last = lax.slice_in_dim(shard, length - width, length, axis=dim)
        first = lax.slice_in_dim(shard, 0, width, axis=dim)
        before = lax.ppermute(last, axis, up)
        after = lax.ppermute(first, axis, down)
        shard = jnp.concatenate([before, shard, after], axis=dim)
    return shard


def rms_rows(value, gain):
    mean_sq = jnp.mean(value * value, axis=-1, keepdims=True)
    return value * lax.rsqrt(mean_sq + EPS) * gain


def feature_map(value):
    return jnp.where(value > 0, value + 1.0, jnp.exp(jnp.minimum(value, 0.0)))


def split_two(value):
    high_part = value.astype(jnp.bfloat16)
    low_part = (value - high_part.astype(jnp.float32)).astype(jnp.bfloat16)
    return (high_part, low_part)


def on_device(
    tokens, norm_one, w_qkv1, lin_gain, w_out1, norm_two, w_qkv2, q_gain, k_gain, w_out2, neighbours
):
    f32, bf16 = jnp.float32, jnp.bfloat16
    tok_rows, feature_width = tokens.shape
    inner_dev = w_qkv1.shape[2]
    head_dim = q_gain.shape[0]
    heads_dev = inner_dev // head_dim
    block_rows = 2 * TILE
    block_count = tok_rows // block_rows
    rows_mine = tok_rows // lax.axis_size("head")
    head_index = lax.axis_index("head")
    ctx_index = lax.axis_index("ctx")
    ctx_size = lax.axis_size("ctx")

    normed = rms_rows(tokens.astype(f32), norm_one).astype(bf16)
    projected = jnp.dot(
        normed, w_qkv1.reshape(feature_width, 3 * inner_dev), preferred_element_type=f32
    )
    projected = projected.reshape(tok_rows, 3, heads_dev, head_dim)
    query_map = feature_map(projected[:, 0]).astype(bf16)
    key_map = feature_map(projected[:, 1]).astype(bf16)
    value_one = projected[:, 2].astype(bf16)
    q_blocks = query_map.reshape(block_count, block_rows, heads_dev, head_dim)
    k_blocks = key_map.reshape(block_count, block_rows, heads_dev, head_dim)
    v_blocks = value_one.reshape(block_count, block_rows, heads_dev, head_dim)
    block_states = jnp.einsum(
        "nthe,nthf->nhef", k_blocks, v_blocks, preferred_element_type=f32
    )
    own_total = jnp.sum(block_states, axis=0)
    all_totals = lax.all_gather(own_total.astype(bf16), "ctx", axis=0).astype(f32)
    earlier_dev = jnp.arange(ctx_size, dtype=jnp.int32) < ctx_index
    carried = jnp.sum(jnp.where(earlier_dev[:, None, None, None], all_totals, 0.0), axis=0)

    causal = lax.broadcasted_iota(jnp.int32, (block_rows, block_rows), 0) >= lax.broadcasted_iota(
        jnp.int32, (block_rows, block_rows), 1
    )
    w_qkv2_flat = w_qkv2.reshape(feature_width, 3 * inner_dev)
    residual_parts = []
    q_parts, k_parts, v_parts = [], [], []
    previous = None
    for n in range(block_count):
        q_n, k_n, v_n = q_blocks[n], k_blocks[n], v_blocks[n]
        scores = jnp.einsum("the,she->hts", q_n, k_n, preferred_element_type=f32)
        scores = jnp.where(causal, scores, 0.0)
        score_high, score_low = split_two(scores)
        within = jnp.einsum("hts,she->the", score_high, v_n, preferred_element_type=f32)
        within = within + jnp.einsum("hts,she->the", score_low, v_n, preferred_element_type=f32)
        state_high, state_low = split_two(carried)
        carried_term = jnp.einsum("the,hef->thf", q_n, state_high, preferred_element_type=f32)
        carried_term = carried_term + jnp.einsum(
            "the,hef->thf", q_n, state_low, preferred_element_type=f32
        )
        carried = carried + block_states[n]
        combined = within + carried_term
        attn_n = (
            rms_rows(combined, lin_gain.reshape(heads_dev, head_dim))
            .astype(bf16)
            .reshape(block_rows, inner_dev)
        )
        partial = jnp.dot(attn_n, w_out1, preferred_element_type=f32).astype(bf16)
        if previous is not None:
            partial, previous = lax.optimization_barrier((partial, previous))
            residual_parts[-1] = previous
        summed = lax.psum(partial, "head").astype(f32)
        tokens_n = tokens[n * block_rows : (n + 1) * block_rows].astype(f32)
        residual_n = (tokens_n + summed).astype(bf16)
        residual_parts.append(residual_n)
        previous = residual_n
        normed_n = rms_rows(residual_n.astype(f32), norm_two).astype(bf16)
        proj_n = jnp.dot(normed_n, w_qkv2_flat, preferred_element_type=f32)
        proj_n = proj_n.reshape(block_rows, 3, heads_dev, head_dim)
        q_parts.append(rms_rows(proj_n[:, 0], q_gain).astype(bf16))
        k_parts.append(rms_rows(proj_n[:, 1], k_gain).astype(bf16))
        v_parts.append(proj_n[:, 2].astype(bf16))
    residual = jnp.concatenate(residual_parts, axis=0)
    query_hat = jnp.concatenate(q_parts, axis=0)
    key_hat = jnp.concatenate(k_parts, axis=0)
    value_two = jnp.concatenate(v_parts, axis=0)

    plane_tiles = GY * GZ
    halo_rows = plane_tiles * TILE
    tile_count = tok_rows // TILE
    head_size = lax.axis_size("head")
    up = [(i, i + 1) for i in range(ctx_size - 1)]
    down = [(i + 1, i) for i in range(ctx_size - 1)]
    key_prev = lax.ppermute(key_hat[tok_rows - halo_rows :], "ctx", up)
    value_prev = lax.ppermute(value_two[tok_rows - halo_rows :], "ctx", up)
    key_next = lax.ppermute(key_hat[:halo_rows], "ctx", down)
    value_next = lax.ppermute(value_two[:halo_rows], "ctx", down)
    own_first = ctx_index * tile_count
    arange_halo = jnp.arange(plane_tiles, dtype=jnp.int32)
    pieces = (
        (key_prev, value_prev, own_first - plane_tiles + arange_halo),
        (key_hat, value_two, own_first + jnp.arange(tile_count, dtype=jnp.int32)),
        (key_next, value_next, own_first + tile_count + arange_halo),
    )
    present = neighbours >= 0
    tile_masks = [
        jnp.any((neighbours[:, :, None] == ids[None, None, :]) & present[:, :, None], axis=1)
        for _, _, ids in pieces
    ]
    score_scale = 1.0 / math.sqrt(head_dim)
    chunks = 2 if rows_mine % 2 == 0 else 1
    part_rows = rows_mine // chunks
    mixed_parts = []
    for c in range(chunks):
        rows = (
            np.arange(head_size)[:, None] * rows_mine + c * part_rows + np.arange(part_rows)[None, :]
        ).reshape(-1)
        row_tiles = rows // TILE
        q_c = query_hat.reshape(head_size, chunks, part_rows, heads_dev, head_dim)[:, c]
        q_c = q_c.reshape(head_size * part_rows, heads_dev, head_dim)
        exps, total = [], 0.0
        for (keys, _, _), mask in zip(pieces, tile_masks):
            key_ok = jnp.repeat(mask[row_tiles], TILE, axis=1)
            scores = (
                jnp.einsum("the,she->hts", q_c, keys, preferred_element_type=f32) * score_scale
            )
            unnormed = jnp.where(key_ok[None], jnp.exp(scores), 0.0)
            exps.append(unnormed)
            total = total + jnp.sum(unnormed, axis=-1, keepdims=True)
        attn_c = 0.0
        for (_, values, _), unnormed in zip(pieces, exps):
            weights = (unnormed / total).astype(bf16)
            attn_c = attn_c + jnp.einsum(
                "hts,she->the", weights, values, preferred_element_type=f32
            )
        attn_c = attn_c.astype(bf16).reshape(head_size * part_rows, inner_dev)
        mixed_parts.append(
            lax.psum_scatter(
                jnp.dot(attn_c, w_out2, preferred_element_type=f32).astype(bf16),
                "head",
                scatter_dimension=0,
                tiled=True,
            )
        )
    summed_two = jnp.concatenate(mixed_parts, axis=0).astype(f32)
    residual_mine = lax.dynamic_slice_in_dim(residual, head_index * rows_mine, rows_mine, 0)
    return (residual_mine.astype(f32) + summed_two).astype(bf16)


def solution(mesh):
    in_specs = (
        P(("groups", "ctx"), None),
        P(),
        P(None, None, "head"),
        P("head"),
        P("head", None),
        P(),
        P(None, None, "head"),
        P(),
        P(),
        P("head", None),
        P("ctx", None),
    )
    out_specs = P(("groups", "ctx", "head"), None)
    return jax.shard_map(
        on_device, mesh=mesh, in_specs=in_specs, out_specs=out_specs, check_vma=False
    )
```

```python
import functools
import math

import jax
import jax.numpy as jnp
import numpy as np
from jax import lax
from jax.experimental import pallas as pl
from jax.sharding import PartitionSpec as P

TILE = 256
GY = 2
GZ = 2


EPS = 1e-06


def with_halo(shard, sides, width):
    for axis, dim in sides:
        size, length = (lax.axis_size(axis), shard.shape[dim])
        up = [(i, (i + 1) % size) for i in range(size - 1)]
        down = [(j, i) for i, j in up]
        last = lax.slice_in_dim(shard, length - width, length, axis=dim)
        first = lax.slice_in_dim(shard, 0, width, axis=dim)
        before = lax.ppermute(last, axis, up)
        after = lax.ppermute(first, axis, down)
        shard = jnp.concatenate([before, shard, after], axis=dim)
    return shard


def rms_rows(value, gain):
    mean_sq = jnp.mean(value * value, axis=-1, keepdims=True)
    return value * lax.rsqrt(mean_sq + EPS) * gain


def feature_map(value):
    return jnp.where(value > 0, value + 1.0, jnp.exp(jnp.minimum(value, 0.0)))


def split_two(value):
    high_part = value.astype(jnp.bfloat16)
    low_part = (value - high_part.astype(jnp.float32)).astype(jnp.bfloat16)
    return (high_part, low_part)


def _attn_kernel(q_ref, kp_ref, ko_ref, kn_ref, vp_ref, vo_ref, vn_ref, m_ref, o_ref, *, scale):
    query = q_ref[...]
    mask = m_ref[0]
    exps = []
    total = None
    offset = 0
    for k_ref in (kp_ref, ko_ref, kn_ref):
        rows = k_ref.shape[0]
        scores = (
            lax.dot_general(
                query, k_ref[...], (((1,), (1,)), ((), ())), preferred_element_type=jnp.float32
            )
            * scale
        )
        unnormed = jnp.where(mask[:, offset : offset + rows] > 0.5, jnp.exp(scores), 0.0)
        exps.append(unnormed)
        part = jnp.sum(unnormed, axis=-1, keepdims=True)
        total = part if total is None else total + part
        offset += rows
    acc = None
    for unnormed, v_ref in zip(exps, (vp_ref, vo_ref, vn_ref)):
        weights = (unnormed / total).astype(jnp.bfloat16)
        term = jnp.dot(weights, v_ref[...], preferred_element_type=jnp.float32)
        acc = term if acc is None else acc + term
    o_ref[...] = acc.astype(o_ref.dtype)


def tile_attention(query, keys, values, mask, block_rows, head_dim, interpret=False):
    rows, inner = query.shape
    heads = inner // head_dim
    blocks = rows // block_rows
    key_width = mask.shape[-1]
    kv_specs = [pl.BlockSpec((k.shape[0], head_dim), lambda h, b: (0, h)) for k in keys]
    return pl.pallas_call(
        functools.partial(_attn_kernel, scale=1.0 / math.sqrt(head_dim)),
        out_shape=jax.ShapeDtypeStruct((rows, inner), jnp.bfloat16),
        grid=(heads, blocks),
        in_specs=[pl.BlockSpec((block_rows, head_dim), lambda h, b: (b, h))]
        + kv_specs
        + kv_specs
        + [pl.BlockSpec((1, 1, key_width), lambda h, b: (b, 0, 0))],
        out_specs=pl.BlockSpec((block_rows, head_dim), lambda h, b: (b, h)),
        interpret=interpret,
    )(query, *keys, *values, mask)


def on_device(
    tokens, norm_one, w_qkv1, lin_gain, w_out1, norm_two, w_qkv2, q_gain, k_gain, w_out2, neighbours
):
    f32, bf16 = jnp.float32, jnp.bfloat16
    tok_rows, feature_width = tokens.shape
    inner_dev = w_qkv1.shape[2]
    head_dim = q_gain.shape[0]
    heads_dev = inner_dev // head_dim
    block_rows = 2 * TILE
    block_count = tok_rows // block_rows
    rows_mine = tok_rows // lax.axis_size("head")
    head_index = lax.axis_index("head")
    ctx_index = lax.axis_index("ctx")
    ctx_size = lax.axis_size("ctx")

    normed = rms_rows(tokens.astype(f32), norm_one).astype(bf16)
    projected = jnp.dot(
        normed, w_qkv1.reshape(feature_width, 3 * inner_dev), preferred_element_type=f32
    )
    projected = projected.reshape(tok_rows, 3, heads_dev, head_dim)
    query_map = feature_map(projected[:, 0]).astype(bf16)
    key_map = feature_map(projected[:, 1]).astype(bf16)
    value_one = projected[:, 2].astype(bf16)
    q_blocks = query_map.reshape(block_count, block_rows, heads_dev, head_dim)
    k_blocks = key_map.reshape(block_count, block_rows, heads_dev, head_dim)
    v_blocks = value_one.reshape(block_count, block_rows, heads_dev, head_dim)
    block_states = jnp.einsum(
        "nthe,nthf->nhef", k_blocks, v_blocks, preferred_element_type=f32
    )
    own_total = jnp.sum(block_states, axis=0)
    all_totals = lax.all_gather(own_total.astype(bf16), "ctx", axis=0).astype(f32)
    earlier_dev = jnp.arange(ctx_size, dtype=jnp.int32) < ctx_index
    carried = jnp.sum(jnp.where(earlier_dev[:, None, None, None], all_totals, 0.0), axis=0)

    causal = lax.broadcasted_iota(jnp.int32, (block_rows, block_rows), 0) >= lax.broadcasted_iota(
        jnp.int32, (block_rows, block_rows), 1
    )
    w_qkv2_flat = w_qkv2.reshape(feature_width, 3 * inner_dev)
    residual_parts = []
    q_parts, k_parts, v_parts = [], [], []
    previous = None
    for n in range(block_count):
        q_n, k_n, v_n = q_blocks[n], k_blocks[n], v_blocks[n]
        scores = jnp.einsum("the,she->hts", q_n, k_n, preferred_element_type=f32)
        scores = jnp.where(causal, scores, 0.0)
        score_high, score_low = split_two(scores)
        within = jnp.einsum("hts,she->the", score_high, v_n, preferred_element_type=f32)
        within = within + jnp.einsum("hts,she->the", score_low, v_n, preferred_element_type=f32)
        state_high, state_low = split_two(carried)
        carried_term = jnp.einsum("the,hef->thf", q_n, state_high, preferred_element_type=f32)
        carried_term = carried_term + jnp.einsum(
            "the,hef->thf", q_n, state_low, preferred_element_type=f32
        )
        carried = carried + block_states[n]
        combined = within + carried_term
        attn_n = (
            rms_rows(combined, lin_gain.reshape(heads_dev, head_dim))
            .astype(bf16)
            .reshape(block_rows, inner_dev)
        )
        partial = jnp.dot(attn_n, w_out1, preferred_element_type=f32).astype(bf16)
        if previous is not None:
            partial, previous = lax.optimization_barrier((partial, previous))
            residual_parts[-1] = previous
        summed = lax.psum(partial, "head").astype(f32)
        tokens_n = tokens[n * block_rows : (n + 1) * block_rows].astype(f32)
        residual_n = (tokens_n + summed).astype(bf16)
        residual_parts.append(residual_n)
        previous = residual_n
        normed_n = rms_rows(residual_n.astype(f32), norm_two).astype(bf16)
        proj_n = jnp.dot(normed_n, w_qkv2_flat, preferred_element_type=f32)
        proj_n = proj_n.reshape(block_rows, 3, heads_dev, head_dim)
        q_parts.append(rms_rows(proj_n[:, 0], q_gain).astype(bf16))
        k_parts.append(rms_rows(proj_n[:, 1], k_gain).astype(bf16))
        v_parts.append(proj_n[:, 2].astype(bf16))
    residual = jnp.concatenate(residual_parts, axis=0)
    query_hat = jnp.concatenate(q_parts, axis=0)
    key_hat = jnp.concatenate(k_parts, axis=0)
    value_two = jnp.concatenate(v_parts, axis=0)

    plane_tiles = GY * GZ
    halo_rows = plane_tiles * TILE
    tile_count = tok_rows // TILE
    head_size = lax.axis_size("head")
    up = [(i, i + 1) for i in range(ctx_size - 1)]
    down = [(i + 1, i) for i in range(ctx_size - 1)]
    key_prev = lax.ppermute(key_hat[tok_rows - halo_rows :], "ctx", up)
    value_prev = lax.ppermute(value_two[tok_rows - halo_rows :], "ctx", up)
    key_next = lax.ppermute(key_hat[:halo_rows], "ctx", down)
    value_next = lax.ppermute(value_two[:halo_rows], "ctx", down)
    own_first = ctx_index * tile_count
    arange_halo = jnp.arange(plane_tiles, dtype=jnp.int32)
    pieces = (
        (key_prev, value_prev, own_first - plane_tiles + arange_halo),
        (key_hat, value_two, own_first + jnp.arange(tile_count, dtype=jnp.int32)),
        (key_next, value_next, own_first + tile_count + arange_halo),
    )
    present = neighbours >= 0
    tile_masks = [
        jnp.any((neighbours[:, :, None] == ids[None, None, :]) & present[:, :, None], axis=1)
        for _, _, ids in pieces
    ]
    chunks = 2 if rows_mine % 2 == 0 else 1
    part_rows = rows_mine // chunks
    keys = [p[0].reshape(-1, inner_dev) for p in pieces]
    values = [p[1].reshape(-1, inner_dev) for p in pieces]
    key_ok = jnp.repeat(jnp.concatenate(tile_masks, axis=1), TILE, axis=1).astype(f32)
    mixed_parts = []
    for c in range(chunks):
        block_tiles = (np.arange(head_size) * rows_mine + c * part_rows) // TILE
        q_c = query_hat.reshape(head_size, chunks, part_rows, inner_dev)[:, c]
        q_c = q_c.reshape(head_size * part_rows, inner_dev)
        mask_c = key_ok[block_tiles][:, None, :]
        attn_c = tile_attention(q_c, keys, values, mask_c, part_rows, head_dim)
        mixed_parts.append(
            lax.psum_scatter(
                jnp.dot(attn_c, w_out2, preferred_element_type=f32).astype(bf16),
                "head",
                scatter_dimension=0,
                tiled=True,
            )
        )
    summed_two = jnp.concatenate(mixed_parts, axis=0).astype(f32)
    residual_mine = lax.dynamic_slice_in_dim(residual, head_index * rows_mine, rows_mine, 0)
    return (residual_mine.astype(f32) + summed_two).astype(bf16)


def solution(mesh):
    in_specs = (
        P(("groups", "ctx"), None),
        P(),
        P(None, None, "head"),
        P("head"),
        P("head", None),
        P(),
        P(None, None, "head"),
        P(),
        P(),
        P("head", None),
        P("ctx", None),
    )
    out_specs = P(("groups", "ctx", "head"), None)
    return jax.shard_map(
        on_device, mesh=mesh, in_specs=in_specs, out_specs=out_specs, check_vma=False
    )
```

```python
import functools
import math

import jax
import jax.numpy as jnp
import numpy as np
from jax import lax
from jax.experimental import pallas as pl
from jax.sharding import PartitionSpec as P

TILE = 256
GY = 2
GZ = 2


EPS = 1e-06


def with_halo(shard, sides, width):
    for axis, dim in sides:
        size, length = (lax.axis_size(axis), shard.shape[dim])
        up = [(i, (i + 1) % size) for i in range(size - 1)]
        down = [(j, i) for i, j in up]
        last = lax.slice_in_dim(shard, length - width, length, axis=dim)
        first = lax.slice_in_dim(shard, 0, width, axis=dim)
        before = lax.ppermute(last, axis, up)
        after = lax.ppermute(first, axis, down)
        shard = jnp.concatenate([before, shard, after], axis=dim)
    return shard


def rms_rows(value, gain):
    mean_sq = jnp.mean(value * value, axis=-1, keepdims=True)
    return value * lax.rsqrt(mean_sq + EPS) * gain


def feature_map(value):
    return jnp.where(value > 0, value + 1.0, jnp.exp(jnp.minimum(value, 0.0)))


def split_two(value):
    high_part = value.astype(jnp.bfloat16)
    low_part = (value - high_part.astype(jnp.float32)).astype(jnp.bfloat16)
    return (high_part, low_part)


def _attn_kernel(q_ref, kp_ref, ko_ref, kn_ref, vp_ref, vo_ref, vn_ref, m_ref, o_ref, *, scale):
    query = q_ref[...]
    mask = m_ref[0]
    exps = []
    total = None
    offset = 0
    for k_ref in (kp_ref, ko_ref, kn_ref):
        rows = k_ref.shape[0]
        scores = (
            lax.dot_general(
                query, k_ref[...], (((1,), (1,)), ((), ())), preferred_element_type=jnp.float32
            )
            * scale
        )
        unnormed = jnp.where(mask[:, offset : offset + rows] > 0.5, jnp.exp(scores), 0.0)
        exps.append(unnormed)
        part = jnp.sum(unnormed, axis=-1, keepdims=True)
        total = part if total is None else total + part
        offset += rows
    acc = None
    for unnormed, v_ref in zip(exps, (vp_ref, vo_ref, vn_ref)):
        weights = (unnormed / total).astype(jnp.bfloat16)
        term = jnp.dot(weights, v_ref[...], preferred_element_type=jnp.float32)
        acc = term if acc is None else acc + term
    o_ref[...] = acc.astype(o_ref.dtype)


def tile_attention(query, keys, values, mask, block_rows, interpret=False):
    heads, rows, head_dim = query.shape
    blocks = rows // block_rows
    key_width = mask.shape[-1]
    kv_specs = [pl.BlockSpec((None, k.shape[1], head_dim), lambda h, b: (h, 0, 0)) for k in keys]
    return pl.pallas_call(
        functools.partial(_attn_kernel, scale=1.0 / math.sqrt(head_dim)),
        out_shape=jax.ShapeDtypeStruct((heads, rows, head_dim), jnp.bfloat16),
        grid=(heads, blocks),
        in_specs=[pl.BlockSpec((None, block_rows, head_dim), lambda h, b: (h, b, 0))]
        + kv_specs
        + kv_specs
        + [pl.BlockSpec((1, 1, key_width), lambda h, b: (b, 0, 0))],
        out_specs=pl.BlockSpec((None, block_rows, head_dim), lambda h, b: (h, b, 0)),
        interpret=interpret,
    )(query, *keys, *values, mask)

def on_device(
    tokens, norm_one, w_qkv1, lin_gain, w_out1, norm_two, w_qkv2, q_gain, k_gain, w_out2, neighbours
):
    f32, bf16 = jnp.float32, jnp.bfloat16
    tok_rows, feature_width = tokens.shape
    inner_dev = w_qkv1.shape[2]
    head_dim = q_gain.shape[0]
    heads_dev = inner_dev // head_dim
    block_rows = 2 * TILE
    block_count = tok_rows // block_rows
    rows_mine = tok_rows // lax.axis_size("head")
    head_index = lax.axis_index("head")
    ctx_index = lax.axis_index("ctx")
    ctx_size = lax.axis_size("ctx")

    normed = rms_rows(tokens.astype(f32), norm_one).astype(bf16)
    projected = jnp.dot(
        normed, w_qkv1.reshape(feature_width, 3 * inner_dev), preferred_element_type=f32
    )
    projected = projected.reshape(tok_rows, 3, heads_dev, head_dim)
    query_map = feature_map(projected[:, 0]).astype(bf16)
    key_map = feature_map(projected[:, 1]).astype(bf16)
    value_one = projected[:, 2].astype(bf16)
    q_blocks = query_map.reshape(block_count, block_rows, heads_dev, head_dim)
    k_blocks = key_map.reshape(block_count, block_rows, heads_dev, head_dim)
    v_blocks = value_one.reshape(block_count, block_rows, heads_dev, head_dim)
    block_states = jnp.einsum(
        "nthe,nthf->nhef", k_blocks, v_blocks, preferred_element_type=f32
    )
    own_total = jnp.sum(block_states, axis=0)
    all_totals = lax.all_gather(own_total.astype(bf16), "ctx", axis=0).astype(f32)
    earlier_dev = jnp.arange(ctx_size, dtype=jnp.int32) < ctx_index
    carried = jnp.sum(jnp.where(earlier_dev[:, None, None, None], all_totals, 0.0), axis=0)

    causal = lax.broadcasted_iota(jnp.int32, (block_rows, block_rows), 0) >= lax.broadcasted_iota(
        jnp.int32, (block_rows, block_rows), 1
    )
    w_qkv2_flat = w_qkv2.reshape(feature_width, 3 * inner_dev)
    residual_parts = []
    q_parts, k_parts, v_parts = [], [], []
    previous = None
    for n in range(block_count):
        q_n, k_n, v_n = q_blocks[n], k_blocks[n], v_blocks[n]
        scores = jnp.einsum("the,she->hts", q_n, k_n, preferred_element_type=f32)
        scores = jnp.where(causal, scores, 0.0)
        score_high, score_low = split_two(scores)
        within = jnp.einsum("hts,she->the", score_high, v_n, preferred_element_type=f32)
        within = within + jnp.einsum("hts,she->the", score_low, v_n, preferred_element_type=f32)
        state_high, state_low = split_two(carried)
        carried_term = jnp.einsum("the,hef->thf", q_n, state_high, preferred_element_type=f32)
        carried_term = carried_term + jnp.einsum(
            "the,hef->thf", q_n, state_low, preferred_element_type=f32
        )
        carried = carried + block_states[n]
        combined = within + carried_term
        attn_n = (
            rms_rows(combined, lin_gain.reshape(heads_dev, head_dim))
            .astype(bf16)
            .reshape(block_rows, inner_dev)
        )
        partial = jnp.dot(attn_n, w_out1, preferred_element_type=f32).astype(bf16)
        if previous is not None:
            partial, previous = lax.optimization_barrier((partial, previous))
            residual_parts[-1] = previous
        summed = lax.psum(partial, "head").astype(f32)
        tokens_n = tokens[n * block_rows : (n + 1) * block_rows].astype(f32)
        residual_n = (tokens_n + summed).astype(bf16)
        residual_parts.append(residual_n)
        previous = residual_n
        normed_n = rms_rows(residual_n.astype(f32), norm_two).astype(bf16)
        proj_n = jnp.dot(normed_n, w_qkv2_flat, preferred_element_type=f32)
        proj_n = proj_n.reshape(block_rows, 3, heads_dev, head_dim)
        q_parts.append(rms_rows(proj_n[:, 0], q_gain).astype(bf16))
        k_parts.append(rms_rows(proj_n[:, 1], k_gain).astype(bf16))
        v_parts.append(proj_n[:, 2].astype(bf16))
    residual = jnp.concatenate(residual_parts, axis=0)
    query_hat = jnp.concatenate(q_parts, axis=0)
    key_hat = jnp.concatenate(k_parts, axis=0)
    value_two = jnp.concatenate(v_parts, axis=0)

    plane_tiles = GY * GZ
    halo_rows = plane_tiles * TILE
    tile_count = tok_rows // TILE
    head_size = lax.axis_size("head")
    up = [(i, i + 1) for i in range(ctx_size - 1)]
    down = [(i + 1, i) for i in range(ctx_size - 1)]
    key_hat = jnp.transpose(key_hat, (1, 0, 2))
    value_two = jnp.transpose(value_two, (1, 0, 2))
    query_hat = jnp.transpose(query_hat, (1, 0, 2))
    key_prev = lax.ppermute(key_hat[:, tok_rows - halo_rows :], "ctx", up)
    value_prev = lax.ppermute(value_two[:, tok_rows - halo_rows :], "ctx", up)
    key_next = lax.ppermute(key_hat[:, :halo_rows], "ctx", down)
    value_next = lax.ppermute(value_two[:, :halo_rows], "ctx", down)
    own_first = ctx_index * tile_count
    arange_halo = jnp.arange(plane_tiles, dtype=jnp.int32)
    pieces = (
        (key_prev, value_prev, own_first - plane_tiles + arange_halo),
        (key_hat, value_two, own_first + jnp.arange(tile_count, dtype=jnp.int32)),
        (key_next, value_next, own_first + tile_count + arange_halo),
    )
    present = neighbours >= 0
    tile_masks = [
        jnp.any((neighbours[:, :, None] == ids[None, None, :]) & present[:, :, None], axis=1)
        for _, _, ids in pieces
    ]
    chunks = 2 if rows_mine % 2 == 0 else 1
    part_rows = rows_mine // chunks
    keys = [p[0] for p in pieces]
    values = [p[1] for p in pieces]
    w_out2_heads = w_out2.reshape(heads_dev, head_dim, w_out2.shape[1])
    key_ok = jnp.repeat(jnp.concatenate(tile_masks, axis=1), TILE, axis=1).astype(f32)
    mixed_parts = []
    for c in range(chunks):
        block_tiles = (np.arange(head_size) * rows_mine + c * part_rows) // TILE
        q_c = query_hat.reshape(heads_dev, head_size, chunks, part_rows, head_dim)[:, :, c]
        q_c = q_c.reshape(heads_dev, head_size * part_rows, head_dim)
        mask_c = key_ok[block_tiles][:, None, :]
        attn_c = tile_attention(q_c, keys, values, mask_c, part_rows)
        out_c = jnp.einsum("hte,hef->tf", attn_c, w_out2_heads, preferred_element_type=f32)
        mixed_parts.append(
            lax.psum_scatter(
                out_c.astype(bf16),
                "head",
                scatter_dimension=0,
                tiled=True,
            )
        )
    summed_two = jnp.concatenate(mixed_parts, axis=0).astype(f32)
    residual_mine = lax.dynamic_slice_in_dim(residual, head_index * rows_mine, rows_mine, 0)
    return (residual_mine.astype(f32) + summed_two).astype(bf16)


def solution(mesh):
    in_specs = (
        P(("groups", "ctx"), None),
        P(),
        P(None, None, "head"),
        P("head"),
        P("head", None),
        P(),
        P(None, None, "head"),
        P(),
        P(),
        P("head", None),
        P("ctx", None),
    )
    out_specs = P(("groups", "ctx", "head"), None)
    return jax.shard_map(
        on_device, mesh=mesh, in_specs=in_specs, out_specs=out_specs, check_vma=False
    )
```

```python
import functools
import math

import jax
import jax.numpy as jnp
import numpy as np
from jax import lax
from jax.experimental import pallas as pl
from jax.sharding import PartitionSpec as P

TILE = 256
GY = 2
GZ = 2


EPS = 1e-06


def with_halo(shard, sides, width):
    for axis, dim in sides:
        size, length = (lax.axis_size(axis), shard.shape[dim])
        up = [(i, (i + 1) % size) for i in range(size - 1)]
        down = [(j, i) for i, j in up]
        last = lax.slice_in_dim(shard, length - width, length, axis=dim)
        first = lax.slice_in_dim(shard, 0, width, axis=dim)
        before = lax.ppermute(last, axis, up)
        after = lax.ppermute(first, axis, down)
        shard = jnp.concatenate([before, shard, after], axis=dim)
    return shard


def rms_rows(value, gain):
    mean_sq = jnp.mean(value * value, axis=-1, keepdims=True)
    return value * lax.rsqrt(mean_sq + EPS) * gain


def feature_map(value):
    return jnp.where(value > 0, value + 1.0, jnp.exp(jnp.minimum(value, 0.0)))


def split_two(value):
    high_part = value.astype(jnp.bfloat16)
    low_part = (value - high_part.astype(jnp.float32)).astype(jnp.bfloat16)
    return (high_part, low_part)


def _attn_kernel(q_ref, kp_ref, ko_ref, kn_ref, vp_ref, vo_ref, vn_ref, m_ref, o_ref, *, scale):
    query = q_ref[...]
    mask = m_ref[0]
    exps = []
    total = None
    offset = 0
    for k_ref in (kp_ref, ko_ref, kn_ref):
        rows = k_ref.shape[0]
        scores = (
            lax.dot_general(
                query, k_ref[...], (((1,), (1,)), ((), ())), preferred_element_type=jnp.float32
            )
            * scale
        )
        unnormed = jnp.where(mask[:, offset : offset + rows] > 0.5, jnp.exp(scores), 0.0)
        exps.append(unnormed)
        part = jnp.sum(unnormed, axis=-1, keepdims=True)
        total = part if total is None else total + part
        offset += rows
    acc = None
    for unnormed, v_ref in zip(exps, (vp_ref, vo_ref, vn_ref)):
        weights = (unnormed / total).astype(jnp.bfloat16)
        term = jnp.dot(weights, v_ref[...], preferred_element_type=jnp.float32)
        acc = term if acc is None else acc + term
    o_ref[...] = acc.astype(o_ref.dtype)


def tile_attention(query, keys, values, mask, block_rows, interpret=False):
    heads, rows, head_dim = query.shape
    blocks = rows // block_rows
    key_width = mask.shape[-1]
    kv_specs = [pl.BlockSpec((None, k.shape[1], head_dim), lambda h, b: (h, 0, 0)) for k in keys]
    return pl.pallas_call(
        functools.partial(_attn_kernel, scale=1.0 / math.sqrt(head_dim)),
        out_shape=jax.ShapeDtypeStruct((heads, rows, head_dim), jnp.bfloat16),
        grid=(heads, blocks),
        in_specs=[pl.BlockSpec((None, block_rows, head_dim), lambda h, b: (h, b, 0))]
        + kv_specs
        + kv_specs
        + [pl.BlockSpec((1, 1, key_width), lambda h, b: (b, 0, 0))],
        out_specs=pl.BlockSpec((None, block_rows, head_dim), lambda h, b: (h, b, 0)),
        interpret=interpret,
    )(query, *keys, *values, mask)

def on_device(
    tokens, norm_one, w_qkv1, lin_gain, w_out1, norm_two, w_qkv2, q_gain, k_gain, w_out2, neighbours
):
    f32, bf16 = jnp.float32, jnp.bfloat16
    tok_rows, feature_width = tokens.shape
    inner_dev = w_qkv1.shape[2]
    head_dim = q_gain.shape[0]
    heads_dev = inner_dev // head_dim
    block_rows = 2 * TILE
    block_count = tok_rows // block_rows
    rows_mine = tok_rows // lax.axis_size("head")
    head_index = lax.axis_index("head")
    ctx_index = lax.axis_index("ctx")
    ctx_size = lax.axis_size("ctx")

    normed = rms_rows(tokens.astype(f32), norm_one).astype(bf16)
    projected = jnp.dot(
        normed, w_qkv1.reshape(feature_width, 3 * inner_dev), preferred_element_type=f32
    )
    projected = projected.reshape(tok_rows, 3, heads_dev, head_dim)
    query_map = feature_map(projected[:, 0]).astype(bf16)
    key_map = feature_map(projected[:, 1]).astype(bf16)
    value_one = projected[:, 2].astype(bf16)
    q_blocks = query_map.reshape(block_count, block_rows, heads_dev, head_dim)
    k_blocks = key_map.reshape(block_count, block_rows, heads_dev, head_dim)
    v_blocks = value_one.reshape(block_count, block_rows, heads_dev, head_dim)
    block_states = jnp.einsum(
        "nthe,nthf->nhef", k_blocks, v_blocks, preferred_element_type=f32
    )
    own_total = jnp.sum(block_states, axis=0)
    all_totals = lax.all_gather(own_total.astype(bf16), "ctx", axis=0).astype(f32)
    earlier_dev = jnp.arange(ctx_size, dtype=jnp.int32) < ctx_index
    carried = jnp.sum(jnp.where(earlier_dev[:, None, None, None], all_totals, 0.0), axis=0)

    causal = lax.broadcasted_iota(jnp.int32, (block_rows, block_rows), 0) >= lax.broadcasted_iota(
        jnp.int32, (block_rows, block_rows), 1
    )
    head_size = lax.axis_size("head")
    core = ctx_index % 2
    partner = [(i, i ^ 1) for i in range(ctx_size)]
    half_rows = inner_dev // 2

    def gather_rows(w):
        local = lax.dynamic_slice_in_dim(w, core * half_rows, half_rows, 0)
        mine = lax.all_gather(local, "head", axis=0)
        other = lax.ppermute(mine, "ctx", partner)
        return mine, other

    def project_out(parts, mine, other):
        total = 0.0
        for g in range(head_size):
            a_mine = lax.dynamic_slice_in_dim(parts[g], core * half_rows, half_rows, 1)
            a_other = lax.dynamic_slice_in_dim(parts[g], (1 - core) * half_rows, half_rows, 1)
            term = jnp.dot(a_mine, mine[g], preferred_element_type=f32) + jnp.dot(
                a_other, other[g], preferred_element_type=f32
            )
            total = total + term.astype(bf16).astype(f32)
        return total

    w1_mine, w1_other = gather_rows(w_out1)
    attn_parts = []
    for n in range(block_count):
        q_n, k_n, v_n = q_blocks[n], k_blocks[n], v_blocks[n]
        scores = jnp.einsum("the,she->hts", q_n, k_n, preferred_element_type=f32)
        scores = jnp.where(causal, scores, 0.0)
        score_high, score_low = split_two(scores)
        within = jnp.einsum("hts,she->the", score_high, v_n, preferred_element_type=f32)
        within = within + jnp.einsum("hts,she->the", score_low, v_n, preferred_element_type=f32)
        state_high, state_low = split_two(carried)
        carried_term = jnp.einsum("the,hef->thf", q_n, state_high, preferred_element_type=f32)
        carried_term = carried_term + jnp.einsum(
            "the,hef->thf", q_n, state_low, preferred_element_type=f32
        )
        carried = carried + block_states[n]
        combined = within + carried_term
        attn_parts.append(
            rms_rows(combined, lin_gain.reshape(heads_dev, head_dim))
            .astype(bf16)
            .reshape(block_rows, inner_dev)
        )
    attn_one = jnp.concatenate(attn_parts, axis=0)
    gathered_one = lax.all_gather(attn_one, "head", axis=0)
    w2_local, gathered_one = lax.optimization_barrier((w_out2, gathered_one))
    w2_mine, w2_other = gather_rows(w2_local)
    residual = (tokens.astype(f32) + project_out(gathered_one, w1_mine, w1_other)).astype(bf16)

    normed_two = rms_rows(residual.astype(f32), norm_two).astype(bf16)
    projected_two = jnp.dot(
        normed_two, w_qkv2.reshape(feature_width, 3 * inner_dev), preferred_element_type=f32
    )
    projected_two = projected_two.reshape(tok_rows, 3, heads_dev, head_dim)
    query_hat = rms_rows(projected_two[:, 0], q_gain).astype(bf16)
    key_hat = rms_rows(projected_two[:, 1], k_gain).astype(bf16)
    value_two = projected_two[:, 2].astype(bf16)

    plane_tiles = GY * GZ
    halo_rows = plane_tiles * TILE
    tile_count = tok_rows // TILE
    up = [(i, i + 1) for i in range(ctx_size - 1)]
    down = [(i + 1, i) for i in range(ctx_size - 1)]
    key_hat = jnp.transpose(key_hat, (1, 0, 2))
    value_two = jnp.transpose(value_two, (1, 0, 2))
    query_hat = jnp.transpose(query_hat, (1, 0, 2))
    key_prev = lax.ppermute(key_hat[:, tok_rows - halo_rows :], "ctx", up)
    value_prev = lax.ppermute(value_two[:, tok_rows - halo_rows :], "ctx", up)
    key_next = lax.ppermute(key_hat[:, :halo_rows], "ctx", down)
    value_next = lax.ppermute(value_two[:, :halo_rows], "ctx", down)
    own_first = ctx_index * tile_count
    arange_halo = jnp.arange(plane_tiles, dtype=jnp.int32)
    pieces = (
        (key_prev, value_prev, own_first - plane_tiles + arange_halo),
        (key_hat, value_two, own_first + jnp.arange(tile_count, dtype=jnp.int32)),
        (key_next, value_next, own_first + tile_count + arange_halo),
    )
    present = neighbours >= 0
    tile_masks = [
        jnp.any((neighbours[:, :, None] == ids[None, None, :]) & present[:, :, None], axis=1)
        for _, _, ids in pieces
    ]
    key_ok = jnp.repeat(jnp.concatenate(tile_masks, axis=1), TILE, axis=1).astype(f32)
    attn_two = tile_attention(
        query_hat, [p[0] for p in pieces], [p[1] for p in pieces], key_ok[:, None, :], TILE
    )
    attn_two = attn_two.reshape(heads_dev, head_size, rows_mine, head_dim)
    attn_two = lax.all_to_all(attn_two, "head", 1, 1, tiled=True)
    attn_two = jnp.transpose(attn_two, (1, 2, 0, 3)).reshape(head_size, rows_mine, inner_dev)
    residual_mine = lax.dynamic_slice_in_dim(residual, head_index * rows_mine, rows_mine, 0)
    mixed = residual_mine.astype(f32) + project_out(attn_two, w2_mine, w2_other)
    return mixed.astype(bf16)


def solution(mesh):
    in_specs = (
        P(("groups", "ctx"), None),
        P(),
        P(None, None, "head"),
        P("head"),
        P("head", None),
        P(),
        P(None, None, "head"),
        P(),
        P(),
        P("head", None),
        P("ctx", None),
    )
    out_specs = P(("groups", "ctx", "head"), None)
    return jax.shard_map(
        on_device, mesh=mesh, in_specs=in_specs, out_specs=out_specs, check_vma=False
    )
```

```python
import functools
import math

import jax
import jax.numpy as jnp
import numpy as np
from jax import lax
from jax.experimental import pallas as pl
from jax.sharding import PartitionSpec as P

TILE = 256
GY = 2
GZ = 2


EPS = 1e-06


def with_halo(shard, sides, width):
    for axis, dim in sides:
        size, length = (lax.axis_size(axis), shard.shape[dim])
        up = [(i, (i + 1) % size) for i in range(size - 1)]
        down = [(j, i) for i, j in up]
        last = lax.slice_in_dim(shard, length - width, length, axis=dim)
        first = lax.slice_in_dim(shard, 0, width, axis=dim)
        before = lax.ppermute(last, axis, up)
        after = lax.ppermute(first, axis, down)
        shard = jnp.concatenate([before, shard, after], axis=dim)
    return shard


def rms_rows(value, gain):
    mean_sq = jnp.mean(value * value, axis=-1, keepdims=True)
    return value * lax.rsqrt(mean_sq + EPS) * gain


def feature_map(value):
    return jnp.where(value > 0, value + 1.0, jnp.exp(jnp.minimum(value, 0.0)))


def split_two(value):
    high_part = value.astype(jnp.bfloat16)
    low_part = (value - high_part.astype(jnp.float32)).astype(jnp.bfloat16)
    return (high_part, low_part)


def _attn_kernel(q_ref, kp_ref, ko_ref, kn_ref, vp_ref, vo_ref, vn_ref, m_ref, o_ref, *, scale):
    query = q_ref[...]
    mask = m_ref[0]
    exps = []
    total = None
    offset = 0
    for k_ref in (kp_ref, ko_ref, kn_ref):
        rows = k_ref.shape[0]
        scores = (
            lax.dot_general(
                query, k_ref[...], (((1,), (1,)), ((), ())), preferred_element_type=jnp.float32
            )
            * scale
        )
        unnormed = jnp.where(mask[:, offset : offset + rows] > 0.5, jnp.exp(scores), 0.0)
        exps.append(unnormed)
        part = jnp.sum(unnormed, axis=-1, keepdims=True)
        total = part if total is None else total + part
        offset += rows
    acc = None
    for unnormed, v_ref in zip(exps, (vp_ref, vo_ref, vn_ref)):
        weights = (unnormed / total).astype(jnp.bfloat16)
        term = jnp.dot(weights, v_ref[...], preferred_element_type=jnp.float32)
        acc = term if acc is None else acc + term
    o_ref[...] = acc.astype(o_ref.dtype)


def tile_attention(query, keys, values, mask, block_rows, interpret=False):
    heads, rows, head_dim = query.shape
    blocks = rows // block_rows
    key_width = mask.shape[-1]
    kv_specs = [pl.BlockSpec((None, k.shape[1], head_dim), lambda h, b: (h, 0, 0)) for k in keys]
    return pl.pallas_call(
        functools.partial(_attn_kernel, scale=1.0 / math.sqrt(head_dim)),
        out_shape=jax.ShapeDtypeStruct((heads, rows, head_dim), jnp.bfloat16),
        grid=(heads, blocks),
        in_specs=[pl.BlockSpec((None, block_rows, head_dim), lambda h, b: (h, b, 0))]
        + kv_specs
        + kv_specs
        + [pl.BlockSpec((1, 1, key_width), lambda h, b: (b, 0, 0))],
        out_specs=pl.BlockSpec((None, block_rows, head_dim), lambda h, b: (h, b, 0)),
        interpret=interpret,
    )(query, *keys, *values, mask)

def on_device(
    tokens, norm_one, w_qkv1, lin_gain, w_out1, norm_two, w_qkv2, q_gain, k_gain, w_out2, neighbours
):
    f32, bf16 = jnp.float32, jnp.bfloat16
    tok_rows, feature_width = tokens.shape
    inner_dev = w_qkv1.shape[2]
    head_dim = q_gain.shape[0]
    heads_dev = inner_dev // head_dim
    block_rows = 2 * TILE
    block_count = tok_rows // block_rows
    rows_mine = tok_rows // lax.axis_size("head")
    head_index = lax.axis_index("head")
    ctx_index = lax.axis_index("ctx")
    ctx_size = lax.axis_size("ctx")

    normed = rms_rows(tokens.astype(f32), norm_one).astype(bf16)
    projected = jnp.dot(
        normed, w_qkv1.reshape(feature_width, 3 * inner_dev), preferred_element_type=f32
    )
    projected = projected.reshape(tok_rows, 3, heads_dev, head_dim)
    query_map = feature_map(projected[:, 0]).astype(bf16)
    key_map = feature_map(projected[:, 1]).astype(bf16)
    value_one = projected[:, 2].astype(bf16)
    q_blocks = query_map.reshape(block_count, block_rows, heads_dev, head_dim)
    k_blocks = key_map.reshape(block_count, block_rows, heads_dev, head_dim)
    v_blocks = value_one.reshape(block_count, block_rows, heads_dev, head_dim)
    block_states = jnp.einsum(
        "nthe,nthf->nhef", k_blocks, v_blocks, preferred_element_type=f32
    )
    own_total = jnp.sum(block_states, axis=0)
    all_totals = lax.all_gather(own_total.astype(bf16), "ctx", axis=0).astype(f32)
    earlier_dev = jnp.arange(ctx_size, dtype=jnp.int32) < ctx_index
    carried = jnp.sum(jnp.where(earlier_dev[:, None, None, None], all_totals, 0.0), axis=0)

    causal = lax.broadcasted_iota(jnp.int32, (block_rows, block_rows), 0) >= lax.broadcasted_iota(
        jnp.int32, (block_rows, block_rows), 1
    )
    head_size = lax.axis_size("head")
    core = ctx_index % 2

    group_index = lax.axis_index("groups")
    y_bit = (ctx_index // 2) % 2
    slot = group_index * 4 + y_bit * 2 + core
    slice_rows = inner_dev // 8
    core_pairs = [(i, i ^ 1) for i in range(ctx_size)]
    y_pairs = [(i, i ^ 2) for i in range(ctx_size)]
    group_pairs = [(i, i ^ 1) for i in range(lax.axis_size("groups"))]

    def ordered(bit, own, other):
        return jnp.where(bit == 0, jnp.stack([own, other]), jnp.stack([other, own]))

    def gather_weight(w):
        local = lax.dynamic_slice_in_dim(w, slot * slice_rows, slice_rows, 0)
        mine = lax.all_gather(local, "head", axis=0)
        by_y = ordered(y_bit, mine, lax.ppermute(mine, "ctx", y_pairs))
        by_group = ordered(group_index, by_y, lax.ppermute(by_y, "groups", group_pairs))
        by_core = ordered(core, by_group, lax.ppermute(by_group, "ctx", core_pairs))
        full = jnp.transpose(by_core, (1, 2, 0, 3, 4, 5)).reshape((8,) + mine.shape)
        return jnp.transpose(full, (1, 0, 2, 3)).reshape(head_size, inner_dev, w.shape[1])

    def project_out(parts, full):
        total = 0.0
        for g in range(head_size):
            term = jnp.dot(parts[g], full[g], preferred_element_type=f32)
            total = total + term.astype(bf16).astype(f32)
        return total

    w1_full = gather_weight(w_out1)
    w2_full = gather_weight(w_out2)
    attn_parts = []
    for n in range(block_count):
        q_n, k_n, v_n = q_blocks[n], k_blocks[n], v_blocks[n]
        scores = jnp.einsum("the,she->hts", q_n, k_n, preferred_element_type=f32)
        scores = jnp.where(causal, scores, 0.0)
        score_high, score_low = split_two(scores)
        within = jnp.einsum("hts,she->the", score_high, v_n, preferred_element_type=f32)
        within = within + jnp.einsum("hts,she->the", score_low, v_n, preferred_element_type=f32)
        state_high, state_low = split_two(carried)
        carried_term = jnp.einsum("the,hef->thf", q_n, state_high, preferred_element_type=f32)
        carried_term = carried_term + jnp.einsum(
            "the,hef->thf", q_n, state_low, preferred_element_type=f32
        )
        carried = carried + block_states[n]
        combined = within + carried_term
        attn_parts.append(
            rms_rows(combined, lin_gain.reshape(heads_dev, head_dim))
            .astype(bf16)
            .reshape(block_rows, inner_dev)
        )
    attn_one = jnp.concatenate(attn_parts, axis=0)
    gathered_one = lax.all_gather(attn_one, "head", axis=0)
    residual = (tokens.astype(f32) + project_out(gathered_one, w1_full)).astype(bf16)

    normed_two = rms_rows(residual.astype(f32), norm_two).astype(bf16)
    projected_two = jnp.dot(
        normed_two, w_qkv2.reshape(feature_width, 3 * inner_dev), preferred_element_type=f32
    )
    projected_two = projected_two.reshape(tok_rows, 3, heads_dev, head_dim)
    query_hat = rms_rows(projected_two[:, 0], q_gain).astype(bf16)
    key_hat = rms_rows(projected_two[:, 1], k_gain).astype(bf16)
    value_two = projected_two[:, 2].astype(bf16)

    plane_tiles = GY * GZ
    halo_rows = plane_tiles * TILE
    tile_count = tok_rows // TILE
    up = [(i, i + 1) for i in range(ctx_size - 1)]
    down = [(i + 1, i) for i in range(ctx_size - 1)]
    key_hat = jnp.transpose(key_hat, (1, 0, 2))
    value_two = jnp.transpose(value_two, (1, 0, 2))
    query_hat = jnp.transpose(query_hat, (1, 0, 2))
    key_prev = lax.ppermute(key_hat[:, tok_rows - halo_rows :], "ctx", up)
    value_prev = lax.ppermute(value_two[:, tok_rows - halo_rows :], "ctx", up)
    key_next = lax.ppermute(key_hat[:, :halo_rows], "ctx", down)
    value_next = lax.ppermute(value_two[:, :halo_rows], "ctx", down)
    own_first = ctx_index * tile_count
    arange_halo = jnp.arange(plane_tiles, dtype=jnp.int32)
    pieces = (
        (key_prev, value_prev, own_first - plane_tiles + arange_halo),
        (key_hat, value_two, own_first + jnp.arange(tile_count, dtype=jnp.int32)),
        (key_next, value_next, own_first + tile_count + arange_halo),
    )
    present = neighbours >= 0
    tile_masks = [
        jnp.any((neighbours[:, :, None] == ids[None, None, :]) & present[:, :, None], axis=1)
        for _, _, ids in pieces
    ]
    key_ok = jnp.repeat(jnp.concatenate(tile_masks, axis=1), TILE, axis=1).astype(f32)
    attn_two = tile_attention(
        query_hat, [p[0] for p in pieces], [p[1] for p in pieces], key_ok[:, None, :], TILE
    )
    attn_two = attn_two.reshape(heads_dev, head_size, rows_mine, head_dim)
    attn_two = lax.all_to_all(attn_two, "head", 1, 1, tiled=True)
    attn_two = jnp.transpose(attn_two, (1, 2, 0, 3)).reshape(head_size, rows_mine, inner_dev)
    residual_mine = lax.dynamic_slice_in_dim(residual, head_index * rows_mine, rows_mine, 0)
    mixed = residual_mine.astype(f32) + project_out(attn_two, w2_full)
    return mixed.astype(bf16)


def solution(mesh):
    in_specs = (
        P(("groups", "ctx"), None),
        P(),
        P(None, None, "head"),
        P("head"),
        P("head", None),
        P(),
        P(None, None, "head"),
        P(),
        P(),
        P("head", None),
        P("ctx", None),
    )
    out_specs = P(("groups", "ctx", "head"), None)
    return jax.shard_map(
        on_device, mesh=mesh, in_specs=in_specs, out_specs=out_specs, check_vma=False
    )
```

```python
import functools
import math

import jax
import jax.numpy as jnp
import numpy as np
from jax import lax
from jax.experimental import pallas as pl
from jax.sharding import PartitionSpec as P

TILE = 256
GY = 2
GZ = 2


EPS = 1e-06


def with_halo(shard, sides, width):
    for axis, dim in sides:
        size, length = (lax.axis_size(axis), shard.shape[dim])
        up = [(i, (i + 1) % size) for i in range(size - 1)]
        down = [(j, i) for i, j in up]
        last = lax.slice_in_dim(shard, length - width, length, axis=dim)
        first = lax.slice_in_dim(shard, 0, width, axis=dim)
        before = lax.ppermute(last, axis, up)
        after = lax.ppermute(first, axis, down)
        shard = jnp.concatenate([before, shard, after], axis=dim)
    return shard


def rms_rows(value, gain):
    mean_sq = jnp.mean(value * value, axis=-1, keepdims=True)
    return value * lax.rsqrt(mean_sq + EPS) * gain


def feature_map(value):
    return jnp.where(value > 0, value + 1.0, jnp.exp(jnp.minimum(value, 0.0)))


def split_two(value):
    high_part = value.astype(jnp.bfloat16)
    low_part = (value - high_part.astype(jnp.float32)).astype(jnp.bfloat16)
    return (high_part, low_part)


def _attn_kernel(q_ref, kp_ref, ko_ref, kn_ref, vp_ref, vo_ref, vn_ref, m_ref, o_ref, *, scale):
    query = q_ref[...]
    mask = m_ref[0]
    exps = []
    total = None
    offset = 0
    for k_ref in (kp_ref, ko_ref, kn_ref):
        rows = k_ref.shape[0]
        scores = (
            lax.dot_general(
                query, k_ref[...], (((1,), (1,)), ((), ())), preferred_element_type=jnp.float32
            )
            * scale
        )
        unnormed = jnp.where(mask[:, offset : offset + rows] > 0.5, jnp.exp(scores), 0.0)
        exps.append(unnormed)
        part = jnp.sum(unnormed, axis=-1, keepdims=True)
        total = part if total is None else total + part
        offset += rows
    acc = None
    for unnormed, v_ref in zip(exps, (vp_ref, vo_ref, vn_ref)):
        weights = (unnormed / total).astype(jnp.bfloat16)
        term = jnp.dot(weights, v_ref[...], preferred_element_type=jnp.float32)
        acc = term if acc is None else acc + term
    o_ref[...] = acc.astype(o_ref.dtype)


def tile_attention(query, keys, values, mask, block_rows, interpret=False):
    heads, rows, head_dim = query.shape
    blocks = rows // block_rows
    key_width = mask.shape[-1]
    kv_specs = [pl.BlockSpec((None, k.shape[1], head_dim), lambda h, b: (h, 0, 0)) for k in keys]
    return pl.pallas_call(
        functools.partial(_attn_kernel, scale=1.0 / math.sqrt(head_dim)),
        out_shape=jax.ShapeDtypeStruct((heads, rows, head_dim), jnp.bfloat16),
        grid=(heads, blocks),
        in_specs=[pl.BlockSpec((None, block_rows, head_dim), lambda h, b: (h, b, 0))]
        + kv_specs
        + kv_specs
        + [pl.BlockSpec((1, 1, key_width), lambda h, b: (b, 0, 0))],
        out_specs=pl.BlockSpec((None, block_rows, head_dim), lambda h, b: (h, b, 0)),
        interpret=interpret,
    )(query, *keys, *values, mask)

def on_device(
    tokens, norm_one, w_qkv1, lin_gain, w_out1, norm_two, w_qkv2, q_gain, k_gain, w_out2, neighbours
):
    f32, bf16 = jnp.float32, jnp.bfloat16
    tok_rows, feature_width = tokens.shape
    inner_dev = w_qkv1.shape[2]
    head_dim = q_gain.shape[0]
    heads_dev = inner_dev // head_dim
    block_rows = 2 * TILE
    block_count = tok_rows // block_rows
    rows_mine = tok_rows // lax.axis_size("head")
    head_index = lax.axis_index("head")
    ctx_index = lax.axis_index("ctx")
    ctx_size = lax.axis_size("ctx")

    normed = rms_rows(tokens.astype(f32), norm_one).astype(bf16)
    projected = jnp.dot(
        normed, w_qkv1.reshape(feature_width, 3 * inner_dev), preferred_element_type=f32
    )
    projected = projected.reshape(tok_rows, 3, heads_dev, head_dim)
    query_map = feature_map(projected[:, 0]).astype(bf16)
    key_map = feature_map(projected[:, 1]).astype(bf16)
    value_one = projected[:, 2].astype(bf16)
    q_blocks = query_map.reshape(block_count, block_rows, heads_dev, head_dim)
    k_blocks = key_map.reshape(block_count, block_rows, heads_dev, head_dim)
    v_blocks = value_one.reshape(block_count, block_rows, heads_dev, head_dim)
    block_states = jnp.einsum(
        "nthe,nthf->nhef", k_blocks, v_blocks, preferred_element_type=f32
    )
    own_total = jnp.sum(block_states, axis=0)
    all_totals = lax.all_gather(own_total.astype(bf16), "ctx", axis=0).astype(f32)
    earlier_dev = jnp.arange(ctx_size, dtype=jnp.int32) < ctx_index
    carried = jnp.sum(jnp.where(earlier_dev[:, None, None, None], all_totals, 0.0), axis=0)

    causal = lax.broadcasted_iota(jnp.int32, (block_rows, block_rows), 0) >= lax.broadcasted_iota(
        jnp.int32, (block_rows, block_rows), 1
    )
    head_size = lax.axis_size("head")
    core = ctx_index % 2

    group_index = lax.axis_index("groups")
    y_bit = (ctx_index // 2) % 2
    slot = group_index * 4 + y_bit * 2 + core
    slice_rows = inner_dev // 8
    core_pairs = [(i, i ^ 1) for i in range(ctx_size)]
    y_pairs = [(i, i ^ 2) for i in range(ctx_size)]
    group_pairs = [(i, i ^ 1) for i in range(lax.axis_size("groups"))]

    def gather_weight(w):
        local = lax.dynamic_slice_in_dim(w, slot * slice_rows, slice_rows, 0)
        first = lax.all_gather(local, "head", axis=0)
        by_y = lax.ppermute(first, "ctx", y_pairs)
        by_group = lax.ppermute(first, "groups", group_pairs)
        by_both = lax.ppermute(by_group, "ctx", y_pairs)
        pieces = [first, by_y, by_group, by_both]
        pieces = pieces + [lax.ppermute(p, "ctx", core_pairs) for p in pieces]
        offsets = [0, 2, 4, 6, 1, 3, 5, 7]
        full = jnp.zeros((head_size, 8) + local.shape, local.dtype)
        for offset, piece in zip(offsets, pieces):
            full = lax.dynamic_update_slice_in_dim(
                full, piece[:, None], jnp.bitwise_xor(slot, offset), 1
            )
        return full.reshape(head_size, inner_dev, w.shape[1])

    def project_out(parts, full):
        total = 0.0
        for g in range(head_size):
            term = jnp.dot(parts[g], full[g], preferred_element_type=f32)
            total = total + term.astype(bf16).astype(f32)
        return total

    w1_full = gather_weight(w_out1)
    w2_full = gather_weight(w_out2)
    attn_parts = []
    for n in range(block_count):
        q_n, k_n, v_n = q_blocks[n], k_blocks[n], v_blocks[n]
        scores = jnp.einsum("the,she->hts", q_n, k_n, preferred_element_type=f32)
        scores = jnp.where(causal, scores, 0.0)
        score_high, score_low = split_two(scores)
        within = jnp.einsum("hts,she->the", score_high, v_n, preferred_element_type=f32)
        within = within + jnp.einsum("hts,she->the", score_low, v_n, preferred_element_type=f32)
        state_high, state_low = split_two(carried)
        carried_term = jnp.einsum("the,hef->thf", q_n, state_high, preferred_element_type=f32)
        carried_term = carried_term + jnp.einsum(
            "the,hef->thf", q_n, state_low, preferred_element_type=f32
        )
        carried = carried + block_states[n]
        combined = within + carried_term
        attn_parts.append(
            rms_rows(combined, lin_gain.reshape(heads_dev, head_dim))
            .astype(bf16)
            .reshape(block_rows, inner_dev)
        )
    attn_one = jnp.concatenate(attn_parts, axis=0)
    gathered_one = lax.all_gather(attn_one, "head", axis=0)
    residual = (tokens.astype(f32) + project_out(gathered_one, w1_full)).astype(bf16)

    normed_two = rms_rows(residual.astype(f32), norm_two).astype(bf16)
    projected_two = jnp.dot(
        normed_two, w_qkv2.reshape(feature_width, 3 * inner_dev), preferred_element_type=f32
    )
    projected_two = projected_two.reshape(tok_rows, 3, heads_dev, head_dim)
    query_hat = rms_rows(projected_two[:, 0], q_gain).astype(bf16)
    key_hat = rms_rows(projected_two[:, 1], k_gain).astype(bf16)
    value_two = projected_two[:, 2].astype(bf16)

    plane_tiles = GY * GZ
    halo_rows = plane_tiles * TILE
    tile_count = tok_rows // TILE
    up = [(i, i + 1) for i in range(ctx_size - 1)]
    down = [(i + 1, i) for i in range(ctx_size - 1)]
    key_hat = jnp.transpose(key_hat, (1, 0, 2))
    value_two = jnp.transpose(value_two, (1, 0, 2))
    query_hat = jnp.transpose(query_hat, (1, 0, 2))
    key_prev = lax.ppermute(key_hat[:, tok_rows - halo_rows :], "ctx", up)
    value_prev = lax.ppermute(value_two[:, tok_rows - halo_rows :], "ctx", up)
    key_next = lax.ppermute(key_hat[:, :halo_rows], "ctx", down)
    value_next = lax.ppermute(value_two[:, :halo_rows], "ctx", down)
    own_first = ctx_index * tile_count
    arange_halo = jnp.arange(plane_tiles, dtype=jnp.int32)
    pieces = (
        (key_prev, value_prev, own_first - plane_tiles + arange_halo),
        (key_hat, value_two, own_first + jnp.arange(tile_count, dtype=jnp.int32)),
        (key_next, value_next, own_first + tile_count + arange_halo),
    )
    present = neighbours >= 0
    tile_masks = [
        jnp.any((neighbours[:, :, None] == ids[None, None, :]) & present[:, :, None], axis=1)
        for _, _, ids in pieces
    ]
    key_ok = jnp.repeat(jnp.concatenate(tile_masks, axis=1), TILE, axis=1).astype(f32)
    attn_two = tile_attention(
        query_hat, [p[0] for p in pieces], [p[1] for p in pieces], key_ok[:, None, :], TILE
    )
    attn_two = attn_two.reshape(heads_dev, head_size, rows_mine, head_dim)
    attn_two = lax.all_to_all(attn_two, "head", 1, 1, tiled=True)
    attn_two = jnp.transpose(attn_two, (1, 2, 0, 3)).reshape(head_size, rows_mine, inner_dev)
    residual_mine = lax.dynamic_slice_in_dim(residual, head_index * rows_mine, rows_mine, 0)
    mixed = residual_mine.astype(f32) + project_out(attn_two, w2_full)
    return mixed.astype(bf16)


def solution(mesh):
    in_specs = (
        P(("groups", "ctx"), None),
        P(),
        P(None, None, "head"),
        P("head"),
        P("head", None),
        P(),
        P(None, None, "head"),
        P(),
        P(),
        P("head", None),
        P("ctx", None),
    )
    out_specs = P(("groups", "ctx", "head"), None)
    return jax.shard_map(
        on_device, mesh=mesh, in_specs=in_specs, out_specs=out_specs, check_vma=False
    )
```

```python
import functools
import math

import jax
import jax.numpy as jnp
import numpy as np
from jax import lax
from jax.experimental import pallas as pl
from jax.sharding import PartitionSpec as P

TILE = 256
GY = 2
GZ = 2


EPS = 1e-06


def with_halo(shard, sides, width):
    for axis, dim in sides:
        size, length = (lax.axis_size(axis), shard.shape[dim])
        up = [(i, (i + 1) % size) for i in range(size - 1)]
        down = [(j, i) for i, j in up]
        last = lax.slice_in_dim(shard, length - width, length, axis=dim)
        first = lax.slice_in_dim(shard, 0, width, axis=dim)
        before = lax.ppermute(last, axis, up)
        after = lax.ppermute(first, axis, down)
        shard = jnp.concatenate([before, shard, after], axis=dim)
    return shard


def rms_rows(value, gain):
    mean_sq = jnp.mean(value * value, axis=-1, keepdims=True)
    return value * lax.rsqrt(mean_sq + EPS) * gain


def feature_map(value):
    return jnp.where(value > 0, value + 1.0, jnp.exp(jnp.minimum(value, 0.0)))


def split_two(value):
    high_part = value.astype(jnp.bfloat16)
    low_part = (value - high_part.astype(jnp.float32)).astype(jnp.bfloat16)
    return (high_part, low_part)


def _attn_kernel(q_ref, kp_ref, ko_ref, kn_ref, vp_ref, vo_ref, vn_ref, m_ref, o_ref, *, scale):
    query = q_ref[...]
    mask = m_ref[0]
    exps = []
    total = None
    offset = 0
    for k_ref in (kp_ref, ko_ref, kn_ref):
        rows = k_ref.shape[0]
        scores = (
            lax.dot_general(
                query, k_ref[...], (((1,), (1,)), ((), ())), preferred_element_type=jnp.float32
            )
            * scale
        )
        unnormed = jnp.where(mask[:, offset : offset + rows] > 0.5, jnp.exp(scores), 0.0)
        exps.append(unnormed)
        part = jnp.sum(unnormed, axis=-1, keepdims=True)
        total = part if total is None else total + part
        offset += rows
    acc = None
    for unnormed, v_ref in zip(exps, (vp_ref, vo_ref, vn_ref)):
        weights = (unnormed / total).astype(jnp.bfloat16)
        term = jnp.dot(weights, v_ref[...], preferred_element_type=jnp.float32)
        acc = term if acc is None else acc + term
    o_ref[...] = acc.astype(o_ref.dtype)


def tile_attention(query, keys, values, mask, block_rows, interpret=False):
    heads, rows, head_dim = query.shape
    blocks = rows // block_rows
    key_width = mask.shape[-1]
    kv_specs = [pl.BlockSpec((None, k.shape[1], head_dim), lambda h, b: (h, 0, 0)) for k in keys]
    return pl.pallas_call(
        functools.partial(_attn_kernel, scale=1.0 / math.sqrt(head_dim)),
        out_shape=jax.ShapeDtypeStruct((heads, rows, head_dim), jnp.bfloat16),
        grid=(heads, blocks),
        in_specs=[pl.BlockSpec((None, block_rows, head_dim), lambda h, b: (h, b, 0))]
        + kv_specs
        + kv_specs
        + [pl.BlockSpec((1, 1, key_width), lambda h, b: (b, 0, 0))],
        out_specs=pl.BlockSpec((None, block_rows, head_dim), lambda h, b: (h, b, 0)),
        interpret=interpret,
    )(query, *keys, *values, mask)

def on_device(
    tokens, norm_one, w_qkv1, lin_gain, w_out1, norm_two, w_qkv2, q_gain, k_gain, w_out2, neighbours
):
    f32, bf16 = jnp.float32, jnp.bfloat16
    tok_rows, feature_width = tokens.shape
    inner_dev = w_qkv1.shape[2]
    head_dim = q_gain.shape[0]
    heads_dev = inner_dev // head_dim
    block_rows = 2 * TILE
    block_count = tok_rows // block_rows
    rows_mine = tok_rows // lax.axis_size("head")
    head_index = lax.axis_index("head")
    ctx_index = lax.axis_index("ctx")
    ctx_size = lax.axis_size("ctx")

    head_size = lax.axis_size("head")
    core = ctx_index % 2

    group_index = lax.axis_index("groups")
    y_bit = (ctx_index // 2) % 2
    slot = group_index * 4 + y_bit * 2 + core
    slice_rows = inner_dev // 8
    core_pairs = [(i, i ^ 1) for i in range(ctx_size)]
    y_pairs = [(i, i ^ 2) for i in range(ctx_size)]
    group_pairs = [(i, i ^ 1) for i in range(lax.axis_size("groups"))]

    def fetch_slice(w):
        local = lax.dynamic_slice_in_dim(w, slot * slice_rows, slice_rows, 0)
        return lax.all_gather(local, "head", axis=0)

    def spread_slice(first):
        by_y = lax.ppermute(first, "ctx", y_pairs)
        by_group = lax.ppermute(first, "groups", group_pairs)
        by_both = lax.ppermute(by_group, "ctx", y_pairs)
        pieces = [first, by_y, by_group, by_both]
        pieces = pieces + [lax.ppermute(p, "ctx", core_pairs) for p in pieces]
        offsets = [0, 2, 4, 6, 1, 3, 5, 7]
        full = jnp.zeros((head_size, 8) + first.shape[1:], first.dtype)
        for offset, piece in zip(offsets, pieces):
            full = lax.dynamic_update_slice_in_dim(
                full, piece[:, None], jnp.bitwise_xor(slot, offset), 1
            )
        return full.reshape(head_size, inner_dev, first.shape[2])

    normed = rms_rows(tokens.astype(f32), norm_one).astype(bf16)
    projected = jnp.dot(
        normed, w_qkv1.reshape(feature_width, 3 * inner_dev), preferred_element_type=f32
    )
    projected = projected.reshape(tok_rows, 3, heads_dev, head_dim)
    query_map = feature_map(projected[:, 0]).astype(bf16)
    key_map = feature_map(projected[:, 1]).astype(bf16)
    value_one = projected[:, 2].astype(bf16)
    q_blocks = query_map.reshape(block_count, block_rows, heads_dev, head_dim)
    k_blocks = key_map.reshape(block_count, block_rows, heads_dev, head_dim)
    v_blocks = value_one.reshape(block_count, block_rows, heads_dev, head_dim)
    block_states = jnp.einsum(
        "nthe,nthf->nhef", k_blocks, v_blocks, preferred_element_type=f32
    )
    own_total = jnp.sum(block_states, axis=0)
    w1_first = fetch_slice(w_out1)
    w2_first = fetch_slice(w_out2)
    own_total, w1_first = lax.optimization_barrier((own_total, w1_first))
    all_totals = lax.all_gather(own_total.astype(bf16), "ctx", axis=0).astype(f32)
    earlier_dev = jnp.arange(ctx_size, dtype=jnp.int32) < ctx_index
    carried = jnp.sum(jnp.where(earlier_dev[:, None, None, None], all_totals, 0.0), axis=0)

    causal = lax.broadcasted_iota(jnp.int32, (block_rows, block_rows), 0) >= lax.broadcasted_iota(
        jnp.int32, (block_rows, block_rows), 1
    )
    def project_out(parts, full):
        total = 0.0
        for g in range(head_size):
            term = jnp.dot(parts[g], full[g], preferred_element_type=f32)
            total = total + term.astype(bf16).astype(f32)
        return total

    w1_full = spread_slice(w1_first)
    w2_first, w1_full = lax.optimization_barrier((w2_first, w1_full))
    w2_full = spread_slice(w2_first)
    attn_parts = []
    for n in range(block_count):
        q_n, k_n, v_n = q_blocks[n], k_blocks[n], v_blocks[n]
        scores = jnp.einsum("the,she->hts", q_n, k_n, preferred_element_type=f32)
        scores = jnp.where(causal, scores, 0.0)
        score_high, score_low = split_two(scores)
        within = jnp.einsum("hts,she->the", score_high, v_n, preferred_element_type=f32)
        within = within + jnp.einsum("hts,she->the", score_low, v_n, preferred_element_type=f32)
        state_high, state_low = split_two(carried)
        carried_term = jnp.einsum("the,hef->thf", q_n, state_high, preferred_element_type=f32)
        carried_term = carried_term + jnp.einsum(
            "the,hef->thf", q_n, state_low, preferred_element_type=f32
        )
        carried = carried + block_states[n]
        combined = within + carried_term
        attn_parts.append(
            rms_rows(combined, lin_gain.reshape(heads_dev, head_dim))
            .astype(bf16)
            .reshape(block_rows, inner_dev)
        )
    attn_one = jnp.concatenate(attn_parts, axis=0)
    gathered_one = lax.all_gather(attn_one, "head", axis=0)
    residual = (tokens.astype(f32) + project_out(gathered_one, w1_full)).astype(bf16)

    normed_two = rms_rows(residual.astype(f32), norm_two).astype(bf16)
    projected_two = jnp.dot(
        normed_two, w_qkv2.reshape(feature_width, 3 * inner_dev), preferred_element_type=f32
    )
    projected_two = projected_two.reshape(tok_rows, 3, heads_dev, head_dim)
    query_hat = rms_rows(projected_two[:, 0], q_gain).astype(bf16)
    key_hat = rms_rows(projected_two[:, 1], k_gain).astype(bf16)
    value_two = projected_two[:, 2].astype(bf16)

    plane_tiles = GY * GZ
    halo_rows = plane_tiles * TILE
    tile_count = tok_rows // TILE
    up = [(i, i + 1) for i in range(ctx_size - 1)]
    down = [(i + 1, i) for i in range(ctx_size - 1)]
    key_hat = jnp.transpose(key_hat, (1, 0, 2))
    value_two = jnp.transpose(value_two, (1, 0, 2))
    query_hat = jnp.transpose(query_hat, (1, 0, 2))
    key_prev = lax.ppermute(key_hat[:, tok_rows - halo_rows :], "ctx", up)
    value_prev = lax.ppermute(value_two[:, tok_rows - halo_rows :], "ctx", up)
    key_next = lax.ppermute(key_hat[:, :halo_rows], "ctx", down)
    value_next = lax.ppermute(value_two[:, :halo_rows], "ctx", down)
    own_first = ctx_index * tile_count
    arange_halo = jnp.arange(plane_tiles, dtype=jnp.int32)
    pieces = (
        (key_prev, value_prev, own_first - plane_tiles + arange_halo),
        (key_hat, value_two, own_first + jnp.arange(tile_count, dtype=jnp.int32)),
        (key_next, value_next, own_first + tile_count + arange_halo),
    )
    present = neighbours >= 0
    tile_masks = [
        jnp.any((neighbours[:, :, None] == ids[None, None, :]) & present[:, :, None], axis=1)
        for _, _, ids in pieces
    ]
    key_ok = jnp.repeat(jnp.concatenate(tile_masks, axis=1), TILE, axis=1).astype(f32)
    attn_two = tile_attention(
        query_hat, [p[0] for p in pieces], [p[1] for p in pieces], key_ok[:, None, :], TILE
    )
    attn_two = attn_two.reshape(heads_dev, head_size, rows_mine, head_dim)
    attn_two = lax.all_to_all(attn_two, "head", 1, 1, tiled=True)
    attn_two = jnp.transpose(attn_two, (1, 2, 0, 3)).reshape(head_size, rows_mine, inner_dev)
    residual_mine = lax.dynamic_slice_in_dim(residual, head_index * rows_mine, rows_mine, 0)
    mixed = residual_mine.astype(f32) + project_out(attn_two, w2_full)
    return mixed.astype(bf16)


def solution(mesh):
    in_specs = (
        P(("groups", "ctx"), None),
        P(),
        P(None, None, "head"),
        P("head"),
        P("head", None),
        P(),
        P(None, None, "head"),
        P(),
        P(),
        P("head", None),
        P("ctx", None),
    )
    out_specs = P(("groups", "ctx", "head"), None)
    return jax.shard_map(
        on_device, mesh=mesh, in_specs=in_specs, out_specs=out_specs, check_vma=False
    )
```

```python
import functools
import math

import jax
import jax.numpy as jnp
import numpy as np
from jax import lax
from jax.experimental import pallas as pl
from jax.sharding import PartitionSpec as P

TILE = 256
GY = 2
GZ = 2


EPS = 1e-06


def with_halo(shard, sides, width):
    for axis, dim in sides:
        size, length = (lax.axis_size(axis), shard.shape[dim])
        up = [(i, (i + 1) % size) for i in range(size - 1)]
        down = [(j, i) for i, j in up]
        last = lax.slice_in_dim(shard, length - width, length, axis=dim)
        first = lax.slice_in_dim(shard, 0, width, axis=dim)
        before = lax.ppermute(last, axis, up)
        after = lax.ppermute(first, axis, down)
        shard = jnp.concatenate([before, shard, after], axis=dim)
    return shard


def rms_rows(value, gain):
    mean_sq = jnp.mean(value * value, axis=-1, keepdims=True)
    return value * lax.rsqrt(mean_sq + EPS) * gain


def feature_map(value):
    return jnp.where(value > 0, value + 1.0, jnp.exp(jnp.minimum(value, 0.0)))


def split_two(value):
    high_part = value.astype(jnp.bfloat16)
    low_part = (value - high_part.astype(jnp.float32)).astype(jnp.bfloat16)
    return (high_part, low_part)


def _attn_kernel(q_ref, kp_ref, ko_ref, kn_ref, vp_ref, vo_ref, vn_ref, m_ref, o_ref, *, scale):
    query = q_ref[...]
    mask = m_ref[0]
    exps = []
    total = None
    offset = 0
    for k_ref in (kp_ref, ko_ref, kn_ref):
        rows = k_ref.shape[0]
        scores = (
            lax.dot_general(
                query, k_ref[...], (((1,), (1,)), ((), ())), preferred_element_type=jnp.float32
            )
            * scale
        )
        unnormed = jnp.where(mask[:, offset : offset + rows] > 0.5, jnp.exp(scores), 0.0)
        exps.append(unnormed)
        part = jnp.sum(unnormed, axis=-1, keepdims=True)
        total = part if total is None else total + part
        offset += rows
    acc = None
    for unnormed, v_ref in zip(exps, (vp_ref, vo_ref, vn_ref)):
        weights = (unnormed / total).astype(jnp.bfloat16)
        term = jnp.dot(weights, v_ref[...], preferred_element_type=jnp.float32)
        acc = term if acc is None else acc + term
    o_ref[...] = acc.astype(o_ref.dtype)


def tile_attention(query, keys, values, mask, block_rows, interpret=False):
    heads, rows, head_dim = query.shape
    blocks = rows // block_rows
    key_width = mask.shape[-1]
    kv_specs = [pl.BlockSpec((None, k.shape[1], head_dim), lambda h, b: (h, 0, 0)) for k in keys]
    return pl.pallas_call(
        functools.partial(_attn_kernel, scale=1.0 / math.sqrt(head_dim)),
        out_shape=jax.ShapeDtypeStruct((heads, rows, head_dim), jnp.bfloat16),
        grid=(heads, blocks),
        in_specs=[pl.BlockSpec((None, block_rows, head_dim), lambda h, b: (h, b, 0))]
        + kv_specs
        + kv_specs
        + [pl.BlockSpec((1, 1, key_width), lambda h, b: (b, 0, 0))],
        out_specs=pl.BlockSpec((None, block_rows, head_dim), lambda h, b: (h, b, 0)),
        interpret=interpret,
    )(query, *keys, *values, mask)

def on_device(
    tokens, norm_one, w_qkv1, lin_gain, w_out1, norm_two, w_qkv2, q_gain, k_gain, w_out2, neighbours
):
    f32, bf16 = jnp.float32, jnp.bfloat16
    tok_rows, feature_width = tokens.shape
    inner_dev = w_qkv1.shape[2]
    head_dim = q_gain.shape[0]
    heads_dev = inner_dev // head_dim
    block_rows = 2 * TILE
    block_count = tok_rows // block_rows
    rows_mine = tok_rows // lax.axis_size("head")
    head_index = lax.axis_index("head")
    ctx_index = lax.axis_index("ctx")
    ctx_size = lax.axis_size("ctx")

    normed = rms_rows(tokens.astype(f32), norm_one).astype(bf16)
    projected = jnp.dot(
        normed, w_qkv1.reshape(feature_width, 3 * inner_dev), preferred_element_type=f32
    )
    projected = projected.reshape(tok_rows, 3, heads_dev, head_dim)
    query_map = feature_map(projected[:, 0]).astype(bf16)
    key_map = feature_map(projected[:, 1]).astype(bf16)
    value_one = projected[:, 2].astype(bf16)
    q_blocks = query_map.reshape(block_count, block_rows, heads_dev, head_dim)
    k_blocks = key_map.reshape(block_count, block_rows, heads_dev, head_dim)
    v_blocks = value_one.reshape(block_count, block_rows, heads_dev, head_dim)
    block_states = jnp.einsum(
        "nthe,nthf->nhef", k_blocks, v_blocks, preferred_element_type=f32
    )
    own_total = jnp.sum(block_states, axis=0)
    all_totals = lax.all_gather(own_total.astype(bf16), "ctx", axis=0).astype(f32)
    earlier_dev = jnp.arange(ctx_size, dtype=jnp.int32) < ctx_index
    carried = jnp.sum(jnp.where(earlier_dev[:, None, None, None], all_totals, 0.0), axis=0)

    causal = lax.broadcasted_iota(jnp.int32, (block_rows, block_rows), 0) >= lax.broadcasted_iota(
        jnp.int32, (block_rows, block_rows), 1
    )
    head_size = lax.axis_size("head")
    core = ctx_index % 2

    group_index = lax.axis_index("groups")
    y_bit = (ctx_index // 2) % 2
    slot = group_index * 4 + y_bit * 2 + core
    slice_rows = inner_dev // 8
    core_pairs = [(i, i ^ 1) for i in range(ctx_size)]
    y_pairs = [(i, i ^ 2) for i in range(ctx_size)]
    group_pairs = [(i, i ^ 1) for i in range(lax.axis_size("groups"))]
    group_count = lax.axis_size("groups")
    cross_pairs = [
        (g * ctx_size + i, (g ^ 1) * ctx_size + i)
        for g in range(group_count)
        for i in range(1, ctx_size, 2)
    ]

    def gather_weight(w):
        local = lax.dynamic_slice_in_dim(w, slot * slice_rows, slice_rows, 0)
        first = lax.all_gather(local, "head", axis=0)
        by_y = lax.ppermute(first, "ctx", y_pairs)
        by_group = lax.ppermute(first, "groups", group_pairs)
        relay_y = lax.ppermute(by_group, "ctx", [p for p in y_pairs if p[0] % 2 == 0])
        relay_group = lax.ppermute(by_y, ("groups", "ctx"), cross_pairs)
        by_both = jnp.where(core == 0, relay_y, relay_group)
        pieces = [first, by_y, by_group, by_both]
        pieces = pieces + [lax.ppermute(p, "ctx", core_pairs) for p in pieces]
        offsets = [0, 2, 4, 6, 1, 3, 5, 7]
        full = jnp.zeros((head_size, 8) + local.shape, local.dtype)
        for offset, piece in zip(offsets, pieces):
            full = lax.dynamic_update_slice_in_dim(
                full, piece[:, None], jnp.bitwise_xor(slot, offset), 1
            )
        return full.reshape(head_size, inner_dev, w.shape[1])

    def project_out(parts, full):
        total = 0.0
        for g in range(head_size):
            term = jnp.dot(parts[g], full[g], preferred_element_type=f32)
            total = total + term.astype(bf16).astype(f32)
        return total

    w1_full = gather_weight(w_out1)
    w2_full = gather_weight(w_out2)
    attn_parts = []
    for n in range(block_count):
        q_n, k_n, v_n = q_blocks[n], k_blocks[n], v_blocks[n]
        scores = jnp.einsum("the,she->hts", q_n, k_n, preferred_element_type=f32)
        scores = jnp.where(causal, scores, 0.0)
        score_high, score_low = split_two(scores)
        within = jnp.einsum("hts,she->the", score_high, v_n, preferred_element_type=f32)
        within = within + jnp.einsum("hts,she->the", score_low, v_n, preferred_element_type=f32)
        state_high, state_low = split_two(carried)
        carried_term = jnp.einsum("the,hef->thf", q_n, state_high, preferred_element_type=f32)
        carried_term = carried_term + jnp.einsum(
            "the,hef->thf", q_n, state_low, preferred_element_type=f32
        )
        carried = carried + block_states[n]
        combined = within + carried_term
        attn_parts.append(
            rms_rows(combined, lin_gain.reshape(heads_dev, head_dim))
            .astype(bf16)
            .reshape(block_rows, inner_dev)
        )
    attn_one = jnp.concatenate(attn_parts, axis=0)
    gathered_one = lax.all_gather(attn_one, "head", axis=0)
    residual = (tokens.astype(f32) + project_out(gathered_one, w1_full)).astype(bf16)

    normed_two = rms_rows(residual.astype(f32), norm_two).astype(bf16)
    projected_two = jnp.dot(
        normed_two, w_qkv2.reshape(feature_width, 3 * inner_dev), preferred_element_type=f32
    )
    projected_two = projected_two.reshape(tok_rows, 3, heads_dev, head_dim)
    query_hat = rms_rows(projected_two[:, 0], q_gain).astype(bf16)
    key_hat = rms_rows(projected_two[:, 1], k_gain).astype(bf16)
    value_two = projected_two[:, 2].astype(bf16)

    plane_tiles = GY * GZ
    halo_rows = plane_tiles * TILE
    tile_count = tok_rows // TILE
    up = [(i, i + 1) for i in range(ctx_size - 1)]
    down = [(i + 1, i) for i in range(ctx_size - 1)]
    key_hat = jnp.transpose(key_hat, (1, 0, 2))
    value_two = jnp.transpose(value_two, (1, 0, 2))
    query_hat = jnp.transpose(query_hat, (1, 0, 2))
    key_prev = lax.ppermute(key_hat[:, tok_rows - halo_rows :], "ctx", up)
    value_prev = lax.ppermute(value_two[:, tok_rows - halo_rows :], "ctx", up)
    key_next = lax.ppermute(key_hat[:, :halo_rows], "ctx", down)
    value_next = lax.ppermute(value_two[:, :halo_rows], "ctx", down)
    own_first = ctx_index * tile_count
    arange_halo = jnp.arange(plane_tiles, dtype=jnp.int32)
    pieces = (
        (key_prev, value_prev, own_first - plane_tiles + arange_halo),
        (key_hat, value_two, own_first + jnp.arange(tile_count, dtype=jnp.int32)),
        (key_next, value_next, own_first + tile_count + arange_halo),
    )
    present = neighbours >= 0
    tile_masks = [
        jnp.any((neighbours[:, :, None] == ids[None, None, :]) & present[:, :, None], axis=1)
        for _, _, ids in pieces
    ]
    key_ok = jnp.repeat(jnp.concatenate(tile_masks, axis=1), TILE, axis=1).astype(f32)
    attn_two = tile_attention(
        query_hat, [p[0] for p in pieces], [p[1] for p in pieces], key_ok[:, None, :], TILE
    )
    attn_two = attn_two.reshape(heads_dev, head_size, rows_mine, head_dim)
    attn_two = lax.all_to_all(attn_two, "head", 1, 1, tiled=True)
    attn_two = jnp.transpose(attn_two, (1, 2, 0, 3)).reshape(head_size, rows_mine, inner_dev)
    residual_mine = lax.dynamic_slice_in_dim(residual, head_index * rows_mine, rows_mine, 0)
    mixed = residual_mine.astype(f32) + project_out(attn_two, w2_full)
    return mixed.astype(bf16)


def solution(mesh):
    in_specs = (
        P(("groups", "ctx"), None),
        P(),
        P(None, None, "head"),
        P("head"),
        P("head", None),
        P(),
        P(None, None, "head"),
        P(),
        P(),
        P("head", None),
        P("ctx", None),
    )
    out_specs = P(("groups", "ctx", "head"), None)
    return jax.shard_map(
        on_device, mesh=mesh, in_specs=in_specs, out_specs=out_specs, check_vma=False
    )
```

```python
import functools
import math

import jax
import jax.numpy as jnp
import numpy as np
from jax import lax
from jax.experimental import pallas as pl
from jax.sharding import PartitionSpec as P

TILE = 256
GY = 2
GZ = 2


EPS = 1e-06


def with_halo(shard, sides, width):
    for axis, dim in sides:
        size, length = (lax.axis_size(axis), shard.shape[dim])
        up = [(i, (i + 1) % size) for i in range(size - 1)]
        down = [(j, i) for i, j in up]
        last = lax.slice_in_dim(shard, length - width, length, axis=dim)
        first = lax.slice_in_dim(shard, 0, width, axis=dim)
        before = lax.ppermute(last, axis, up)
        after = lax.ppermute(first, axis, down)
        shard = jnp.concatenate([before, shard, after], axis=dim)
    return shard


def rms_rows(value, gain):
    mean_sq = jnp.mean(value * value, axis=-1, keepdims=True)
    return value * lax.rsqrt(mean_sq + EPS) * gain


def feature_map(value):
    return jnp.where(value > 0, value + 1.0, jnp.exp(jnp.minimum(value, 0.0)))


def split_two(value):
    high_part = value.astype(jnp.bfloat16)
    low_part = (value - high_part.astype(jnp.float32)).astype(jnp.bfloat16)
    return (high_part, low_part)


def _attn_kernel(q_ref, kp_ref, ko_ref, kn_ref, vp_ref, vo_ref, vn_ref, m_ref, o_ref, *, scale):
    query = q_ref[...]
    mask = m_ref[0]
    exps = []
    total = None
    offset = 0
    for k_ref in (kp_ref, ko_ref, kn_ref):
        rows = k_ref.shape[0]
        scores = (
            lax.dot_general(
                query, k_ref[...], (((1,), (1,)), ((), ())), preferred_element_type=jnp.float32
            )
            * scale
        )
        unnormed = jnp.where(mask[:, offset : offset + rows] > 0.5, jnp.exp(scores), 0.0)
        exps.append(unnormed)
        part = jnp.sum(unnormed, axis=-1, keepdims=True)
        total = part if total is None else total + part
        offset += rows
    acc = None
    for unnormed, v_ref in zip(exps, (vp_ref, vo_ref, vn_ref)):
        weights = (unnormed / total).astype(jnp.bfloat16)
        term = jnp.dot(weights, v_ref[...], preferred_element_type=jnp.float32)
        acc = term if acc is None else acc + term
    o_ref[...] = acc.astype(o_ref.dtype)


def tile_attention(query, keys, values, mask, block_rows, interpret=False):
    heads, rows, head_dim = query.shape
    blocks = rows // block_rows
    key_width = mask.shape[-1]
    kv_specs = [pl.BlockSpec((None, k.shape[1], head_dim), lambda h, b: (h, 0, 0)) for k in keys]
    return pl.pallas_call(
        functools.partial(_attn_kernel, scale=1.0 / math.sqrt(head_dim)),
        out_shape=jax.ShapeDtypeStruct((heads, rows, head_dim), jnp.bfloat16),
        grid=(heads, blocks),
        in_specs=[pl.BlockSpec((None, block_rows, head_dim), lambda h, b: (h, b, 0))]
        + kv_specs
        + kv_specs
        + [pl.BlockSpec((1, 1, key_width), lambda h, b: (b, 0, 0))],
        out_specs=pl.BlockSpec((None, block_rows, head_dim), lambda h, b: (h, b, 0)),
        interpret=interpret,
    )(query, *keys, *values, mask)

def on_device(
    tokens, norm_one, w_qkv1, lin_gain, w_out1, norm_two, w_qkv2, q_gain, k_gain, w_out2, neighbours
):
    f32, bf16 = jnp.float32, jnp.bfloat16
    tok_rows, feature_width = tokens.shape
    inner_dev = w_qkv1.shape[2]
    head_dim = q_gain.shape[0]
    heads_dev = inner_dev // head_dim
    block_rows = 2 * TILE
    block_count = tok_rows // block_rows
    rows_mine = tok_rows // lax.axis_size("head")
    head_index = lax.axis_index("head")
    ctx_index = lax.axis_index("ctx")
    ctx_size = lax.axis_size("ctx")

    normed = rms_rows(tokens.astype(f32), norm_one).astype(bf16)
    projected = jnp.dot(
        normed, w_qkv1.reshape(feature_width, 3 * inner_dev), preferred_element_type=f32
    )
    projected = projected.reshape(tok_rows, 3, heads_dev, head_dim)
    query_map = feature_map(projected[:, 0]).astype(bf16)
    key_map = feature_map(projected[:, 1]).astype(bf16)
    value_one = projected[:, 2].astype(bf16)
    q_blocks = query_map.reshape(block_count, block_rows, heads_dev, head_dim)
    k_blocks = key_map.reshape(block_count, block_rows, heads_dev, head_dim)
    v_blocks = value_one.reshape(block_count, block_rows, heads_dev, head_dim)
    block_states = jnp.einsum(
        "nthe,nthf->nhef", k_blocks, v_blocks, preferred_element_type=f32
    )
    own_total = jnp.sum(block_states, axis=0)
    all_totals = lax.all_gather(own_total.astype(bf16), "ctx", axis=0).astype(f32)
    earlier_dev = jnp.arange(ctx_size, dtype=jnp.int32) < ctx_index
    carried = jnp.sum(jnp.where(earlier_dev[:, None, None, None], all_totals, 0.0), axis=0)

    causal = lax.broadcasted_iota(jnp.int32, (block_rows, block_rows), 0) >= lax.broadcasted_iota(
        jnp.int32, (block_rows, block_rows), 1
    )
    head_size = lax.axis_size("head")
    core = ctx_index % 2

    group_index = lax.axis_index("groups")
    y_bit = (ctx_index // 2) % 2
    slot = group_index * 4 + y_bit * 2 + core
    slice_rows = inner_dev // 8
    core_pairs = [(i, i ^ 1) for i in range(ctx_size)]
    y_pairs = [(i, i ^ 2) for i in range(ctx_size)]
    group_pairs = [(i, i ^ 1) for i in range(lax.axis_size("groups"))]
    group_count = lax.axis_size("groups")
    cross_pairs = [
        (g * ctx_size + i, (g ^ 1) * ctx_size + i)
        for g in range(group_count)
        for i in range(1, ctx_size, 2)
    ]

    def fetch_slice(w):
        local = lax.dynamic_slice_in_dim(w, slot * slice_rows, slice_rows, 0)
        return lax.all_gather(local, "head", axis=0)

    def spread_slice(first):
        by_y = lax.ppermute(first, "ctx", y_pairs)
        by_group = lax.ppermute(first, "groups", group_pairs)
        relay_y = lax.ppermute(by_group, "ctx", [p for p in y_pairs if p[0] % 2 == 0])
        relay_group = lax.ppermute(by_y, ("groups", "ctx"), cross_pairs)
        by_both = jnp.where(core == 0, relay_y, relay_group)
        pieces = [first, by_y, by_group, by_both]
        pieces = pieces + [lax.ppermute(p, "ctx", core_pairs) for p in pieces]
        offsets = [0, 2, 4, 6, 1, 3, 5, 7]
        full = jnp.zeros((head_size, 8) + first.shape[1:], first.dtype)
        for offset, piece in zip(offsets, pieces):
            full = lax.dynamic_update_slice_in_dim(
                full, piece[:, None], jnp.bitwise_xor(slot, offset), 1
            )
        return full.reshape(head_size, inner_dev, first.shape[2])

    def project_out(parts, full):
        total = 0.0
        for g in range(head_size):
            term = jnp.dot(parts[g], full[g], preferred_element_type=f32)
            total = total + term.astype(bf16).astype(f32)
        return total

    w1_full = spread_slice(fetch_slice(w_out1))
    attn_parts = []
    for n in range(block_count):
        q_n, k_n, v_n = q_blocks[n], k_blocks[n], v_blocks[n]
        scores = jnp.einsum("the,she->hts", q_n, k_n, preferred_element_type=f32)
        scores = jnp.where(causal, scores, 0.0)
        score_high, score_low = split_two(scores)
        within = jnp.einsum("hts,she->the", score_high, v_n, preferred_element_type=f32)
        within = within + jnp.einsum("hts,she->the", score_low, v_n, preferred_element_type=f32)
        state_high, state_low = split_two(carried)
        carried_term = jnp.einsum("the,hef->thf", q_n, state_high, preferred_element_type=f32)
        carried_term = carried_term + jnp.einsum(
            "the,hef->thf", q_n, state_low, preferred_element_type=f32
        )
        carried = carried + block_states[n]
        combined = within + carried_term
        attn_parts.append(
            rms_rows(combined, lin_gain.reshape(heads_dev, head_dim))
            .astype(bf16)
            .reshape(block_rows, inner_dev)
        )
    attn_one = jnp.concatenate(attn_parts, axis=0)
    gathered_one = lax.all_gather(attn_one, "head", axis=0)
    w2_local, attn_one = lax.optimization_barrier((w_out2, attn_one))
    w2_first, gathered_one = lax.optimization_barrier((fetch_slice(w2_local), gathered_one))
    w2_full = spread_slice(w2_first)
    residual = (tokens.astype(f32) + project_out(gathered_one, w1_full)).astype(bf16)

    normed_two = rms_rows(residual.astype(f32), norm_two).astype(bf16)
    projected_two = jnp.dot(
        normed_two, w_qkv2.reshape(feature_width, 3 * inner_dev), preferred_element_type=f32
    )
    projected_two = projected_two.reshape(tok_rows, 3, heads_dev, head_dim)
    query_hat = rms_rows(projected_two[:, 0], q_gain).astype(bf16)
    key_hat = rms_rows(projected_two[:, 1], k_gain).astype(bf16)
    value_two = projected_two[:, 2].astype(bf16)

    plane_tiles = GY * GZ
    halo_rows = plane_tiles * TILE
    tile_count = tok_rows // TILE
    up = [(i, i + 1) for i in range(ctx_size - 1)]
    down = [(i + 1, i) for i in range(ctx_size - 1)]
    key_hat = jnp.transpose(key_hat, (1, 0, 2))
    value_two = jnp.transpose(value_two, (1, 0, 2))
    query_hat = jnp.transpose(query_hat, (1, 0, 2))
    key_prev = lax.ppermute(key_hat[:, tok_rows - halo_rows :], "ctx", up)
    value_prev = lax.ppermute(value_two[:, tok_rows - halo_rows :], "ctx", up)
    key_next = lax.ppermute(key_hat[:, :halo_rows], "ctx", down)
    value_next = lax.ppermute(value_two[:, :halo_rows], "ctx", down)
    own_first = ctx_index * tile_count
    arange_halo = jnp.arange(plane_tiles, dtype=jnp.int32)
    pieces = (
        (key_prev, value_prev, own_first - plane_tiles + arange_halo),
        (key_hat, value_two, own_first + jnp.arange(tile_count, dtype=jnp.int32)),
        (key_next, value_next, own_first + tile_count + arange_halo),
    )
    present = neighbours >= 0
    tile_masks = [
        jnp.any((neighbours[:, :, None] == ids[None, None, :]) & present[:, :, None], axis=1)
        for _, _, ids in pieces
    ]
    key_ok = jnp.repeat(jnp.concatenate(tile_masks, axis=1), TILE, axis=1).astype(f32)
    attn_two = tile_attention(
        query_hat, [p[0] for p in pieces], [p[1] for p in pieces], key_ok[:, None, :], TILE
    )
    attn_two = attn_two.reshape(heads_dev, head_size, rows_mine, head_dim)
    attn_two = lax.all_to_all(attn_two, "head", 1, 1, tiled=True)
    attn_two = jnp.transpose(attn_two, (1, 2, 0, 3)).reshape(head_size, rows_mine, inner_dev)
    residual_mine = lax.dynamic_slice_in_dim(residual, head_index * rows_mine, rows_mine, 0)
    mixed = residual_mine.astype(f32) + project_out(attn_two, w2_full)
    return mixed.astype(bf16)


def solution(mesh):
    in_specs = (
        P(("groups", "ctx"), None),
        P(),
        P(None, None, "head"),
        P("head"),
        P("head", None),
        P(),
        P(None, None, "head"),
        P(),
        P(),
        P("head", None),
        P("ctx", None),
    )
    out_specs = P(("groups", "ctx", "head"), None)
    return jax.shard_map(
        on_device, mesh=mesh, in_specs=in_specs, out_specs=out_specs, check_vma=False
    )
```

```python
import functools
import math

import jax
import jax.numpy as jnp
import numpy as np
from jax import lax
from jax.experimental import pallas as pl
from jax.sharding import PartitionSpec as P

TILE = 256
GY = 2
GZ = 2


EPS = 1e-06


def with_halo(shard, sides, width):
    for axis, dim in sides:
        size, length = (lax.axis_size(axis), shard.shape[dim])
        up = [(i, (i + 1) % size) for i in range(size - 1)]
        down = [(j, i) for i, j in up]
        last = lax.slice_in_dim(shard, length - width, length, axis=dim)
        first = lax.slice_in_dim(shard, 0, width, axis=dim)
        before = lax.ppermute(last, axis, up)
        after = lax.ppermute(first, axis, down)
        shard = jnp.concatenate([before, shard, after], axis=dim)
    return shard


def rms_rows(value, gain):
    mean_sq = jnp.mean(value * value, axis=-1, keepdims=True)
    return value * lax.rsqrt(mean_sq + EPS) * gain


def feature_map(value):
    return jnp.where(value > 0, value + 1.0, jnp.exp(jnp.minimum(value, 0.0)))


def split_two(value):
    high_part = value.astype(jnp.bfloat16)
    low_part = (value - high_part.astype(jnp.float32)).astype(jnp.bfloat16)
    return (high_part, low_part)


def _attn_kernel(q_ref, kp_ref, ko_ref, kn_ref, vp_ref, vo_ref, vn_ref, m_ref, o_ref, *, scale):
    query = q_ref[...]
    mask = m_ref[0]
    exps = []
    total = None
    offset = 0
    for k_ref in (kp_ref, ko_ref, kn_ref):
        rows = k_ref.shape[0]
        scores = (
            lax.dot_general(
                query, k_ref[...], (((1,), (1,)), ((), ())), preferred_element_type=jnp.float32
            )
            * scale
        )
        unnormed = jnp.where(mask[:, offset : offset + rows] > 0.5, jnp.exp(scores), 0.0)
        exps.append(unnormed)
        part = jnp.sum(unnormed, axis=-1, keepdims=True)
        total = part if total is None else total + part
        offset += rows
    acc = None
    for unnormed, v_ref in zip(exps, (vp_ref, vo_ref, vn_ref)):
        weights = (unnormed / total).astype(jnp.bfloat16)
        term = jnp.dot(weights, v_ref[...], preferred_element_type=jnp.float32)
        acc = term if acc is None else acc + term
    o_ref[...] = acc.astype(o_ref.dtype)


def tile_attention(query, keys, values, mask, block_rows, interpret=False):
    heads, rows, head_dim = query.shape
    blocks = rows // block_rows
    key_width = mask.shape[-1]
    kv_specs = [pl.BlockSpec((None, k.shape[1], head_dim), lambda h, b: (h, 0, 0)) for k in keys]
    return pl.pallas_call(
        functools.partial(_attn_kernel, scale=1.0 / math.sqrt(head_dim)),
        out_shape=jax.ShapeDtypeStruct((heads, rows, head_dim), jnp.bfloat16),
        grid=(heads, blocks),
        in_specs=[pl.BlockSpec((None, block_rows, head_dim), lambda h, b: (h, b, 0))]
        + kv_specs
        + kv_specs
        + [pl.BlockSpec((1, 1, key_width), lambda h, b: (b, 0, 0))],
        out_specs=pl.BlockSpec((None, block_rows, head_dim), lambda h, b: (h, b, 0)),
        interpret=interpret,
    )(query, *keys, *values, mask)

def on_device(
    tokens, norm_one, w_qkv1, lin_gain, w_out1, norm_two, w_qkv2, q_gain, k_gain, w_out2, neighbours
):
    f32, bf16 = jnp.float32, jnp.bfloat16
    tok_rows, feature_width = tokens.shape
    inner_dev = w_qkv1.shape[2]
    head_dim = q_gain.shape[0]
    heads_dev = inner_dev // head_dim
    block_rows = 2 * TILE
    block_count = tok_rows // block_rows
    rows_mine = tok_rows // lax.axis_size("head")
    head_index = lax.axis_index("head")
    ctx_index = lax.axis_index("ctx")
    ctx_size = lax.axis_size("ctx")

    normed = rms_rows(tokens.astype(f32), norm_one).astype(bf16)
    projected = jnp.dot(
        normed, w_qkv1.reshape(feature_width, 3 * inner_dev), preferred_element_type=f32
    )
    projected = projected.reshape(tok_rows, 3, heads_dev, head_dim)
    query_map = feature_map(projected[:, 0]).astype(bf16)
    key_map = feature_map(projected[:, 1]).astype(bf16)
    value_one = projected[:, 2].astype(bf16)
    q_blocks = query_map.reshape(block_count, block_rows, heads_dev, head_dim)
    k_blocks = key_map.reshape(block_count, block_rows, heads_dev, head_dim)
    v_blocks = value_one.reshape(block_count, block_rows, heads_dev, head_dim)
    block_states = jnp.einsum(
        "nthe,nthf->nhef", k_blocks, v_blocks, preferred_element_type=f32
    )
    own_total = jnp.sum(block_states, axis=0)
    all_totals = lax.all_gather(own_total.astype(bf16), "ctx", axis=0).astype(f32)
    earlier_dev = jnp.arange(ctx_size, dtype=jnp.int32) < ctx_index
    carried = jnp.sum(jnp.where(earlier_dev[:, None, None, None], all_totals, 0.0), axis=0)

    causal = lax.broadcasted_iota(jnp.int32, (block_rows, block_rows), 0) >= lax.broadcasted_iota(
        jnp.int32, (block_rows, block_rows), 1
    )
    head_size = lax.axis_size("head")
    core = ctx_index % 2

    group_index = lax.axis_index("groups")
    y_bit = (ctx_index // 2) % 2
    slot = group_index * 4 + y_bit * 2 + core
    slice_rows = inner_dev // 8
    core_pairs = [(i, i ^ 1) for i in range(ctx_size)]
    y_pairs = [(i, i ^ 2) for i in range(ctx_size)]
    group_pairs = [(i, i ^ 1) for i in range(lax.axis_size("groups"))]
    group_count = lax.axis_size("groups")
    cross_pairs = [
        (g * ctx_size + i, (g ^ 1) * ctx_size + i)
        for g in range(group_count)
        for i in range(1, ctx_size, 2)
    ]

    def fetch_slice(w):
        local = lax.dynamic_slice_in_dim(w, slot * slice_rows, slice_rows, 0)
        return lax.all_gather(local, "head", axis=0)

    def spread_slice(first):
        by_y = lax.ppermute(first, "ctx", y_pairs)
        by_group = lax.ppermute(first, "groups", group_pairs)
        relay_y = lax.ppermute(by_group, "ctx", [p for p in y_pairs if p[0] % 2 == 0])
        relay_group = lax.ppermute(by_y, ("groups", "ctx"), cross_pairs)
        by_both = jnp.where(core == 0, relay_y, relay_group)
        pieces = [first, by_y, by_group, by_both]
        pieces = pieces + [lax.ppermute(p, "ctx", core_pairs) for p in pieces]
        offsets = [0, 2, 4, 6, 1, 3, 5, 7]
        full = jnp.zeros((head_size, 8) + first.shape[1:], first.dtype)
        for offset, piece in zip(offsets, pieces):
            full = lax.dynamic_update_slice_in_dim(
                full, piece[:, None], jnp.bitwise_xor(slot, offset), 1
            )
        return full.reshape(head_size, inner_dev, first.shape[2])

    def project_out(parts, full):
        total = 0.0
        for g in range(head_size):
            term = jnp.dot(parts[g], full[g], preferred_element_type=f32)
            total = total + term.astype(bf16).astype(f32)
        return total

    w1_full = spread_slice(fetch_slice(w_out1))
    attn_parts = []
    for n in range(block_count):
        q_n, k_n, v_n = q_blocks[n], k_blocks[n], v_blocks[n]
        scores = jnp.einsum("the,she->hts", q_n, k_n, preferred_element_type=f32)
        scores = jnp.where(causal, scores, 0.0)
        score_high, score_low = split_two(scores)
        within = jnp.einsum("hts,she->the", score_high, v_n, preferred_element_type=f32)
        within = within + jnp.einsum("hts,she->the", score_low, v_n, preferred_element_type=f32)
        state_high, state_low = split_two(carried)
        carried_term = jnp.einsum("the,hef->thf", q_n, state_high, preferred_element_type=f32)
        carried_term = carried_term + jnp.einsum(
            "the,hef->thf", q_n, state_low, preferred_element_type=f32
        )
        carried = carried + block_states[n]
        combined = within + carried_term
        attn_parts.append(
            rms_rows(combined, lin_gain.reshape(heads_dev, head_dim))
            .astype(bf16)
            .reshape(block_rows, inner_dev)
        )
    attn_one = jnp.concatenate(attn_parts, axis=0)
    gathered_one = lax.all_gather(attn_one, "head", axis=0)
    w2_local, attn_one = lax.optimization_barrier((w_out2, attn_one))
    w2_first, _ = lax.optimization_barrier((fetch_slice(w2_local), gathered_one))
    w2_full = spread_slice(w2_first)
    residual = (tokens.astype(f32) + project_out(gathered_one, w1_full)).astype(bf16)

    normed_two = rms_rows(residual.astype(f32), norm_two).astype(bf16)
    projected_two = jnp.dot(
        normed_two, w_qkv2.reshape(feature_width, 3 * inner_dev), preferred_element_type=f32
    )
    projected_two = projected_two.reshape(tok_rows, 3, heads_dev, head_dim)
    query_hat = rms_rows(projected_two[:, 0], q_gain).astype(bf16)
    key_hat = rms_rows(projected_two[:, 1], k_gain).astype(bf16)
    value_two = projected_two[:, 2].astype(bf16)

    plane_tiles = GY * GZ
    halo_rows = plane_tiles * TILE
    tile_count = tok_rows // TILE
    up = [(i, i + 1) for i in range(ctx_size - 1)]
    down = [(i + 1, i) for i in range(ctx_size - 1)]
    key_hat = jnp.transpose(key_hat, (1, 0, 2))
    value_two = jnp.transpose(value_two, (1, 0, 2))
    query_hat = jnp.transpose(query_hat, (1, 0, 2))
    key_prev = lax.ppermute(key_hat[:, tok_rows - halo_rows :], "ctx", up)
    value_prev = lax.ppermute(value_two[:, tok_rows - halo_rows :], "ctx", up)
    key_next = lax.ppermute(key_hat[:, :halo_rows], "ctx", down)
    value_next = lax.ppermute(value_two[:, :halo_rows], "ctx", down)
    own_first = ctx_index * tile_count
    arange_halo = jnp.arange(plane_tiles, dtype=jnp.int32)
    pieces = (
        (key_prev, value_prev, own_first - plane_tiles + arange_halo),
        (key_hat, value_two, own_first + jnp.arange(tile_count, dtype=jnp.int32)),
        (key_next, value_next, own_first + tile_count + arange_halo),
    )
    present = neighbours >= 0
    tile_masks = [
        jnp.any((neighbours[:, :, None] == ids[None, None, :]) & present[:, :, None], axis=1)
        for _, _, ids in pieces
    ]
    key_ok = jnp.repeat(jnp.concatenate(tile_masks, axis=1), TILE, axis=1).astype(f32)
    attn_two = tile_attention(
        query_hat, [p[0] for p in pieces], [p[1] for p in pieces], key_ok[:, None, :], TILE
    )
    attn_two = attn_two.reshape(heads_dev, head_size, rows_mine, head_dim)
    attn_two = lax.all_to_all(attn_two, "head", 1, 1, tiled=True)
    attn_two = jnp.transpose(attn_two, (1, 2, 0, 3)).reshape(head_size, rows_mine, inner_dev)
    residual_mine = lax.dynamic_slice_in_dim(residual, head_index * rows_mine, rows_mine, 0)
    mixed = residual_mine.astype(f32) + project_out(attn_two, w2_full)
    return mixed.astype(bf16)


def solution(mesh):
    in_specs = (
        P(("groups", "ctx"), None),
        P(),
        P(None, None, "head"),
        P("head"),
        P("head", None),
        P(),
        P(None, None, "head"),
        P(),
        P(),
        P("head", None),
        P("ctx", None),
    )
    out_specs = P(("groups", "ctx", "head"), None)
    return jax.shard_map(
        on_device, mesh=mesh, in_specs=in_specs, out_specs=out_specs, check_vma=False
    )
```

```python
import functools
import math

import jax
import jax.numpy as jnp
import numpy as np
from jax import lax
from jax.experimental import pallas as pl
from jax.sharding import PartitionSpec as P

TILE = 256
GY = 2
GZ = 2


EPS = 1e-06


def with_halo(shard, sides, width):
    for axis, dim in sides:
        size, length = (lax.axis_size(axis), shard.shape[dim])
        up = [(i, (i + 1) % size) for i in range(size - 1)]
        down = [(j, i) for i, j in up]
        last = lax.slice_in_dim(shard, length - width, length, axis=dim)
        first = lax.slice_in_dim(shard, 0, width, axis=dim)
        before = lax.ppermute(last, axis, up)
        after = lax.ppermute(first, axis, down)
        shard = jnp.concatenate([before, shard, after], axis=dim)
    return shard


def rms_rows(value, gain):
    mean_sq = jnp.mean(value * value, axis=-1, keepdims=True)
    return value * lax.rsqrt(mean_sq + EPS) * gain


def feature_map(value):
    return jnp.where(value > 0, value + 1.0, jnp.exp(jnp.minimum(value, 0.0)))


def split_two(value):
    high_part = value.astype(jnp.bfloat16)
    low_part = (value - high_part.astype(jnp.float32)).astype(jnp.bfloat16)
    return (high_part, low_part)


def _attn_kernel(q_ref, kp_ref, ko_ref, kn_ref, vp_ref, vo_ref, vn_ref, m_ref, o_ref, *, scale):
    query = q_ref[...]
    mask = m_ref[0]
    exps = []
    total = None
    offset = 0
    for k_ref in (kp_ref, ko_ref, kn_ref):
        rows = k_ref.shape[0]
        scores = (
            lax.dot_general(
                query, k_ref[...], (((1,), (1,)), ((), ())), preferred_element_type=jnp.float32
            )
            * scale
        )
        unnormed = jnp.where(mask[:, offset : offset + rows] > 0.5, jnp.exp(scores), 0.0)
        exps.append(unnormed)
        part = jnp.sum(unnormed, axis=-1, keepdims=True)
        total = part if total is None else total + part
        offset += rows
    acc = None
    for unnormed, v_ref in zip(exps, (vp_ref, vo_ref, vn_ref)):
        weights = (unnormed / total).astype(jnp.bfloat16)
        term = jnp.dot(weights, v_ref[...], preferred_element_type=jnp.float32)
        acc = term if acc is None else acc + term
    o_ref[...] = acc.astype(o_ref.dtype)


def tile_attention(query, keys, values, mask, block_rows, interpret=False):
    heads, rows, head_dim = query.shape
    blocks = rows // block_rows
    key_width = mask.shape[-1]
    kv_specs = [pl.BlockSpec((None, k.shape[1], head_dim), lambda h, b: (h, 0, 0)) for k in keys]
    return pl.pallas_call(
        functools.partial(_attn_kernel, scale=1.0 / math.sqrt(head_dim)),
        out_shape=jax.ShapeDtypeStruct((heads, rows, head_dim), jnp.bfloat16),
        grid=(heads, blocks),
        in_specs=[pl.BlockSpec((None, block_rows, head_dim), lambda h, b: (h, b, 0))]
        + kv_specs
        + kv_specs
        + [pl.BlockSpec((1, 1, key_width), lambda h, b: (b, 0, 0))],
        out_specs=pl.BlockSpec((None, block_rows, head_dim), lambda h, b: (h, b, 0)),
        interpret=interpret,
    )(query, *keys, *values, mask)

def on_device(
    tokens, norm_one, w_qkv1, lin_gain, w_out1, norm_two, w_qkv2, q_gain, k_gain, w_out2, neighbours
):
    f32, bf16 = jnp.float32, jnp.bfloat16
    tok_rows, feature_width = tokens.shape
    inner_dev = w_qkv1.shape[2]
    head_dim = q_gain.shape[0]
    heads_dev = inner_dev // head_dim
    block_rows = 2 * TILE
    block_count = tok_rows // block_rows
    rows_mine = tok_rows // lax.axis_size("head")
    head_index = lax.axis_index("head")
    ctx_index = lax.axis_index("ctx")
    ctx_size = lax.axis_size("ctx")

    normed = rms_rows(tokens.astype(f32), norm_one).astype(bf16)
    projected = jnp.dot(
        normed, w_qkv1.reshape(feature_width, 3 * inner_dev), preferred_element_type=f32
    )
    projected = projected.reshape(tok_rows, 3, heads_dev, head_dim)
    query_map = feature_map(projected[:, 0]).astype(bf16)
    key_map = feature_map(projected[:, 1]).astype(bf16)
    value_one = projected[:, 2].astype(bf16)
    q_blocks = query_map.reshape(block_count, block_rows, heads_dev, head_dim)
    k_blocks = key_map.reshape(block_count, block_rows, heads_dev, head_dim)
    v_blocks = value_one.reshape(block_count, block_rows, heads_dev, head_dim)
    block_states = jnp.einsum(
        "nthe,nthf->nhef", k_blocks, v_blocks, preferred_element_type=f32
    )
    own_total = jnp.sum(block_states, axis=0)
    all_totals = lax.all_gather(own_total.astype(bf16), "ctx", axis=0).astype(f32)
    earlier_dev = jnp.arange(ctx_size, dtype=jnp.int32) < ctx_index
    carried = jnp.sum(jnp.where(earlier_dev[:, None, None, None], all_totals, 0.0), axis=0)

    causal = lax.broadcasted_iota(jnp.int32, (block_rows, block_rows), 0) >= lax.broadcasted_iota(
        jnp.int32, (block_rows, block_rows), 1
    )
    head_size = lax.axis_size("head")
    core = ctx_index % 2

    group_index = lax.axis_index("groups")
    y_bit = (ctx_index // 2) % 2
    slot = group_index * 4 + y_bit * 2 + core
    slice_rows = inner_dev // 8
    core_pairs = [(i, i ^ 1) for i in range(ctx_size)]
    y_pairs = [(i, i ^ 2) for i in range(ctx_size)]
    group_pairs = [(i, i ^ 1) for i in range(lax.axis_size("groups"))]
    group_count = lax.axis_size("groups")
    cross_pairs = [
        (g * ctx_size + i, (g ^ 1) * ctx_size + i)
        for g in range(group_count)
        for i in range(1, ctx_size, 2)
    ]

    def gather_weight(w, by_permute=False):
        local = lax.dynamic_slice_in_dim(w, slot * slice_rows, slice_rows, 0)
        if by_permute:
            first = jnp.zeros((head_size,) + local.shape, local.dtype)
            first = lax.dynamic_update_slice_in_dim(first, local[None], head_index, 0)
            for shift in range(1, head_size):
                pairs = [(i, (i + shift) % head_size) for i in range(head_size)]
                moved = lax.ppermute(local, "head", pairs)
                source = (head_index + head_size - shift) % head_size
                first = lax.dynamic_update_slice_in_dim(first, moved[None], source, 0)
        else:
            first = lax.all_gather(local, "head", axis=0)
        by_y = lax.ppermute(first, "ctx", y_pairs)
        by_group = lax.ppermute(first, "groups", group_pairs)
        relay_y = lax.ppermute(by_group, "ctx", [p for p in y_pairs if p[0] % 2 == 0])
        relay_group = lax.ppermute(by_y, ("groups", "ctx"), cross_pairs)
        by_both = jnp.where(core == 0, relay_y, relay_group)
        pieces = [first, by_y, by_group, by_both]
        pieces = pieces + [lax.ppermute(p, "ctx", core_pairs) for p in pieces]
        offsets = [0, 2, 4, 6, 1, 3, 5, 7]
        full = jnp.zeros((head_size, 8) + local.shape, local.dtype)
        for offset, piece in zip(offsets, pieces):
            full = lax.dynamic_update_slice_in_dim(
                full, piece[:, None], jnp.bitwise_xor(slot, offset), 1
            )
        return full.reshape(head_size, inner_dev, w.shape[1])

    def project_out(parts, full):
        total = 0.0
        for g in range(head_size):
            term = jnp.dot(parts[g], full[g], preferred_element_type=f32)
            total = total + term.astype(bf16).astype(f32)
        return total

    w1_full = gather_weight(w_out1)
    w2_full = gather_weight(w_out2, by_permute=True)
    attn_parts = []
    for n in range(block_count):
        q_n, k_n, v_n = q_blocks[n], k_blocks[n], v_blocks[n]
        scores = jnp.einsum("the,she->hts", q_n, k_n, preferred_element_type=f32)
        scores = jnp.where(causal, scores, 0.0)
        score_high, score_low = split_two(scores)
        within = jnp.einsum("hts,she->the", score_high, v_n, preferred_element_type=f32)
        within = within + jnp.einsum("hts,she->the", score_low, v_n, preferred_element_type=f32)
        state_high, state_low = split_two(carried)
        carried_term = jnp.einsum("the,hef->thf", q_n, state_high, preferred_element_type=f32)
        carried_term = carried_term + jnp.einsum(
            "the,hef->thf", q_n, state_low, preferred_element_type=f32
        )
        carried = carried + block_states[n]
        combined = within + carried_term
        attn_parts.append(
            rms_rows(combined, lin_gain.reshape(heads_dev, head_dim))
            .astype(bf16)
            .reshape(block_rows, inner_dev)
        )
    attn_one = jnp.concatenate(attn_parts, axis=0)
    gathered_one = lax.all_gather(attn_one, "head", axis=0)
    residual = (tokens.astype(f32) + project_out(gathered_one, w1_full)).astype(bf16)

    normed_two = rms_rows(residual.astype(f32), norm_two).astype(bf16)
    projected_two = jnp.dot(
        normed_two, w_qkv2.reshape(feature_width, 3 * inner_dev), preferred_element_type=f32
    )
    projected_two = projected_two.reshape(tok_rows, 3, heads_dev, head_dim)
    query_hat = rms_rows(projected_two[:, 0], q_gain).astype(bf16)
    key_hat = rms_rows(projected_two[:, 1], k_gain).astype(bf16)
    value_two = projected_two[:, 2].astype(bf16)

    plane_tiles = GY * GZ
    halo_rows = plane_tiles * TILE
    tile_count = tok_rows // TILE
    up = [(i, i + 1) for i in range(ctx_size - 1)]
    down = [(i + 1, i) for i in range(ctx_size - 1)]
    key_hat = jnp.transpose(key_hat, (1, 0, 2))
    value_two = jnp.transpose(value_two, (1, 0, 2))
    query_hat = jnp.transpose(query_hat, (1, 0, 2))
    key_prev = lax.ppermute(key_hat[:, tok_rows - halo_rows :], "ctx", up)
    value_prev = lax.ppermute(value_two[:, tok_rows - halo_rows :], "ctx", up)
    key_next = lax.ppermute(key_hat[:, :halo_rows], "ctx", down)
    value_next = lax.ppermute(value_two[:, :halo_rows], "ctx", down)
    own_first = ctx_index * tile_count
    arange_halo = jnp.arange(plane_tiles, dtype=jnp.int32)
    pieces = (
        (key_prev, value_prev, own_first - plane_tiles + arange_halo),
        (key_hat, value_two, own_first + jnp.arange(tile_count, dtype=jnp.int32)),
        (key_next, value_next, own_first + tile_count + arange_halo),
    )
    present = neighbours >= 0
    tile_masks = [
        jnp.any((neighbours[:, :, None] == ids[None, None, :]) & present[:, :, None], axis=1)
        for _, _, ids in pieces
    ]
    key_ok = jnp.repeat(jnp.concatenate(tile_masks, axis=1), TILE, axis=1).astype(f32)
    attn_two = tile_attention(
        query_hat, [p[0] for p in pieces], [p[1] for p in pieces], key_ok[:, None, :], TILE
    )
    attn_two = attn_two.reshape(heads_dev, head_size, rows_mine, head_dim)
    attn_two = lax.all_to_all(attn_two, "head", 1, 1, tiled=True)
    attn_two = jnp.transpose(attn_two, (1, 2, 0, 3)).reshape(head_size, rows_mine, inner_dev)
    residual_mine = lax.dynamic_slice_in_dim(residual, head_index * rows_mine, rows_mine, 0)
    mixed = residual_mine.astype(f32) + project_out(attn_two, w2_full)
    return mixed.astype(bf16)


def solution(mesh):
    in_specs = (
        P(("groups", "ctx"), None),
        P(),
        P(None, None, "head"),
        P("head"),
        P("head", None),
        P(),
        P(None, None, "head"),
        P(),
        P(),
        P("head", None),
        P("ctx", None),
    )
    out_specs = P(("groups", "ctx", "head"), None)
    return jax.shard_map(
        on_device, mesh=mesh, in_specs=in_specs, out_specs=out_specs, check_vma=False
    )
```

```python
import functools
import math

import jax
import jax.numpy as jnp
import numpy as np
from jax import lax
from jax.experimental import pallas as pl
from jax.sharding import PartitionSpec as P

TILE = 256
GY = 2
GZ = 2


EPS = 1e-06


def with_halo(shard, sides, width):
    for axis, dim in sides:
        size, length = (lax.axis_size(axis), shard.shape[dim])
        up = [(i, (i + 1) % size) for i in range(size - 1)]
        down = [(j, i) for i, j in up]
        last = lax.slice_in_dim(shard, length - width, length, axis=dim)
        first = lax.slice_in_dim(shard, 0, width, axis=dim)
        before = lax.ppermute(last, axis, up)
        after = lax.ppermute(first, axis, down)
        shard = jnp.concatenate([before, shard, after], axis=dim)
    return shard


def rms_rows(value, gain):
    mean_sq = jnp.mean(value * value, axis=-1, keepdims=True)
    return value * lax.rsqrt(mean_sq + EPS) * gain


def feature_map(value):
    return jnp.where(value > 0, value + 1.0, jnp.exp(jnp.minimum(value, 0.0)))


def split_two(value):
    high_part = value.astype(jnp.bfloat16)
    low_part = (value - high_part.astype(jnp.float32)).astype(jnp.bfloat16)
    return (high_part, low_part)


def _attn_kernel(q_ref, kp_ref, ko_ref, kn_ref, vp_ref, vo_ref, vn_ref, m_ref, o_ref, *, scale):
    query = q_ref[...]
    mask = m_ref[0]
    exps = []
    total = None
    offset = 0
    for k_ref in (kp_ref, ko_ref, kn_ref):
        rows = k_ref.shape[0]
        scores = (
            lax.dot_general(
                query, k_ref[...], (((1,), (1,)), ((), ())), preferred_element_type=jnp.float32
            )
            * scale
        )
        unnormed = jnp.where(mask[:, offset : offset + rows] > 0.5, jnp.exp(scores), 0.0)
        exps.append(unnormed)
        part = jnp.sum(unnormed, axis=-1, keepdims=True)
        total = part if total is None else total + part
        offset += rows
    inverse = 1.0 / total
    acc = None
    for unnormed, v_ref in zip(exps, (vp_ref, vo_ref, vn_ref)):
        weights = (unnormed * inverse).astype(jnp.bfloat16)
        term = jnp.dot(weights, v_ref[...], preferred_element_type=jnp.float32)
        acc = term if acc is None else acc + term
    o_ref[...] = acc.astype(o_ref.dtype)


def tile_attention(query, keys, values, mask, block_rows, interpret=False):
    heads, rows, head_dim = query.shape
    blocks = rows // block_rows
    key_width = mask.shape[-1]
    kv_specs = [pl.BlockSpec((None, k.shape[1], head_dim), lambda h, b: (h, 0, 0)) for k in keys]
    return pl.pallas_call(
        functools.partial(_attn_kernel, scale=1.0 / math.sqrt(head_dim)),
        out_shape=jax.ShapeDtypeStruct((heads, rows, head_dim), jnp.bfloat16),
        grid=(heads, blocks),
        in_specs=[pl.BlockSpec((None, block_rows, head_dim), lambda h, b: (h, b, 0))]
        + kv_specs
        + kv_specs
        + [pl.BlockSpec((1, 1, key_width), lambda h, b: (b, 0, 0))],
        out_specs=pl.BlockSpec((None, block_rows, head_dim), lambda h, b: (h, b, 0)),
        interpret=interpret,
    )(query, *keys, *values, mask)

def on_device(
    tokens, norm_one, w_qkv1, lin_gain, w_out1, norm_two, w_qkv2, q_gain, k_gain, w_out2, neighbours
):
    f32, bf16 = jnp.float32, jnp.bfloat16
    tok_rows, feature_width = tokens.shape
    inner_dev = w_qkv1.shape[2]
    head_dim = q_gain.shape[0]
    heads_dev = inner_dev // head_dim
    block_rows = 2 * TILE
    block_count = tok_rows // block_rows
    rows_mine = tok_rows // lax.axis_size("head")
    head_index = lax.axis_index("head")
    ctx_index = lax.axis_index("ctx")
    ctx_size = lax.axis_size("ctx")

    normed = rms_rows(tokens.astype(f32), norm_one).astype(bf16)
    projected = jnp.dot(
        normed, w_qkv1.reshape(feature_width, 3 * inner_dev), preferred_element_type=f32
    )
    projected = projected.reshape(tok_rows, 3, heads_dev, head_dim)
    query_map = feature_map(projected[:, 0]).astype(bf16)
    key_map = feature_map(projected[:, 1]).astype(bf16)
    value_one = projected[:, 2].astype(bf16)
    q_blocks = query_map.reshape(block_count, block_rows, heads_dev, head_dim)
    k_blocks = key_map.reshape(block_count, block_rows, heads_dev, head_dim)
    v_blocks = value_one.reshape(block_count, block_rows, heads_dev, head_dim)
    block_states = jnp.einsum(
        "nthe,nthf->nhef", k_blocks, v_blocks, preferred_element_type=f32
    )
    own_total = jnp.sum(block_states, axis=0)
    all_totals = lax.all_gather(own_total.astype(bf16), "ctx", axis=0).astype(f32)
    earlier_dev = jnp.arange(ctx_size, dtype=jnp.int32) < ctx_index
    carried = jnp.sum(jnp.where(earlier_dev[:, None, None, None], all_totals, 0.0), axis=0)

    causal = lax.broadcasted_iota(jnp.int32, (block_rows, block_rows), 0) >= lax.broadcasted_iota(
        jnp.int32, (block_rows, block_rows), 1
    )
    head_size = lax.axis_size("head")
    core = ctx_index % 2

    group_index = lax.axis_index("groups")
    y_bit = (ctx_index // 2) % 2
    slot = group_index * 4 + y_bit * 2 + core
    slice_rows = inner_dev // 8
    core_pairs = [(i, i ^ 1) for i in range(ctx_size)]
    y_pairs = [(i, i ^ 2) for i in range(ctx_size)]
    group_pairs = [(i, i ^ 1) for i in range(lax.axis_size("groups"))]
    group_count = lax.axis_size("groups")
    cross_pairs = [
        (g * ctx_size + i, (g ^ 1) * ctx_size + i)
        for g in range(group_count)
        for i in range(1, ctx_size, 2)
    ]

    def gather_weight(w):
        local = lax.dynamic_slice_in_dim(w, slot * slice_rows, slice_rows, 0)
        first = lax.all_gather(local, "head", axis=0)
        by_y = lax.ppermute(first, "ctx", y_pairs)
        by_group = lax.ppermute(first, "groups", group_pairs)
        relay_y = lax.ppermute(by_group, "ctx", [p for p in y_pairs if p[0] % 2 == 0])
        relay_group = lax.ppermute(by_y, ("groups", "ctx"), cross_pairs)
        by_both = jnp.where(core == 0, relay_y, relay_group)
        pieces = [first, by_y, by_group, by_both]
        pieces = pieces + [lax.ppermute(p, "ctx", core_pairs) for p in pieces]
        offsets = [0, 2, 4, 6, 1, 3, 5, 7]
        full = jnp.zeros((head_size, 8) + local.shape, local.dtype)
        for offset, piece in zip(offsets, pieces):
            full = lax.dynamic_update_slice_in_dim(
                full, piece[:, None], jnp.bitwise_xor(slot, offset), 1
            )
        return full.reshape(head_size, inner_dev, w.shape[1])

    def project_out(parts, full):
        total = 0.0
        for g in range(head_size):
            term = jnp.dot(parts[g], full[g], preferred_element_type=f32)
            total = total + term.astype(bf16).astype(f32)
        return total

    w1_full = gather_weight(w_out1)
    w2_full = gather_weight(w_out2)
    attn_parts = []
    for n in range(block_count):
        q_n, k_n, v_n = q_blocks[n], k_blocks[n], v_blocks[n]
        scores = jnp.einsum("the,she->hts", q_n, k_n, preferred_element_type=f32)
        scores = jnp.where(causal, scores, 0.0)
        score_high, score_low = split_two(scores)
        within = jnp.einsum("hts,she->the", score_high, v_n, preferred_element_type=f32)
        within = within + jnp.einsum("hts,she->the", score_low, v_n, preferred_element_type=f32)
        state_high, state_low = split_two(carried)
        carried_term = jnp.einsum("the,hef->thf", q_n, state_high, preferred_element_type=f32)
        carried_term = carried_term + jnp.einsum(
            "the,hef->thf", q_n, state_low, preferred_element_type=f32
        )
        carried = carried + block_states[n]
        combined = within + carried_term
        attn_parts.append(
            rms_rows(combined, lin_gain.reshape(heads_dev, head_dim))
            .astype(bf16)
            .reshape(block_rows, inner_dev)
        )
    attn_one = jnp.concatenate(attn_parts, axis=0)
    gathered_one = lax.all_gather(attn_one, "head", axis=0)
    residual = (tokens.astype(f32) + project_out(gathered_one, w1_full)).astype(bf16)

    normed_two = rms_rows(residual.astype(f32), norm_two).astype(bf16)
    projected_two = jnp.dot(
        normed_two, w_qkv2.reshape(feature_width, 3 * inner_dev), preferred_element_type=f32
    )
    projected_two = projected_two.reshape(tok_rows, 3, heads_dev, head_dim)
    query_hat = rms_rows(projected_two[:, 0], q_gain).astype(bf16)
    key_hat = rms_rows(projected_two[:, 1], k_gain).astype(bf16)
    value_two = projected_two[:, 2].astype(bf16)

    plane_tiles = GY * GZ
    halo_rows = plane_tiles * TILE
    tile_count = tok_rows // TILE
    up = [(i, i + 1) for i in range(ctx_size - 1)]
    down = [(i + 1, i) for i in range(ctx_size - 1)]
    key_hat = jnp.transpose(key_hat, (1, 0, 2))
    value_two = jnp.transpose(value_two, (1, 0, 2))
    query_hat = jnp.transpose(query_hat, (1, 0, 2))
    key_prev = lax.ppermute(key_hat[:, tok_rows - halo_rows :], "ctx", up)
    value_prev = lax.ppermute(value_two[:, tok_rows - halo_rows :], "ctx", up)
    key_next = lax.ppermute(key_hat[:, :halo_rows], "ctx", down)
    value_next = lax.ppermute(value_two[:, :halo_rows], "ctx", down)
    own_first = ctx_index * tile_count
    arange_halo = jnp.arange(plane_tiles, dtype=jnp.int32)
    pieces = (
        (key_prev, value_prev, own_first - plane_tiles + arange_halo),
        (key_hat, value_two, own_first + jnp.arange(tile_count, dtype=jnp.int32)),
        (key_next, value_next, own_first + tile_count + arange_halo),
    )
    present = neighbours >= 0
    tile_masks = [
        jnp.any((neighbours[:, :, None] == ids[None, None, :]) & present[:, :, None], axis=1)
        for _, _, ids in pieces
    ]
    key_ok = jnp.repeat(jnp.concatenate(tile_masks, axis=1), TILE, axis=1).astype(f32)
    attn_two = tile_attention(
        query_hat, [p[0] for p in pieces], [p[1] for p in pieces], key_ok[:, None, :], TILE
    )
    attn_two = attn_two.reshape(heads_dev, head_size, rows_mine, head_dim)
    attn_two = lax.all_to_all(attn_two, "head", 1, 1, tiled=True)
    attn_two = jnp.transpose(attn_two, (1, 2, 0, 3)).reshape(head_size, rows_mine, inner_dev)
    residual_mine = lax.dynamic_slice_in_dim(residual, head_index * rows_mine, rows_mine, 0)
    mixed = residual_mine.astype(f32) + project_out(attn_two, w2_full)
    return mixed.astype(bf16)


def solution(mesh):
    in_specs = (
        P(("groups", "ctx"), None),
        P(),
        P(None, None, "head"),
        P("head"),
        P("head", None),
        P(),
        P(None, None, "head"),
        P(),
        P(),
        P("head", None),
        P("ctx", None),
    )
    out_specs = P(("groups", "ctx", "head"), None)
    return jax.shard_map(
        on_device, mesh=mesh, in_specs=in_specs, out_specs=out_specs, check_vma=False
    )
```

```python
import functools
import math

import jax
import jax.numpy as jnp
import numpy as np
from jax import lax
from jax.experimental import pallas as pl
from jax.experimental.pallas import tpu as pltpu
from jax.sharding import PartitionSpec as P

TILE = 256
GY = 2
GZ = 2


EPS = 1e-06


def with_halo(shard, sides, width):
    for axis, dim in sides:
        size, length = (lax.axis_size(axis), shard.shape[dim])
        up = [(i, (i + 1) % size) for i in range(size - 1)]
        down = [(j, i) for i, j in up]
        last = lax.slice_in_dim(shard, length - width, length, axis=dim)
        first = lax.slice_in_dim(shard, 0, width, axis=dim)
        before = lax.ppermute(last, axis, up)
        after = lax.ppermute(first, axis, down)
        shard = jnp.concatenate([before, shard, after], axis=dim)
    return shard


def rms_rows(value, gain):
    mean_sq = jnp.mean(value * value, axis=-1, keepdims=True)
    return value * lax.rsqrt(mean_sq + EPS) * gain


def feature_map(value):
    return jnp.where(value > 0, value + 1.0, jnp.exp(jnp.minimum(value, 0.0)))


def split_two(value):
    high_part = value.astype(jnp.bfloat16)
    low_part = (value - high_part.astype(jnp.float32)).astype(jnp.bfloat16)
    return (high_part, low_part)


def _attn_kernel(valid_ref, q_ref, kp_ref, ko_ref, kn_ref, vp_ref, vo_ref, vn_ref, o_ref,
                 exp_ref, sum_ref, acc_ref, *, scale):
    block = pl.program_id(1)
    query = q_ref[...]
    slots = []
    for k_ref, v_ref in ((kp_ref, vp_ref), (ko_ref, vo_ref), (kn_ref, vn_ref)):
        for start in range(0, k_ref.shape[0], TILE):
            slots.append((k_ref, v_ref, start))
    sum_ref[...] = jnp.zeros_like(sum_ref)
    acc_ref[...] = jnp.zeros_like(acc_ref)
    for index, (k_ref, _, start) in enumerate(slots):

        @pl.when(valid_ref[block, index] > 0)
        def _():
            scores = (
                lax.dot_general(
                    query,
                    k_ref[pl.ds(start, TILE), :],
                    (((1,), (1,)), ((), ())),
                    preferred_element_type=jnp.float32,
                )
                * scale
            )
            unnormed = jnp.exp(scores)
            exp_ref[index] = unnormed
            sum_ref[...] += jnp.sum(unnormed, axis=-1, keepdims=True)

    inverse = 1.0 / sum_ref[...]
    for index, (_, v_ref, start) in enumerate(slots):

        @pl.when(valid_ref[block, index] > 0)
        def _():
            weights = (exp_ref[index] * inverse).astype(jnp.bfloat16)
            acc_ref[...] += jnp.dot(
                weights, v_ref[pl.ds(start, TILE), :], preferred_element_type=jnp.float32
            )

    o_ref[...] = acc_ref[...].astype(o_ref.dtype)


def tile_attention(query, keys, values, valid, block_rows, interpret=False):
    heads, rows, head_dim = query.shape
    blocks = rows // block_rows
    key_tiles = valid.shape[1]
    kv_specs = [
        pl.BlockSpec((None, k.shape[1], head_dim), lambda h, b, v: (h, 0, 0)) for k in keys
    ]
    grid_spec = pltpu.PrefetchScalarGridSpec(
        num_scalar_prefetch=1,
        grid=(heads, blocks),
        in_specs=[pl.BlockSpec((None, block_rows, head_dim), lambda h, b, v: (h, b, 0))]
        + kv_specs
        + kv_specs,
        out_specs=pl.BlockSpec((None, block_rows, head_dim), lambda h, b, v: (h, b, 0)),
        scratch_shapes=[
            pltpu.VMEM((key_tiles, block_rows, TILE), jnp.float32),
            pltpu.VMEM((block_rows, 1), jnp.float32),
            pltpu.VMEM((block_rows, head_dim), jnp.float32),
        ],
    )
    return pl.pallas_call(
        functools.partial(_attn_kernel, scale=1.0 / math.sqrt(head_dim)),
        out_shape=jax.ShapeDtypeStruct((heads, rows, head_dim), jnp.bfloat16),
        grid_spec=grid_spec,
        interpret=interpret,
    )(valid, query, *keys, *values)

def on_device(
    tokens, norm_one, w_qkv1, lin_gain, w_out1, norm_two, w_qkv2, q_gain, k_gain, w_out2, neighbours
):
    f32, bf16 = jnp.float32, jnp.bfloat16
    tok_rows, feature_width = tokens.shape
    inner_dev = w_qkv1.shape[2]
    head_dim = q_gain.shape[0]
    heads_dev = inner_dev // head_dim
    block_rows = 2 * TILE
    block_count = tok_rows // block_rows
    rows_mine = tok_rows // lax.axis_size("head")
    head_index = lax.axis_index("head")
    ctx_index = lax.axis_index("ctx")
    ctx_size = lax.axis_size("ctx")

    normed = rms_rows(tokens.astype(f32), norm_one).astype(bf16)
    projected = jnp.dot(
        normed, w_qkv1.reshape(feature_width, 3 * inner_dev), preferred_element_type=f32
    )
    projected = projected.reshape(tok_rows, 3, heads_dev, head_dim)
    query_map = feature_map(projected[:, 0]).astype(bf16)
    key_map = feature_map(projected[:, 1]).astype(bf16)
    value_one = projected[:, 2].astype(bf16)
    q_blocks = query_map.reshape(block_count, block_rows, heads_dev, head_dim)
    k_blocks = key_map.reshape(block_count, block_rows, heads_dev, head_dim)
    v_blocks = value_one.reshape(block_count, block_rows, heads_dev, head_dim)
    block_states = jnp.einsum(
        "nthe,nthf->nhef", k_blocks, v_blocks, preferred_element_type=f32
    )
    own_total = jnp.sum(block_states, axis=0)
    all_totals = lax.all_gather(own_total.astype(bf16), "ctx", axis=0).astype(f32)
    earlier_dev = jnp.arange(ctx_size, dtype=jnp.int32) < ctx_index
    carried = jnp.sum(jnp.where(earlier_dev[:, None, None, None], all_totals, 0.0), axis=0)

    causal = lax.broadcasted_iota(jnp.int32, (block_rows, block_rows), 0) >= lax.broadcasted_iota(
        jnp.int32, (block_rows, block_rows), 1
    )
    head_size = lax.axis_size("head")
    core = ctx_index % 2

    group_index = lax.axis_index("groups")
    y_bit = (ctx_index // 2) % 2
    slot = group_index * 4 + y_bit * 2 + core
    slice_rows = inner_dev // 8
    core_pairs = [(i, i ^ 1) for i in range(ctx_size)]
    y_pairs = [(i, i ^ 2) for i in range(ctx_size)]
    group_pairs = [(i, i ^ 1) for i in range(lax.axis_size("groups"))]
    group_count = lax.axis_size("groups")
    cross_pairs = [
        (g * ctx_size + i, (g ^ 1) * ctx_size + i)
        for g in range(group_count)
        for i in range(1, ctx_size, 2)
    ]

    def gather_weight(w):
        local = lax.dynamic_slice_in_dim(w, slot * slice_rows, slice_rows, 0)
        first = lax.all_gather(local, "head", axis=0)
        by_y = lax.ppermute(first, "ctx", y_pairs)
        by_group = lax.ppermute(first, "groups", group_pairs)
        relay_y = lax.ppermute(by_group, "ctx", [p for p in y_pairs if p[0] % 2 == 0])
        relay_group = lax.ppermute(by_y, ("groups", "ctx"), cross_pairs)
        by_both = jnp.where(core == 0, relay_y, relay_group)
        pieces = [first, by_y, by_group, by_both]
        pieces = pieces + [lax.ppermute(p, "ctx", core_pairs) for p in pieces]
        offsets = [0, 2, 4, 6, 1, 3, 5, 7]
        full = jnp.zeros((head_size, 8) + local.shape, local.dtype)
        for offset, piece in zip(offsets, pieces):
            full = lax.dynamic_update_slice_in_dim(
                full, piece[:, None], jnp.bitwise_xor(slot, offset), 1
            )
        return full.reshape(head_size, inner_dev, w.shape[1])

    def project_out(parts, full):
        total = 0.0
        for g in range(head_size):
            term = jnp.dot(parts[g], full[g], preferred_element_type=f32)
            total = total + term.astype(bf16).astype(f32)
        return total

    w1_full = gather_weight(w_out1)
    w2_full = gather_weight(w_out2)
    attn_parts = []
    for n in range(block_count):
        q_n, k_n, v_n = q_blocks[n], k_blocks[n], v_blocks[n]
        scores = jnp.einsum("the,she->hts", q_n, k_n, preferred_element_type=f32)
        scores = jnp.where(causal, scores, 0.0)
        score_high, score_low = split_two(scores)
        within = jnp.einsum("hts,she->the", score_high, v_n, preferred_element_type=f32)
        within = within + jnp.einsum("hts,she->the", score_low, v_n, preferred_element_type=f32)
        state_high, state_low = split_two(carried)
        carried_term = jnp.einsum("the,hef->thf", q_n, state_high, preferred_element_type=f32)
        carried_term = carried_term + jnp.einsum(
            "the,hef->thf", q_n, state_low, preferred_element_type=f32
        )
        carried = carried + block_states[n]
        combined = within + carried_term
        attn_parts.append(
            rms_rows(combined, lin_gain.reshape(heads_dev, head_dim))
            .astype(bf16)
            .reshape(block_rows, inner_dev)
        )
    attn_one = jnp.concatenate(attn_parts, axis=0)
    gathered_one = lax.all_gather(attn_one, "head", axis=0)
    residual = (tokens.astype(f32) + project_out(gathered_one, w1_full)).astype(bf16)

    normed_two = rms_rows(residual.astype(f32), norm_two).astype(bf16)
    projected_two = jnp.dot(
        normed_two, w_qkv2.reshape(feature_width, 3 * inner_dev), preferred_element_type=f32
    )
    projected_two = projected_two.reshape(tok_rows, 3, heads_dev, head_dim)
    query_hat = rms_rows(projected_two[:, 0], q_gain).astype(bf16)
    key_hat = rms_rows(projected_two[:, 1], k_gain).astype(bf16)
    value_two = projected_two[:, 2].astype(bf16)

    plane_tiles = GY * GZ
    halo_rows = plane_tiles * TILE
    tile_count = tok_rows // TILE
    up = [(i, i + 1) for i in range(ctx_size - 1)]
    down = [(i + 1, i) for i in range(ctx_size - 1)]
    key_hat = jnp.transpose(key_hat, (1, 0, 2))
    value_two = jnp.transpose(value_two, (1, 0, 2))
    query_hat = jnp.transpose(query_hat, (1, 0, 2))
    key_prev = lax.ppermute(key_hat[:, tok_rows - halo_rows :], "ctx", up)
    value_prev = lax.ppermute(value_two[:, tok_rows - halo_rows :], "ctx", up)
    key_next = lax.ppermute(key_hat[:, :halo_rows], "ctx", down)
    value_next = lax.ppermute(value_two[:, :halo_rows], "ctx", down)
    own_first = ctx_index * tile_count
    arange_halo = jnp.arange(plane_tiles, dtype=jnp.int32)
    pieces = (
        (key_prev, value_prev, own_first - plane_tiles + arange_halo),
        (key_hat, value_two, own_first + jnp.arange(tile_count, dtype=jnp.int32)),
        (key_next, value_next, own_first + tile_count + arange_halo),
    )
    present = neighbours >= 0
    tile_masks = [
        jnp.any((neighbours[:, :, None] == ids[None, None, :]) & present[:, :, None], axis=1)
        for _, _, ids in pieces
    ]
    tile_ok = jnp.concatenate(tile_masks, axis=1).astype(jnp.int32)
    attn_two = tile_attention(
        query_hat, [p[0] for p in pieces], [p[1] for p in pieces], tile_ok, TILE
    )
    attn_two = attn_two.reshape(heads_dev, head_size, rows_mine, head_dim)
    attn_two = lax.all_to_all(attn_two, "head", 1, 1, tiled=True)
    attn_two = jnp.transpose(attn_two, (1, 2, 0, 3)).reshape(head_size, rows_mine, inner_dev)
    residual_mine = lax.dynamic_slice_in_dim(residual, head_index * rows_mine, rows_mine, 0)
    mixed = residual_mine.astype(f32) + project_out(attn_two, w2_full)
    return mixed.astype(bf16)


def solution(mesh):
    in_specs = (
        P(("groups", "ctx"), None),
        P(),
        P(None, None, "head"),
        P("head"),
        P("head", None),
        P(),
        P(None, None, "head"),
        P(),
        P(),
        P("head", None),
        P("ctx", None),
    )
    out_specs = P(("groups", "ctx", "head"), None)
    return jax.shard_map(
        on_device, mesh=mesh, in_specs=in_specs, out_specs=out_specs, check_vma=False
    )
```

```python
import functools
import math

import jax
import jax.numpy as jnp
import numpy as np
from jax import lax
from jax.experimental import pallas as pl
from jax.sharding import PartitionSpec as P

TILE = 256
GY = 2
GZ = 2


EPS = 1e-06


def with_halo(shard, sides, width):
    for axis, dim in sides:
        size, length = (lax.axis_size(axis), shard.shape[dim])
        up = [(i, (i + 1) % size) for i in range(size - 1)]
        down = [(j, i) for i, j in up]
        last = lax.slice_in_dim(shard, length - width, length, axis=dim)
        first = lax.slice_in_dim(shard, 0, width, axis=dim)
        before = lax.ppermute(last, axis, up)
        after = lax.ppermute(first, axis, down)
        shard = jnp.concatenate([before, shard, after], axis=dim)
    return shard


def rms_rows(value, gain):
    mean_sq = jnp.mean(value * value, axis=-1, keepdims=True)
    return value * lax.rsqrt(mean_sq + EPS) * gain


def feature_map(value):
    return jnp.where(value > 0, value + 1.0, jnp.exp(jnp.minimum(value, 0.0)))


def split_two(value):
    high_part = value.astype(jnp.bfloat16)
    low_part = (value - high_part.astype(jnp.float32)).astype(jnp.bfloat16)
    return (high_part, low_part)


def _attn_kernel(q_ref, kp_ref, ko_ref, kn_ref, vp_ref, vo_ref, vn_ref, m_ref, o_ref, *, scale):
    query = q_ref[...]
    mask = m_ref[0]
    exps = []
    total = None
    offset = 0
    for k_ref in (kp_ref, ko_ref, kn_ref):
        rows = k_ref.shape[0]
        scores = (
            lax.dot_general(
                query, k_ref[...], (((1,), (1,)), ((), ())), preferred_element_type=jnp.float32
            )
            * scale
        )
        unnormed = jnp.where(mask[:, offset : offset + rows] > 0.5, jnp.exp(scores), 0.0)
        exps.append(unnormed)
        part = jnp.sum(unnormed, axis=-1, keepdims=True)
        total = part if total is None else total + part
        offset += rows
    inverse = 1.0 / total
    acc = None
    for unnormed, v_ref in zip(exps, (vp_ref, vo_ref, vn_ref)):
        weights = (unnormed * inverse).astype(jnp.bfloat16)
        term = jnp.dot(weights, v_ref[...], preferred_element_type=jnp.float32)
        acc = term if acc is None else acc + term
    o_ref[...] = acc.astype(o_ref.dtype)


def tile_attention(query, keys, values, mask, block_rows, interpret=False):
    heads, rows, head_dim = query.shape
    blocks = rows // block_rows
    key_width = mask.shape[-1]
    kv_specs = [pl.BlockSpec((None, k.shape[1], head_dim), lambda h, b: (h, 0, 0)) for k in keys]
    return pl.pallas_call(
        functools.partial(_attn_kernel, scale=1.0 / math.sqrt(head_dim)),
        out_shape=jax.ShapeDtypeStruct((heads, rows, head_dim), jnp.bfloat16),
        grid=(heads, blocks),
        in_specs=[pl.BlockSpec((None, block_rows, head_dim), lambda h, b: (h, b, 0))]
        + kv_specs
        + kv_specs
        + [pl.BlockSpec((1, 1, key_width), lambda h, b: (b, 0, 0))],
        out_specs=pl.BlockSpec((None, block_rows, head_dim), lambda h, b: (h, b, 0)),
        interpret=interpret,
    )(query, *keys, *values, mask)

def on_device(
    tokens, norm_one, w_qkv1, lin_gain, w_out1, norm_two, w_qkv2, q_gain, k_gain, w_out2, neighbours
):
    f32, bf16 = jnp.float32, jnp.bfloat16
    tok_rows, feature_width = tokens.shape
    inner_dev = w_qkv1.shape[2]
    head_dim = q_gain.shape[0]
    heads_dev = inner_dev // head_dim
    block_rows = 2 * TILE
    block_count = tok_rows // block_rows
    rows_mine = tok_rows // lax.axis_size("head")
    head_index = lax.axis_index("head")
    ctx_index = lax.axis_index("ctx")
    ctx_size = lax.axis_size("ctx")

    normed = rms_rows(tokens.astype(f32), norm_one).astype(bf16)
    projected = jnp.dot(
        normed, w_qkv1.reshape(feature_width, 3 * inner_dev), preferred_element_type=f32
    )
    projected = projected.reshape(tok_rows, 3, heads_dev, head_dim)
    query_map = feature_map(projected[:, 0]).astype(bf16)
    key_map = feature_map(projected[:, 1]).astype(bf16)
    value_one = projected[:, 2].astype(bf16)
    q_blocks = query_map.reshape(block_count, block_rows, heads_dev, head_dim)
    k_blocks = key_map.reshape(block_count, block_rows, heads_dev, head_dim)
    v_blocks = value_one.reshape(block_count, block_rows, heads_dev, head_dim)
    block_states = jnp.einsum(
        "nthe,nthf->nhef", k_blocks, v_blocks, preferred_element_type=f32
    )
    own_total = jnp.sum(block_states, axis=0)
    all_totals = lax.all_gather(own_total.astype(bf16), "ctx", axis=0).astype(f32)
    earlier_dev = jnp.arange(ctx_size, dtype=jnp.int32) < ctx_index
    carried = jnp.sum(jnp.where(earlier_dev[:, None, None, None], all_totals, 0.0), axis=0)

    causal = lax.broadcasted_iota(jnp.int32, (block_rows, block_rows), 0) >= lax.broadcasted_iota(
        jnp.int32, (block_rows, block_rows), 1
    )
    head_size = lax.axis_size("head")
    core = ctx_index % 2

    group_index = lax.axis_index("groups")
    y_bit = (ctx_index // 2) % 2
    slot = group_index * 4 + y_bit * 2 + core
    slice_rows = inner_dev // 8
    core_pairs = [(i, i ^ 1) for i in range(ctx_size)]
    y_pairs = [(i, i ^ 2) for i in range(ctx_size)]
    group_pairs = [(i, i ^ 1) for i in range(lax.axis_size("groups"))]
    group_count = lax.axis_size("groups")
    cross_pairs = [
        (g * ctx_size + i, (g ^ 1) * ctx_size + i)
        for g in range(group_count)
        for i in range(1, ctx_size, 2)
    ]

    def gather_weight(w):
        local = lax.dynamic_slice_in_dim(w, slot * slice_rows, slice_rows, 0)
        first = lax.all_gather(local, "head", axis=0)
        by_y = lax.ppermute(first, "ctx", y_pairs)
        by_group = lax.ppermute(first, "groups", group_pairs)
        relay_y = lax.ppermute(by_group, "ctx", [p for p in y_pairs if p[0] % 2 == 0])
        relay_group = lax.ppermute(by_y, ("groups", "ctx"), cross_pairs)
        by_both = jnp.where(core == 0, relay_y, relay_group)
        pieces = [first, by_y, by_group, by_both]
        pieces = pieces + [lax.ppermute(p, "ctx", core_pairs) for p in pieces]
        offsets = [0, 2, 4, 6, 1, 3, 5, 7]
        full = jnp.zeros((head_size, 8) + local.shape, local.dtype)
        for offset, piece in zip(offsets, pieces):
            full = lax.dynamic_update_slice_in_dim(
                full, piece[:, None], jnp.bitwise_xor(slot, offset), 1
            )
        return full.reshape(head_size, inner_dev, w.shape[1])

    def project_out(parts, full):
        total = 0.0
        for g in range(head_size):
            term = jnp.dot(parts[g], full[g], preferred_element_type=f32)
            total = total + term.astype(bf16).astype(f32)
        return total

    w1_full = gather_weight(w_out1)
    w2_full = gather_weight(w_out2)
    attn_parts = []
    for n in range(block_count):
        q_n, k_n, v_n = q_blocks[n], k_blocks[n], v_blocks[n]
        scores = jnp.einsum("the,she->hts", q_n, k_n, preferred_element_type=f32)
        scores = jnp.where(causal, scores, 0.0)
        score_high, score_low = split_two(scores)
        within = jnp.einsum("hts,she->the", score_high, v_n, preferred_element_type=f32)
        within = within + jnp.einsum("hts,she->the", score_low, v_n, preferred_element_type=f32)
        state_high, state_low = split_two(carried)
        carried_term = jnp.einsum("the,hef->thf", q_n, state_high, preferred_element_type=f32)
        carried_term = carried_term + jnp.einsum(
            "the,hef->thf", q_n, state_low, preferred_element_type=f32
        )
        carried = carried + block_states[n]
        combined = within + carried_term
        attn_parts.append(
            rms_rows(combined, lin_gain.reshape(heads_dev, head_dim))
            .astype(bf16)
            .reshape(block_rows, inner_dev)
        )
    attn_one = jnp.concatenate(attn_parts, axis=0)
    gathered_one = lax.all_gather(attn_one, "head", axis=0)
    residual = (tokens.astype(f32) + project_out(gathered_one, w1_full)).astype(bf16)

    normed_two = rms_rows(residual.astype(f32), norm_two).astype(bf16)
    projected_kv = jnp.dot(
        normed_two, w_qkv2[:, 1:].reshape(feature_width, 2 * inner_dev), preferred_element_type=f32
    ).reshape(tok_rows, 2, heads_dev, head_dim)
    key_hat = rms_rows(projected_kv[:, 0], k_gain).astype(bf16)
    value_two = projected_kv[:, 1].astype(bf16)
    key_hat, value_two, normed_two = lax.optimization_barrier((key_hat, value_two, normed_two))
    projected_q = jnp.dot(normed_two, w_qkv2[:, 0], preferred_element_type=f32)
    query_hat = rms_rows(projected_q.reshape(tok_rows, heads_dev, head_dim), q_gain).astype(bf16)

    plane_tiles = GY * GZ
    halo_rows = plane_tiles * TILE
    tile_count = tok_rows // TILE
    up = [(i, i + 1) for i in range(ctx_size - 1)]
    down = [(i + 1, i) for i in range(ctx_size - 1)]
    key_hat = jnp.transpose(key_hat, (1, 0, 2))
    value_two = jnp.transpose(value_two, (1, 0, 2))
    query_hat = jnp.transpose(query_hat, (1, 0, 2))
    key_prev = lax.ppermute(key_hat[:, tok_rows - halo_rows :], "ctx", up)
    value_prev = lax.ppermute(value_two[:, tok_rows - halo_rows :], "ctx", up)
    key_next = lax.ppermute(key_hat[:, :halo_rows], "ctx", down)
    value_next = lax.ppermute(value_two[:, :halo_rows], "ctx", down)
    own_first = ctx_index * tile_count
    arange_halo = jnp.arange(plane_tiles, dtype=jnp.int32)
    pieces = (
        (key_prev, value_prev, own_first - plane_tiles + arange_halo),
        (key_hat, value_two, own_first + jnp.arange(tile_count, dtype=jnp.int32)),
        (key_next, value_next, own_first + tile_count + arange_halo),
    )
    present = neighbours >= 0
    tile_masks = [
        jnp.any((neighbours[:, :, None] == ids[None, None, :]) & present[:, :, None], axis=1)
        for _, _, ids in pieces
    ]
    key_ok = jnp.repeat(jnp.concatenate(tile_masks, axis=1), TILE, axis=1).astype(f32)
    attn_two = tile_attention(
        query_hat, [p[0] for p in pieces], [p[1] for p in pieces], key_ok[:, None, :], TILE
    )
    attn_two = attn_two.reshape(heads_dev, head_size, rows_mine, head_dim)
    attn_two = lax.all_to_all(attn_two, "head", 1, 1, tiled=True)
    attn_two = jnp.transpose(attn_two, (1, 2, 0, 3)).reshape(head_size, rows_mine, inner_dev)
    residual_mine = lax.dynamic_slice_in_dim(residual, head_index * rows_mine, rows_mine, 0)
    mixed = residual_mine.astype(f32) + project_out(attn_two, w2_full)
    return mixed.astype(bf16)


def solution(mesh):
    in_specs = (
        P(("groups", "ctx"), None),
        P(),
        P(None, None, "head"),
        P("head"),
        P("head", None),
        P(),
        P(None, None, "head"),
        P(),
        P(),
        P("head", None),
        P("ctx", None),
    )
    out_specs = P(("groups", "ctx", "head"), None)
    return jax.shard_map(
        on_device, mesh=mesh, in_specs=in_specs, out_specs=out_specs, check_vma=False
    )
```

```python
import functools
import math

import jax
import jax.numpy as jnp
import numpy as np
from jax import lax
from jax.experimental import pallas as pl
from jax.sharding import PartitionSpec as P

TILE = 256
GY = 2
GZ = 2


EPS = 1e-06


def with_halo(shard, sides, width):
    for axis, dim in sides:
        size, length = (lax.axis_size(axis), shard.shape[dim])
        up = [(i, (i + 1) % size) for i in range(size - 1)]
        down = [(j, i) for i, j in up]
        last = lax.slice_in_dim(shard, length - width, length, axis=dim)
        first = lax.slice_in_dim(shard, 0, width, axis=dim)
        before = lax.ppermute(last, axis, up)
        after = lax.ppermute(first, axis, down)
        shard = jnp.concatenate([before, shard, after], axis=dim)
    return shard


def rms_rows(value, gain):
    mean_sq = jnp.mean(value * value, axis=-1, keepdims=True)
    return value * lax.rsqrt(mean_sq + EPS) * gain


def feature_map(value):
    return jnp.where(value > 0, value + 1.0, jnp.exp(jnp.minimum(value, 0.0)))


def split_two(value):
    high_part = value.astype(jnp.bfloat16)
    low_part = (value - high_part.astype(jnp.float32)).astype(jnp.bfloat16)
    return (high_part, low_part)


def _attn_kernel(q_ref, kp_ref, ko_ref, kn_ref, vp_ref, vo_ref, vn_ref, m_ref, o_ref, *, scale):
    query = q_ref[...]
    mask = m_ref[0]
    exps = []
    total = None
    offset = 0
    for k_ref in (kp_ref, ko_ref, kn_ref):
        rows = k_ref.shape[0]
        scores = (
            lax.dot_general(
                query, k_ref[...], (((1,), (1,)), ((), ())), preferred_element_type=jnp.float32
            )
            * scale
        )
        unnormed = jnp.where(mask[:, offset : offset + rows] > 0.5, jnp.exp(scores), 0.0)
        exps.append(unnormed)
        part = jnp.sum(unnormed, axis=-1, keepdims=True)
        total = part if total is None else total + part
        offset += rows
    inverse = 1.0 / total
    acc = None
    for unnormed, v_ref in zip(exps, (vp_ref, vo_ref, vn_ref)):
        weights = (unnormed * inverse).astype(jnp.bfloat16)
        term = jnp.dot(weights, v_ref[...], preferred_element_type=jnp.float32)
        acc = term if acc is None else acc + term
    o_ref[...] = acc.astype(o_ref.dtype)


def tile_attention(query, keys, values, mask, block_rows, head_offset=0, head_count=None):
    heads, rows, head_dim = query.shape
    head_count = heads if head_count is None else head_count
    blocks = rows // block_rows
    key_width = mask.shape[-1]
    kv_specs = [
        pl.BlockSpec((None, k.shape[1], head_dim), lambda h, b: (h + head_offset, 0, 0))
        for k in keys
    ]
    return pl.pallas_call(
        functools.partial(_attn_kernel, scale=1.0 / math.sqrt(head_dim)),
        out_shape=jax.ShapeDtypeStruct((head_count, rows, head_dim), jnp.bfloat16),
        grid=(head_count, blocks),
        in_specs=[
            pl.BlockSpec((None, block_rows, head_dim), lambda h, b: (h + head_offset, b, 0))
        ]
        + kv_specs
        + kv_specs
        + [pl.BlockSpec((1, 1, key_width), lambda h, b: (b, 0, 0))],
        out_specs=pl.BlockSpec((None, block_rows, head_dim), lambda h, b: (h, b, 0)),
    )(query, *keys, *values, mask)


def on_device(
    tokens, norm_one, w_qkv1, lin_gain, w_out1, norm_two, w_qkv2, q_gain, k_gain, w_out2, neighbours
):
    f32, bf16 = jnp.float32, jnp.bfloat16
    tok_rows, feature_width = tokens.shape
    inner_dev = w_qkv1.shape[2]
    head_dim = q_gain.shape[0]
    heads_dev = inner_dev // head_dim
    block_rows = 2 * TILE
    block_count = tok_rows // block_rows
    rows_mine = tok_rows // lax.axis_size("head")
    head_index = lax.axis_index("head")
    ctx_index = lax.axis_index("ctx")
    ctx_size = lax.axis_size("ctx")

    normed = rms_rows(tokens.astype(f32), norm_one).astype(bf16)
    projected = jnp.dot(
        normed, w_qkv1.reshape(feature_width, 3 * inner_dev), preferred_element_type=f32
    )
    projected = projected.reshape(tok_rows, 3, heads_dev, head_dim)
    query_map = feature_map(projected[:, 0]).astype(bf16)
    key_map = feature_map(projected[:, 1]).astype(bf16)
    value_one = projected[:, 2].astype(bf16)
    q_blocks = query_map.reshape(block_count, block_rows, heads_dev, head_dim)
    k_blocks = key_map.reshape(block_count, block_rows, heads_dev, head_dim)
    v_blocks = value_one.reshape(block_count, block_rows, heads_dev, head_dim)
    block_states = jnp.einsum(
        "nthe,nthf->nhef", k_blocks, v_blocks, preferred_element_type=f32
    )
    own_total = jnp.sum(block_states, axis=0)
    all_totals = lax.all_gather(own_total.astype(bf16), "ctx", axis=0).astype(f32)
    earlier_dev = jnp.arange(ctx_size, dtype=jnp.int32) < ctx_index
    carried = jnp.sum(jnp.where(earlier_dev[:, None, None, None], all_totals, 0.0), axis=0)

    causal = lax.broadcasted_iota(jnp.int32, (block_rows, block_rows), 0) >= lax.broadcasted_iota(
        jnp.int32, (block_rows, block_rows), 1
    )
    head_size = lax.axis_size("head")
    core = ctx_index % 2

    group_index = lax.axis_index("groups")
    y_bit = (ctx_index // 2) % 2
    slot = group_index * 4 + y_bit * 2 + core
    slice_rows = inner_dev // 8
    core_pairs = [(i, i ^ 1) for i in range(ctx_size)]
    y_pairs = [(i, i ^ 2) for i in range(ctx_size)]
    group_pairs = [(i, i ^ 1) for i in range(lax.axis_size("groups"))]
    group_count = lax.axis_size("groups")
    cross_pairs = [
        (g * ctx_size + i, (g ^ 1) * ctx_size + i)
        for g in range(group_count)
        for i in range(1, ctx_size, 2)
    ]

    def gather_weight(w):
        local = lax.dynamic_slice_in_dim(w, slot * slice_rows, slice_rows, 0)
        first = lax.all_gather(local, "head", axis=0)
        by_y = lax.ppermute(first, "ctx", y_pairs)
        by_group = lax.ppermute(first, "groups", group_pairs)
        relay_y = lax.ppermute(by_group, "ctx", [p for p in y_pairs if p[0] % 2 == 0])
        relay_group = lax.ppermute(by_y, ("groups", "ctx"), cross_pairs)
        by_both = jnp.where(core == 0, relay_y, relay_group)
        pieces = [first, by_y, by_group, by_both]
        pieces = pieces + [lax.ppermute(p, "ctx", core_pairs) for p in pieces]
        offsets = [0, 2, 4, 6, 1, 3, 5, 7]
        full = jnp.zeros((head_size, 8) + local.shape, local.dtype)
        for offset, piece in zip(offsets, pieces):
            full = lax.dynamic_update_slice_in_dim(
                full, piece[:, None], jnp.bitwise_xor(slot, offset), 1
            )
        return full.reshape(head_size, inner_dev, w.shape[1])

    def project_out(parts, full):
        total = 0.0
        for g in range(head_size):
            term = jnp.dot(parts[g], full[g], preferred_element_type=f32)
            total = total + term.astype(bf16).astype(f32)
        return total

    w1_full = gather_weight(w_out1)
    w2_full = gather_weight(w_out2)
    attn_parts = []
    for n in range(block_count):
        q_n, k_n, v_n = q_blocks[n], k_blocks[n], v_blocks[n]
        scores = jnp.einsum("the,she->hts", q_n, k_n, preferred_element_type=f32)
        scores = jnp.where(causal, scores, 0.0)
        score_high, score_low = split_two(scores)
        within = jnp.einsum("hts,she->the", score_high, v_n, preferred_element_type=f32)
        within = within + jnp.einsum("hts,she->the", score_low, v_n, preferred_element_type=f32)
        state_high, state_low = split_two(carried)
        carried_term = jnp.einsum("the,hef->thf", q_n, state_high, preferred_element_type=f32)
        carried_term = carried_term + jnp.einsum(
            "the,hef->thf", q_n, state_low, preferred_element_type=f32
        )
        carried = carried + block_states[n]
        combined = within + carried_term
        attn_parts.append(
            rms_rows(combined, lin_gain.reshape(heads_dev, head_dim))
            .astype(bf16)
            .reshape(block_rows, inner_dev)
        )
    attn_one = jnp.concatenate(attn_parts, axis=0)
    gathered_one = lax.all_gather(attn_one, "head", axis=0)
    residual = (tokens.astype(f32) + project_out(gathered_one, w1_full)).astype(bf16)

    normed_two = rms_rows(residual.astype(f32), norm_two).astype(bf16)
    projected_kv = jnp.dot(
        normed_two, w_qkv2[:, 1:].reshape(feature_width, 2 * inner_dev), preferred_element_type=f32
    ).reshape(tok_rows, 2, heads_dev, head_dim)
    key_hat = rms_rows(projected_kv[:, 0], k_gain).astype(bf16)
    value_two = projected_kv[:, 1].astype(bf16)
    key_hat, value_two, normed_two = lax.optimization_barrier((key_hat, value_two, normed_two))
    projected_q = jnp.dot(normed_two, w_qkv2[:, 0], preferred_element_type=f32)
    query_hat = rms_rows(projected_q.reshape(tok_rows, heads_dev, head_dim), q_gain).astype(bf16)

    plane_tiles = GY * GZ
    halo_rows = plane_tiles * TILE
    tile_count = tok_rows // TILE
    up = [(i, i + 1) for i in range(ctx_size - 1)]
    down = [(i + 1, i) for i in range(ctx_size - 1)]
    key_hat = jnp.transpose(key_hat, (1, 0, 2))
    value_two = jnp.transpose(value_two, (1, 0, 2))
    query_hat = jnp.transpose(query_hat, (1, 0, 2))
    key_prev = lax.ppermute(key_hat[:, tok_rows - halo_rows :], "ctx", up)
    value_prev = lax.ppermute(value_two[:, tok_rows - halo_rows :], "ctx", up)
    key_next = lax.ppermute(key_hat[:, :halo_rows], "ctx", down)
    value_next = lax.ppermute(value_two[:, :halo_rows], "ctx", down)
    own_first = ctx_index * tile_count
    arange_halo = jnp.arange(plane_tiles, dtype=jnp.int32)
    pieces = (
        (key_prev, value_prev, own_first - plane_tiles + arange_halo),
        (key_hat, value_two, own_first + jnp.arange(tile_count, dtype=jnp.int32)),
        (key_next, value_next, own_first + tile_count + arange_halo),
    )
    present = neighbours >= 0
    tile_masks = [
        jnp.any((neighbours[:, :, None] == ids[None, None, :]) & present[:, :, None], axis=1)
        for _, _, ids in pieces
    ]
    key_ok = jnp.repeat(jnp.concatenate(tile_masks, axis=1), TILE, axis=1).astype(f32)
    half_heads = heads_dev // 2
    halves = []
    for part in range(2):
        attn_half = tile_attention(
            query_hat,
            [p[0] for p in pieces],
            [p[1] for p in pieces],
            key_ok[:, None, :],
            TILE,
            part * half_heads,
            half_heads,
        )
        attn_half = attn_half.reshape(half_heads, head_size, rows_mine, head_dim)
        attn_half = lax.all_to_all(attn_half, "head", 1, 1, tiled=True)
        halves.append(
            jnp.transpose(attn_half, (1, 2, 0, 3)).reshape(
                head_size, rows_mine, half_heads * head_dim
            )
        )
    residual_mine = lax.dynamic_slice_in_dim(residual, head_index * rows_mine, rows_mine, 0)
    half_width = half_heads * head_dim
    total_two = 0.0
    for g in range(head_size):
        term = jnp.dot(halves[0][g], w2_full[g, :half_width], preferred_element_type=f32)
        term = term + jnp.dot(halves[1][g], w2_full[g, half_width:], preferred_element_type=f32)
        total_two = total_two + term.astype(bf16).astype(f32)
    mixed = residual_mine.astype(f32) + total_two
    return mixed.astype(bf16)


def solution(mesh):
    in_specs = (
        P(("groups", "ctx"), None),
        P(),
        P(None, None, "head"),
        P("head"),
        P("head", None),
        P(),
        P(None, None, "head"),
        P(),
        P(),
        P("head", None),
        P("ctx", None),
    )
    out_specs = P(("groups", "ctx", "head"), None)
    return jax.shard_map(
        on_device, mesh=mesh, in_specs=in_specs, out_specs=out_specs, check_vma=False
    )
```

```python
import functools
import math

import jax
import jax.numpy as jnp
import numpy as np
from jax import lax
from jax.experimental import pallas as pl
from jax.sharding import PartitionSpec as P

TILE = 256
GY = 2
GZ = 2


EPS = 1e-06


def with_halo(shard, sides, width):
    for axis, dim in sides:
        size, length = (lax.axis_size(axis), shard.shape[dim])
        up = [(i, (i + 1) % size) for i in range(size - 1)]
        down = [(j, i) for i, j in up]
        last = lax.slice_in_dim(shard, length - width, length, axis=dim)
        first = lax.slice_in_dim(shard, 0, width, axis=dim)
        before = lax.ppermute(last, axis, up)
        after = lax.ppermute(first, axis, down)
        shard = jnp.concatenate([before, shard, after], axis=dim)
    return shard


def rms_rows(value, gain):
    mean_sq = jnp.mean(value * value, axis=-1, keepdims=True)
    return value * lax.rsqrt(mean_sq + EPS) * gain


def feature_map(value):
    return jnp.where(value > 0, value + 1.0, jnp.exp(jnp.minimum(value, 0.0)))


def split_two(value):
    high_part = value.astype(jnp.bfloat16)
    low_part = (value - high_part.astype(jnp.float32)).astype(jnp.bfloat16)
    return (high_part, low_part)


def _attn_kernel(q_ref, kp_ref, ko_ref, kn_ref, vp_ref, vo_ref, vn_ref, m_ref, o_ref, *, scale):
    query = q_ref[...]
    mask = m_ref[0]
    exps = []
    total = None
    offset = 0
    for k_ref in (kp_ref, ko_ref, kn_ref):
        rows = k_ref.shape[0]
        scores = (
            lax.dot_general(
                query, k_ref[...], (((1,), (1,)), ((), ())), preferred_element_type=jnp.float32
            )
            * scale
        )
        unnormed = jnp.where(mask[:, offset : offset + rows] > 0.5, jnp.exp(scores), 0.0)
        exps.append(unnormed)
        part = jnp.sum(unnormed, axis=-1, keepdims=True)
        total = part if total is None else total + part
        offset += rows
    inverse = 1.0 / total
    acc = None
    for unnormed, v_ref in zip(exps, (vp_ref, vo_ref, vn_ref)):
        weights = (unnormed * inverse).astype(jnp.bfloat16)
        term = jnp.dot(weights, v_ref[...], preferred_element_type=jnp.float32)
        acc = term if acc is None else acc + term
    o_ref[...] = acc.astype(o_ref.dtype)


def tile_attention(query, keys, values, mask, block_rows, interpret=False):
    heads, rows, head_dim = query.shape
    blocks = rows // block_rows
    key_width = mask.shape[-1]
    kv_specs = [pl.BlockSpec((None, k.shape[1], head_dim), lambda h, b: (h, 0, 0)) for k in keys]
    return pl.pallas_call(
        functools.partial(_attn_kernel, scale=1.0 / math.sqrt(head_dim)),
        out_shape=jax.ShapeDtypeStruct((heads, rows, head_dim), jnp.bfloat16),
        grid=(heads, blocks),
        in_specs=[pl.BlockSpec((None, block_rows, head_dim), lambda h, b: (h, b, 0))]
        + kv_specs
        + kv_specs
        + [pl.BlockSpec((1, 1, key_width), lambda h, b: (b, 0, 0))],
        out_specs=pl.BlockSpec((None, block_rows, head_dim), lambda h, b: (h, b, 0)),
        interpret=interpret,
    )(query, *keys, *values, mask)

def on_device(
    tokens, norm_one, w_qkv1, lin_gain, w_out1, norm_two, w_qkv2, q_gain, k_gain, w_out2, neighbours
):
    f32, bf16 = jnp.float32, jnp.bfloat16
    tok_rows, feature_width = tokens.shape
    inner_dev = w_qkv1.shape[2]
    head_dim = q_gain.shape[0]
    heads_dev = inner_dev // head_dim
    block_rows = 2 * TILE
    block_count = tok_rows // block_rows
    rows_mine = tok_rows // lax.axis_size("head")
    head_index = lax.axis_index("head")
    ctx_index = lax.axis_index("ctx")
    ctx_size = lax.axis_size("ctx")

    normed = rms_rows(tokens.astype(f32), norm_one).astype(bf16)
    projected = jnp.dot(
        normed, w_qkv1.reshape(feature_width, 3 * inner_dev), preferred_element_type=f32
    )
    projected = projected.reshape(tok_rows, 3, heads_dev, head_dim)
    query_map = feature_map(projected[:, 0]).astype(bf16)
    key_map = feature_map(projected[:, 1]).astype(bf16)
    value_one = projected[:, 2].astype(bf16)
    q_blocks = query_map.reshape(block_count, block_rows, heads_dev, head_dim)
    k_blocks = key_map.reshape(block_count, block_rows, heads_dev, head_dim)
    v_blocks = value_one.reshape(block_count, block_rows, heads_dev, head_dim)
    block_states = jnp.einsum(
        "nthe,nthf->nhef", k_blocks, v_blocks, preferred_element_type=f32
    )
    own_total = jnp.sum(block_states, axis=0)
    all_totals = lax.all_gather(own_total.astype(bf16), "ctx", axis=0).astype(f32)
    earlier_dev = jnp.arange(ctx_size, dtype=jnp.int32) < ctx_index
    carried = jnp.sum(jnp.where(earlier_dev[:, None, None, None], all_totals, 0.0), axis=0)

    causal = lax.broadcasted_iota(jnp.int32, (block_rows, block_rows), 0) >= lax.broadcasted_iota(
        jnp.int32, (block_rows, block_rows), 1
    )
    head_size = lax.axis_size("head")
    core = ctx_index % 2

    group_index = lax.axis_index("groups")
    y_bit = (ctx_index // 2) % 2
    slot = group_index * 4 + y_bit * 2 + core
    slice_rows = inner_dev // 8
    core_pairs = [(i, i ^ 1) for i in range(ctx_size)]
    y_pairs = [(i, i ^ 2) for i in range(ctx_size)]
    group_pairs = [(i, i ^ 1) for i in range(lax.axis_size("groups"))]
    group_count = lax.axis_size("groups")
    cross_pairs = [
        (g * ctx_size + i, (g ^ 1) * ctx_size + i)
        for g in range(group_count)
        for i in range(1, ctx_size, 2)
    ]

    def gather_weight(w):
        local = lax.dynamic_slice_in_dim(w, slot * slice_rows, slice_rows, 0)
        first = lax.all_gather(local, "head", axis=0)
        by_y = lax.ppermute(first, "ctx", y_pairs)
        by_group = lax.ppermute(first, "groups", group_pairs)
        relay_y = lax.ppermute(by_group, "ctx", [p for p in y_pairs if p[0] % 2 == 0])
        relay_group = lax.ppermute(by_y, ("groups", "ctx"), cross_pairs)
        by_both = jnp.where(core == 0, relay_y, relay_group)
        pieces = [first, by_y, by_group, by_both]
        pieces = pieces + [lax.ppermute(p, "ctx", core_pairs) for p in pieces]
        offsets = [0, 2, 4, 6, 1, 3, 5, 7]
        full = jnp.zeros((head_size, 8) + local.shape, local.dtype)
        for offset, piece in zip(offsets, pieces):
            full = lax.dynamic_update_slice_in_dim(
                full, piece[:, None], jnp.bitwise_xor(slot, offset), 1
            )
        return full.reshape(head_size, inner_dev, w.shape[1])

    def project_out(parts, full):
        total = 0.0
        for g in range(head_size):
            term = jnp.dot(parts[g], full[g], preferred_element_type=f32)
            total = total + term.astype(bf16).astype(f32)
        return total

    w1_full = gather_weight(w_out1)
    w2_full = gather_weight(w_out2)
    attn_parts = []
    for n in range(block_count):
        q_n, k_n, v_n = q_blocks[n], k_blocks[n], v_blocks[n]
        scores = jnp.einsum("the,she->hts", q_n, k_n, preferred_element_type=f32)
        scores = jnp.where(causal, scores, 0.0)
        score_high, score_low = split_two(scores)
        within = jnp.einsum("hts,she->the", score_high, v_n, preferred_element_type=f32)
        within = within + jnp.einsum("hts,she->the", score_low, v_n, preferred_element_type=f32)
        state_high, state_low = split_two(carried)
        carried_term = jnp.einsum("the,hef->thf", q_n, state_high, preferred_element_type=f32)
        carried_term = carried_term + jnp.einsum(
            "the,hef->thf", q_n, state_low, preferred_element_type=f32
        )
        carried = carried + block_states[n]
        combined = within + carried_term
        attn_parts.append(
            rms_rows(combined, lin_gain.reshape(heads_dev, head_dim))
            .astype(bf16)
            .reshape(block_rows, inner_dev)
        )
    attn_one = jnp.concatenate(attn_parts, axis=0)
    gathered_one = lax.all_gather(attn_one, "head", axis=0)
    summed_one = jnp.dot(attn_one, w_out1, preferred_element_type=f32).astype(bf16).astype(f32)
    for shift in range(1, head_size):
        source = (head_index + shift) % head_size
        term = jnp.dot(
            lax.dynamic_index_in_dim(gathered_one, source, 0, keepdims=False),
            lax.dynamic_index_in_dim(w1_full, source, 0, keepdims=False),
            preferred_element_type=f32,
        )
        summed_one = summed_one + term.astype(bf16).astype(f32)
    residual = (tokens.astype(f32) + summed_one).astype(bf16)

    normed_two = rms_rows(residual.astype(f32), norm_two).astype(bf16)
    projected_kv = jnp.dot(
        normed_two, w_qkv2[:, 1:].reshape(feature_width, 2 * inner_dev), preferred_element_type=f32
    ).reshape(tok_rows, 2, heads_dev, head_dim)
    key_hat = rms_rows(projected_kv[:, 0], k_gain).astype(bf16)
    value_two = projected_kv[:, 1].astype(bf16)
    key_hat, value_two, normed_two = lax.optimization_barrier((key_hat, value_two, normed_two))
    projected_q = jnp.dot(normed_two, w_qkv2[:, 0], preferred_element_type=f32)
    query_hat = rms_rows(projected_q.reshape(tok_rows, heads_dev, head_dim), q_gain).astype(bf16)

    plane_tiles = GY * GZ
    halo_rows = plane_tiles * TILE
    tile_count = tok_rows // TILE
    up = [(i, i + 1) for i in range(ctx_size - 1)]
    down = [(i + 1, i) for i in range(ctx_size - 1)]
    key_hat = jnp.transpose(key_hat, (1, 0, 2))
    value_two = jnp.transpose(value_two, (1, 0, 2))
    query_hat = jnp.transpose(query_hat, (1, 0, 2))
    key_prev = lax.ppermute(key_hat[:, tok_rows - halo_rows :], "ctx", up)
    value_prev = lax.ppermute(value_two[:, tok_rows - halo_rows :], "ctx", up)
    key_next = lax.ppermute(key_hat[:, :halo_rows], "ctx", down)
    value_next = lax.ppermute(value_two[:, :halo_rows], "ctx", down)
    own_first = ctx_index * tile_count
    arange_halo = jnp.arange(plane_tiles, dtype=jnp.int32)
    pieces = (
        (key_prev, value_prev, own_first - plane_tiles + arange_halo),
        (key_hat, value_two, own_first + jnp.arange(tile_count, dtype=jnp.int32)),
        (key_next, value_next, own_first + tile_count + arange_halo),
    )
    present = neighbours >= 0
    tile_masks = [
        jnp.any((neighbours[:, :, None] == ids[None, None, :]) & present[:, :, None], axis=1)
        for _, _, ids in pieces
    ]
    key_ok = jnp.repeat(jnp.concatenate(tile_masks, axis=1), TILE, axis=1).astype(f32)
    attn_two = tile_attention(
        query_hat, [p[0] for p in pieces], [p[1] for p in pieces], key_ok[:, None, :], TILE
    )
    attn_two = attn_two.reshape(heads_dev, head_size, rows_mine, head_dim)
    attn_two = lax.all_to_all(attn_two, "head", 1, 1, tiled=True)
    attn_two = jnp.transpose(attn_two, (1, 2, 0, 3)).reshape(head_size, rows_mine, inner_dev)
    residual_mine = lax.dynamic_slice_in_dim(residual, head_index * rows_mine, rows_mine, 0)
    mixed = residual_mine.astype(f32) + project_out(attn_two, w2_full)
    return mixed.astype(bf16)


def solution(mesh):
    in_specs = (
        P(("groups", "ctx"), None),
        P(),
        P(None, None, "head"),
        P("head"),
        P("head", None),
        P(),
        P(None, None, "head"),
        P(),
        P(),
        P("head", None),
        P("ctx", None),
    )
    out_specs = P(("groups", "ctx", "head"), None)
    return jax.shard_map(
        on_device, mesh=mesh, in_specs=in_specs, out_specs=out_specs, check_vma=False
    )
```

```python
import functools
import math

import jax
import jax.numpy as jnp
import numpy as np
from jax import lax
from jax.experimental import pallas as pl
from jax.sharding import PartitionSpec as P

TILE = 256
GY = 2
GZ = 2


EPS = 1e-06


def with_halo(shard, sides, width):
    for axis, dim in sides:
        size, length = (lax.axis_size(axis), shard.shape[dim])
        up = [(i, (i + 1) % size) for i in range(size - 1)]
        down = [(j, i) for i, j in up]
        last = lax.slice_in_dim(shard, length - width, length, axis=dim)
        first = lax.slice_in_dim(shard, 0, width, axis=dim)
        before = lax.ppermute(last, axis, up)
        after = lax.ppermute(first, axis, down)
        shard = jnp.concatenate([before, shard, after], axis=dim)
    return shard


def rms_rows(value, gain):
    mean_sq = jnp.mean(value * value, axis=-1, keepdims=True)
    return value * lax.rsqrt(mean_sq + EPS) * gain


def feature_map(value):
    return jnp.where(value > 0, value + 1.0, jnp.exp(jnp.minimum(value, 0.0)))


def split_two(value):
    high_part = value.astype(jnp.bfloat16)
    low_part = (value - high_part.astype(jnp.float32)).astype(jnp.bfloat16)
    return (high_part, low_part)


def _attn_kernel(q_ref, kp_ref, ko_ref, kn_ref, vp_ref, vo_ref, vn_ref, m_ref, o_ref, *, scale):
    query = q_ref[...]
    mask = m_ref[0]
    exps = []
    total = None
    offset = 0
    for k_ref in (kp_ref, ko_ref, kn_ref):
        rows = k_ref.shape[0]
        scores = (
            lax.dot_general(
                query, k_ref[...], (((1,), (1,)), ((), ())), preferred_element_type=jnp.float32
            )
            * scale
        )
        unnormed = jnp.where(mask[:, offset : offset + rows] > 0.5, jnp.exp(scores), 0.0)
        exps.append(unnormed)
        part = jnp.sum(unnormed, axis=-1, keepdims=True)
        total = part if total is None else total + part
        offset += rows
    inverse = 1.0 / total
    acc = None
    for unnormed, v_ref in zip(exps, (vp_ref, vo_ref, vn_ref)):
        weights = (unnormed * inverse).astype(jnp.bfloat16)
        term = jnp.dot(weights, v_ref[...], preferred_element_type=jnp.float32)
        acc = term if acc is None else acc + term
    o_ref[...] = acc.astype(o_ref.dtype)


def tile_attention(query, keys, values, mask, block_rows, interpret=False):
    heads, rows, head_dim = query.shape
    blocks = rows // block_rows
    key_width = mask.shape[-1]
    kv_specs = [pl.BlockSpec((None, k.shape[1], head_dim), lambda h, b: (h, 0, 0)) for k in keys]
    return pl.pallas_call(
        functools.partial(_attn_kernel, scale=1.0 / math.sqrt(head_dim)),
        out_shape=jax.ShapeDtypeStruct((heads, rows, head_dim), jnp.bfloat16),
        grid=(heads, blocks),
        in_specs=[pl.BlockSpec((None, block_rows, head_dim), lambda h, b: (h, b, 0))]
        + kv_specs
        + kv_specs
        + [pl.BlockSpec((1, 1, key_width), lambda h, b: (b, 0, 0))],
        out_specs=pl.BlockSpec((None, block_rows, head_dim), lambda h, b: (h, b, 0)),
        interpret=interpret,
    )(query, *keys, *values, mask)

def on_device(
    tokens, norm_one, w_qkv1, lin_gain, w_out1, norm_two, w_qkv2, q_gain, k_gain, w_out2, neighbours
):
    f32, bf16 = jnp.float32, jnp.bfloat16
    tok_rows, feature_width = tokens.shape
    inner_dev = w_qkv1.shape[2]
    head_dim = q_gain.shape[0]
    heads_dev = inner_dev // head_dim
    block_rows = 2 * TILE
    block_count = tok_rows // block_rows
    rows_mine = tok_rows // lax.axis_size("head")
    head_index = lax.axis_index("head")
    ctx_index = lax.axis_index("ctx")
    ctx_size = lax.axis_size("ctx")

    normed = rms_rows(tokens.astype(f32), norm_one).astype(bf16)
    projected = jnp.dot(
        normed, w_qkv1.reshape(feature_width, 3 * inner_dev), preferred_element_type=f32
    )
    projected = projected.reshape(tok_rows, 3, heads_dev, head_dim)
    query_map = feature_map(projected[:, 0]).astype(bf16)
    key_map = feature_map(projected[:, 1]).astype(bf16)
    value_one = projected[:, 2].astype(bf16)
    q_blocks = query_map.reshape(block_count, block_rows, heads_dev, head_dim)
    k_blocks = key_map.reshape(block_count, block_rows, heads_dev, head_dim)
    v_blocks = value_one.reshape(block_count, block_rows, heads_dev, head_dim)
    block_states = jnp.einsum(
        "nthe,nthf->nhef", k_blocks, v_blocks, preferred_element_type=f32
    )
    own_total = jnp.sum(block_states, axis=0)
    all_totals = lax.all_gather(own_total.astype(bf16), "ctx", axis=0).astype(f32)
    earlier_dev = jnp.arange(ctx_size, dtype=jnp.int32) < ctx_index
    carried = jnp.sum(jnp.where(earlier_dev[:, None, None, None], all_totals, 0.0), axis=0)

    causal = lax.broadcasted_iota(jnp.int32, (block_rows, block_rows), 0) >= lax.broadcasted_iota(
        jnp.int32, (block_rows, block_rows), 1
    )
    head_size = lax.axis_size("head")
    core = ctx_index % 2

    group_index = lax.axis_index("groups")
    y_bit = (ctx_index // 2) % 2
    slot = group_index * 4 + y_bit * 2 + core
    slice_rows = inner_dev // 8
    core_pairs = [(i, i ^ 1) for i in range(ctx_size)]
    y_pairs = [(i, i ^ 2) for i in range(ctx_size)]
    group_pairs = [(i, i ^ 1) for i in range(lax.axis_size("groups"))]
    group_count = lax.axis_size("groups")
    cross_pairs = [
        (g * ctx_size + i, (g ^ 1) * ctx_size + i)
        for g in range(group_count)
        for i in range(1, ctx_size, 2)
    ]

    def gather_weight(w):
        local = lax.dynamic_slice_in_dim(w, slot * slice_rows, slice_rows, 0)
        first = lax.all_gather(local, "head", axis=0)
        by_y = lax.ppermute(first, "ctx", y_pairs)
        by_group = lax.ppermute(first, "groups", group_pairs)
        relay_y = lax.ppermute(by_group, "ctx", [p for p in y_pairs if p[0] % 2 == 0])
        relay_group = lax.ppermute(by_y, ("groups", "ctx"), cross_pairs)
        by_both = jnp.where(core == 0, relay_y, relay_group)
        pieces = [first, by_y, by_group, by_both]
        pieces = pieces + [lax.ppermute(p, "ctx", core_pairs) for p in pieces]
        offsets = [0, 2, 4, 6, 1, 3, 5, 7]
        full = jnp.zeros((head_size, 8) + local.shape, local.dtype)
        for offset, piece in zip(offsets, pieces):
            full = lax.dynamic_update_slice_in_dim(
                full, piece[:, None], jnp.bitwise_xor(slot, offset), 1
            )
        return full.reshape(head_size, inner_dev, w.shape[1])

    def project_out(parts, full):
        total = 0.0
        for g in range(head_size):
            term = jnp.dot(parts[g], full[g], preferred_element_type=f32)
            total = total + term.astype(bf16).astype(f32)
        return total

    w1_full = gather_weight(w_out1)
    w2_full = gather_weight(w_out2)
    attn_parts = []
    for n in range(block_count):
        q_n, k_n, v_n = q_blocks[n], k_blocks[n], v_blocks[n]
        scores = jnp.einsum("the,she->hts", q_n, k_n, preferred_element_type=f32)
        scores = jnp.where(causal, scores, 0.0)
        score_high, score_low = split_two(scores)
        within = jnp.einsum("hts,she->the", score_high, v_n, preferred_element_type=f32)
        within = within + jnp.einsum("hts,she->the", score_low, v_n, preferred_element_type=f32)
        state_high, state_low = split_two(carried)
        carried_term = jnp.einsum("the,hef->thf", q_n, state_high, preferred_element_type=f32)
        carried_term = carried_term + jnp.einsum(
            "the,hef->thf", q_n, state_low, preferred_element_type=f32
        )
        carried = carried + block_states[n]
        combined = within + carried_term
        attn_parts.append(
            rms_rows(combined, lin_gain.reshape(heads_dev, head_dim))
            .astype(bf16)
            .reshape(block_rows, inner_dev)
        )
    attn_one = jnp.concatenate(attn_parts, axis=0)
    gathered_one = lax.all_gather(attn_one, "head", axis=0)
    residual = (tokens.astype(f32) + project_out(gathered_one, w1_full)).astype(bf16)

    normed_two = rms_rows(residual.astype(f32), norm_two).astype(bf16)
    projected_kv = jnp.dot(
        normed_two, w_qkv2[:, 1:].reshape(feature_width, 2 * inner_dev), preferred_element_type=f32
    ).reshape(tok_rows, 2, heads_dev, head_dim)
    key_hat = rms_rows(projected_kv[:, 0], k_gain).astype(bf16)
    value_two = projected_kv[:, 1].astype(bf16)
    key_hat, value_two, normed_two = lax.optimization_barrier((key_hat, value_two, normed_two))
    projected_q = jnp.einsum(
        "td,dhe->hte",
        normed_two,
        w_qkv2[:, 0].reshape(feature_width, heads_dev, head_dim),
        preferred_element_type=f32,
    )
    query_hat = rms_rows(projected_q, q_gain).astype(bf16)

    plane_tiles = GY * GZ
    halo_rows = plane_tiles * TILE
    tile_count = tok_rows // TILE
    up = [(i, i + 1) for i in range(ctx_size - 1)]
    down = [(i + 1, i) for i in range(ctx_size - 1)]
    key_hat = jnp.transpose(key_hat, (1, 0, 2))
    value_two = jnp.transpose(value_two, (1, 0, 2))
    key_prev = lax.ppermute(key_hat[:, tok_rows - halo_rows :], "ctx", up)
    value_prev = lax.ppermute(value_two[:, tok_rows - halo_rows :], "ctx", up)
    key_next = lax.ppermute(key_hat[:, :halo_rows], "ctx", down)
    value_next = lax.ppermute(value_two[:, :halo_rows], "ctx", down)
    own_first = ctx_index * tile_count
    arange_halo = jnp.arange(plane_tiles, dtype=jnp.int32)
    pieces = (
        (key_prev, value_prev, own_first - plane_tiles + arange_halo),
        (key_hat, value_two, own_first + jnp.arange(tile_count, dtype=jnp.int32)),
        (key_next, value_next, own_first + tile_count + arange_halo),
    )
    present = neighbours >= 0
    tile_masks = [
        jnp.any((neighbours[:, :, None] == ids[None, None, :]) & present[:, :, None], axis=1)
        for _, _, ids in pieces
    ]
    key_ok = jnp.repeat(jnp.concatenate(tile_masks, axis=1), TILE, axis=1).astype(f32)
    attn_two = tile_attention(
        query_hat, [p[0] for p in pieces], [p[1] for p in pieces], key_ok[:, None, :], TILE
    )
    attn_two = attn_two.reshape(heads_dev, head_size, rows_mine, head_dim)
    attn_two = lax.all_to_all(attn_two, "head", 1, 1, tiled=True)
    attn_two = jnp.transpose(attn_two, (1, 2, 0, 3)).reshape(head_size, rows_mine, inner_dev)
    residual_mine = lax.dynamic_slice_in_dim(residual, head_index * rows_mine, rows_mine, 0)
    mixed = residual_mine.astype(f32) + project_out(attn_two, w2_full)
    return mixed.astype(bf16)


def solution(mesh):
    in_specs = (
        P(("groups", "ctx"), None),
        P(),
        P(None, None, "head"),
        P("head"),
        P("head", None),
        P(),
        P(None, None, "head"),
        P(),
        P(),
        P("head", None),
        P("ctx", None),
    )
    out_specs = P(("groups", "ctx", "head"), None)
    return jax.shard_map(
        on_device, mesh=mesh, in_specs=in_specs, out_specs=out_specs, check_vma=False
    )
```
